32 devices in a mesh: circ: 4 (over z), normal: 2 (over y), span: 4 (over x, core).
Axes of the slice: x: 2, y: 2, z: 4, core: 2. Of those that a mesh axis runs over, the one named last changes fastest.
Arguments:
- adjoint: float32 [5, 16, 32, 512], P(None, 'span', 'normal', 'circ'), may hold values from -6 to 6
- objective_grad: float32 [5, 16, 32, 512], P(None, 'span', 'normal', 'circ'), may hold values from -6 to 6
- face_weights: float32 [3, 16, 32, 512], P(None, 'span', 'normal', 'circ'), may hold values from 0.2 to 2
- owner_jac: float32 [3, 5, 5], replicated, may hold values from -2.5 to 2.5
- neighbor_jac: float32 [3, 5, 5], replicated, may hold values from -2.5 to 2.5
- coupling: float32 [3, 5], replicated, may hold values from -2.5 to 2.5
- stiffness: float32 [16, 32, 512], P('span', 'normal', 'circ'), may hold values from 0.3 to 3
- wall_kernel: float32 [16, 32, 512], P('span', 'normal', 'circ'), may hold values from -0.25 to 0.25
- panel_owner: int32 [16, 512], P('span', 'circ'), may hold values from 0 to 511, as said below
Outputs:
- adjoint_residual: float32 [5, 16, 32, 512], P(None, 'span', 'normal', 'circ')
- mesh_adjoint: float32 [3, 16, 32, 512], P(None, 'span', 'normal', 'circ')
- panel_sens: float32 [3, 512], P(None, 'span')
The draws below stay inside these ranges and needn't reach their ends.
Inputs may be any that keep to these rules, and one draw needn't show every extreme that they name: `panel_owner`: the panel of a wall face at station k is owned by span index k // 4 or the one beside it; panels hold ragged numbers of faces.
All inputs are finite; a program needn't handle non-finite values.
Results may differ from the reference program's by a relative error of at most 0.00011.
Values sent between devices are 32-bit elements; how exact they have to be, the bound alone decides.
No kernel may reach another device: no remote copies, remote signals or barrier semaphores. Data moves between devices by JAX's collectives and lax.ppermute only.
A program may use at most 64 MiB of HBM per device.

```python
import math
import jax
import jax.numpy as jnp
from jax import lax

CK = 4
PANEL_DEV = 128
SWEEPS = 4
NK = 16
NJ = 32
NI = 512
PANELS = 512
N_SPAN = 4


def draw_panel_owner(key, part):
    first, second = jax.random.split(key)
    station = jnp.arange(NK, dtype=jnp.int32) // CK
    offset = jax.random.randint(first, (NK, NI), -1, 2)
    owners = jnp.clip(station[:, None] + offset, 0, N_SPAN - 1)
    ids = owners * PANEL_DEV + jax.random.randint(second, (NK, NI), 0, PANEL_DEV)
    ids = ids.at[0, 0].set(0)
    ids = ids.at[NK - 1, NI - 1].set(PANELS - 1)
    return ids.astype(jnp.int32)


def block_levels(stream_key, dims, pieces, least, top_value):
    loudness, own = 1.0, jax.random.fold_in(stream_key, 6)
    for position, shards_of in pieces:
        heights = jnp.exp(jax.random.uniform(jax.random.fold_in(own, position), (shards_of,), jnp.float32, least / len(pieces), top_value / len(pieces)))
        loudness = loudness * jnp.repeat(heights, dims[position] // shards_of).reshape([-1 if axis == position else 1 for axis in range(len(dims))])
    return loudness


def bell_draw(own_key, shape, spread, most, pieces=(), kind=jnp.bfloat16):
    factor_of = block_levels(own_key, shape, pieces, -0.22, 0.18) if pieces else 1.0
    drawn = jax.random.normal(own_key, shape, jnp.float32) * spread * factor_of
    return jnp.minimum(jnp.maximum(drawn, -most), most).astype(kind)


def setup_inputs(seed: int = 0) -> dict:
    arg_keys = jax.random.split(jax.random.key(seed), 10)
    adjoint = bell_draw(arg_keys[0], (5, NK, NJ, NI), 1.0, 6.0, ((1, 4), (2, 2), (3, 4)), jnp.float32)
    objective_grad = bell_draw(arg_keys[1], (5, NK, NJ, NI), 1.0, 6.0, ((1, 4), (2, 2), (3, 4)), jnp.float32)
    face_weights = jnp.clip(jnp.exp(math.log(2.0) - 2.3025851 * jax.random.uniform(arg_keys[2], (3, NK, NJ, NI), jnp.float32) ** block_levels(arg_keys[2], (3, NK, NJ, NI), ((1, 4), (2, 2), (3, 4)), -0.2, 0.2)), 0.2, 2.0)
    owner_jac = bell_draw(arg_keys[3], (3, 5, 5), 5 ** -0.5, 2.5, (), jnp.float32)
    neighbor_jac = bell_draw(arg_keys[4], (3, 5, 5), 5 ** -0.5, 2.5, (), jnp.float32)
    coupling = bell_draw(arg_keys[5], (3, 5), 5 ** -0.5, 2.5, (), jnp.float32)
    stiffness = jnp.clip(jnp.exp(math.log(3.0) - 2.3025851 * jax.random.uniform(arg_keys[6], (NK, NJ, NI), jnp.float32) ** block_levels(arg_keys[6], (NK, NJ, NI), ((0, 4), (1, 2), (2, 4)), -0.2, 0.2)), 0.3, 3.0)
    wall_kernel = bell_draw(arg_keys[7], (NK, NJ, NI), (NJ * 16) ** -0.5, 0.25, ((0, 4), (1, 2), (2, 4)), jnp.float32)
    panel_owner = draw_panel_owner(jax.random.fold_in(arg_keys[9], 71), 0)
    return dict(adjoint=adjoint, objective_grad=objective_grad, face_weights=face_weights, owner_jac=owner_jac, neighbor_jac=neighbor_jac, coupling=coupling, stiffness=stiffness, wall_kernel=wall_kernel, panel_owner=panel_owner)


def pad_field(field, width):
    field = jnp.pad(field, ((0, 0), (width, width), (width, width), (0, 0)))
    return jnp.pad(field, ((0, 0), (0, 0), (0, 0), (width, width)), mode="wrap")


def neighbor_sum(padded):
    total = padded[:, 2:, 1:-1, 1:-1] + padded[:, :-2, 1:-1, 1:-1]
    total = total + padded[:, 1:-1, 2:, 1:-1] + padded[:, 1:-1, :-2, 1:-1]
    return total + padded[:, 1:-1, 1:-1, 2:] + padded[:, 1:-1, 1:-1, :-2]


def flux_transpose(padded, owner_jac, neighbor_jac):
    psi = padded[:5]
    weights = padded[5:]
    center = psi[:, 1:-1, 1:-1, 1:-1]
    total = jnp.zeros_like(center)
    for direction in range(3):
        lower = [slice(None), slice(1, -1), slice(1, -1), slice(1, -1)]
        upper = [slice(None), slice(1, -1), slice(1, -1), slice(1, -1)]
        lower[direction + 1] = slice(0, -2)
        upper[direction + 1] = slice(2, None)
        w_here = weights[direction, 1:-1, 1:-1, 1:-1]
        w_lower = weights[direction][tuple(lower[1:])]
        up_term = w_here[None] * (center - psi[tuple(upper)])
        down_term = w_lower[None] * (psi[tuple(lower)] - center)
        total = total + jnp.einsum("uv,ukji->vkji", owner_jac[direction], up_term, precision=lax.Precision.HIGHEST)
        total = total + jnp.einsum("uv,ukji->vkji", neighbor_jac[direction], down_term, precision=lax.Precision.HIGHEST)
    return total


def reference(adjoint, objective_grad, face_weights, owner_jac, neighbor_jac, coupling, stiffness, wall_kernel, panel_owner):
    stacked = jnp.concatenate([adjoint, face_weights], axis=0)
    padded = pad_field(stacked, 1)
    residual = flux_transpose(padded, owner_jac, neighbor_jac) + adjoint - objective_grad
    forcing = jnp.einsum("mv,vkji->mkji", coupling, residual, precision=lax.Precision.HIGHEST)
    diag_term = 6.0 * stiffness + 1.0
    mesh = jnp.zeros_like(forcing)
    for sweep in range(SWEEPS):
        weighted = pad_field(stiffness[None] * mesh, 1)
        mesh = mesh + 0.8 * (forcing - diag_term[None] * mesh + neighbor_sum(weighted)) / diag_term[None]
    wall_sens = jnp.sum(wall_kernel[None] * mesh, axis=2)
    flat = wall_sens.reshape(3, -1).T
    panels = jax.ops.segment_sum(flat, panel_owner.reshape(-1), num_segments=PANELS).T
    return residual, mesh, panels
```

```python
import jax
import jax.numpy as jnp
from jax import lax
from jax.sharding import PartitionSpec as P

PANEL_DEV = 128
SWEEPS = 4


def padded_2(array, sides, width, wrap):
    for axis, dim in sides:
        peers, length = (lax.axis_size(axis), array.shape[dim])
        up = [(i, (i + 1) % peers) for i in range(peers if wrap else peers - 1)]
        down = [(j, i) for i, j in up]
        last = lax.slice_in_dim(array, length - width, length, axis=dim)
        initial = lax.slice_in_dim(array, 0, width, axis=dim)
        before = lax.ppermute(last, axis, up)
        after = lax.ppermute(initial, axis, down)
        array = jnp.concatenate([before, array, after], axis=dim)
    return array


def neighbor_sum(padded):
    total = padded[:, 2:, 1:-1, 1:-1] + padded[:, :-2, 1:-1, 1:-1]
    total = total + padded[:, 1:-1, 2:, 1:-1] + padded[:, 1:-1, :-2, 1:-1]
    return total + padded[:, 1:-1, 1:-1, 2:] + padded[:, 1:-1, 1:-1, :-2]


def inner(field):
    return field[:, 1:-1, 1:-1, 1:-1]


def flux_transpose(padded, owner_jac, neighbor_jac):
    psi = padded[:5]
    weights = padded[5:]
    center = inner(psi)
    total = jnp.zeros_like(center)
    for direction in range(3):
        lower = [slice(None), slice(1, -1), slice(1, -1), slice(1, -1)]
        upper = [slice(None), slice(1, -1), slice(1, -1), slice(1, -1)]
        lower[direction + 1] = slice(0, -2)
        upper[direction + 1] = slice(2, None)
        w_here = weights[direction, 1:-1, 1:-1, 1:-1]
        w_lower = weights[direction][tuple(lower[1:])]
        up_term = w_here[None] * (center - psi[tuple(upper)])
        down_term = w_lower[None] * (psi[tuple(lower)] - center)
        total = total + jnp.einsum(
            "uv,ukji->vkji", owner_jac[direction], up_term, precision=lax.Precision.HIGHEST
        )
        total = total + jnp.einsum(
            "uv,ukji->vkji", neighbor_jac[direction], down_term, precision=lax.Precision.HIGHEST
        )
    return total


def relax(mesh_pad, stiff_pad, force_pad):
    weighted = stiff_pad[None] * mesh_pad
    stiff_in = stiff_pad[1:-1, 1:-1, 1:-1]
    diag_term = 6.0 * stiff_in + 1.0
    mesh_in = inner(mesh_pad)
    return (
        mesh_in
        + 0.8
        * (inner(force_pad) - diag_term[None] * mesh_in + neighbor_sum(weighted))
        / diag_term[None]
    )


def run_sweeps(stiff_pad, force_pad):
    mesh_pad = 0.8 * force_pad / (6.0 * stiff_pad[None] + 1.0)
    for sweep in range(1, SWEEPS):
        mesh_pad = relax(mesh_pad, stiff_pad, force_pad)
        stiff_pad = stiff_pad[1:-1, 1:-1, 1:-1]
        force_pad = inner(force_pad)
    return mesh_pad


def face_halos(array, axis, dim, wrap):
    peers, length = (lax.axis_size(axis), array.shape[dim])
    up = [(i, (i + 1) % peers) for i in range(peers if wrap else peers - 1)]
    down = [(j, i) for i, j in up]
    before = lax.ppermute(lax.slice_in_dim(array, length - 1, length, axis=dim), axis, up)
    after = lax.ppermute(lax.slice_in_dim(array, 0, 1, axis=dim), axis, down)
    return before, after


def flux_faces(stacked, halos, owner_jac, neighbor_jac):
    center = stacked[:5]
    total = jnp.zeros_like(center)
    for direction in range(3):
        dim = direction + 1
        before, after = halos[direction]
        line = jnp.concatenate([before, stacked, after], axis=dim)
        length = line.shape[dim]
        upper = lax.slice_in_dim(line[:5], 2, length, axis=dim)
        lower = lax.slice_in_dim(line[:5], 0, length - 2, axis=dim)
        w_here = stacked[5 + direction]
        w_lower = lax.slice_in_dim(line[5 + direction], 0, length - 2, axis=direction)
        up_term = w_here[None] * (center - upper)
        down_term = w_lower[None] * (lower - center)
        total = total + jnp.einsum(
            "uv,ukji->vkji", owner_jac[direction], up_term, precision=lax.Precision.HIGHEST
        )
        total = total + jnp.einsum(
            "uv,ukji->vkji", neighbor_jac[direction], down_term, precision=lax.Precision.HIGHEST
        )
    return total


def on_device(
    adjoint,
    objective_grad,
    face_weights,
    owner_jac,
    neighbor_jac,
    coupling,
    stiffness,
    wall_kernel,
    panel_owner,
):
    stacked = jnp.concatenate([adjoint, face_weights], axis=0)
    halos = [
        face_halos(stacked, "span", 1, False),
        face_halos(stacked, "normal", 2, False),
        face_halos(stacked, "circ", 3, True),
    ]
    residual = flux_faces(stacked, halos, owner_jac, neighbor_jac) + adjoint - objective_grad
    forcing = jnp.einsum("mv,vkji->mkji", coupling, residual, precision=lax.Precision.HIGHEST)
    margin = SWEEPS - 1
    joined = jnp.concatenate([stiffness[None], forcing], axis=0)
    cycle_pad = padded_2(joined, (("circ", 3),), margin, True)
    full_pad = padded_2(cycle_pad, (("normal", 2), ("span", 1)), margin, False)
    mesh = run_sweeps(full_pad[0], full_pad[1:])
    wall_sens = jnp.sum(wall_kernel[None] * mesh, axis=2)
    span = lax.axis_index("span")
    first = (span - 1) * PANEL_DEV
    local = panel_owner - first
    onehot = (
        local[:, :, None] == jnp.arange(3 * PANEL_DEV, dtype=jnp.int32)[None, None, :]
    ).astype(jnp.float32)
    terms = jnp.einsum("mki,kip->mp", wall_sens, onehot, precision=lax.Precision.HIGHEST)
    terms = lax.psum(terms, ("circ", "normal"))
    peers = lax.axis_size("span")
    up = [(i, i + 1) for i in range(peers - 1)]
    down = [(j, i) for i, j in up]
    from_below = lax.ppermute(terms[:, 2 * PANEL_DEV :], "span", up)
    from_above = lax.ppermute(terms[:, :PANEL_DEV], "span", down)
    panels = terms[:, PANEL_DEV : 2 * PANEL_DEV] + from_below + from_above
    return (residual, mesh, panels)


def solution(mesh):
    placed = (
        P(None, "span", "normal", "circ"),
        P(None, "span", "normal", "circ"),
        P(None, "span", "normal", "circ"),
        P(),
        P(),
        P(),
        P("span", "normal", "circ"),
        P("span", "normal", "circ"),
        P("span", "circ"),
    )
    return jax.shard_map(
        on_device,
        mesh=mesh,
        in_specs=placed,
        out_specs=(
            P(None, "span", "normal", "circ"),
            P(None, "span", "normal", "circ"),
            P(None, "span"),
        ),
        check_vma=False,
    )
```

```python
import itertools
import math

import jax
import jax.numpy as jnp
from jax import lax
from jax.sharding import PartitionSpec as P

PANEL_DEV = 128
SWEEPS = 4


def padded_2(array, sides, width, wrap):
    for axis, dim in sides:
        peers, length = (lax.axis_size(axis), array.shape[dim])
        up = [(i, (i + 1) % peers) for i in range(peers if wrap else peers - 1)]
        down = [(j, i) for i, j in up]
        last = lax.slice_in_dim(array, length - width, length, axis=dim)
        initial = lax.slice_in_dim(array, 0, width, axis=dim)
        before = lax.ppermute(last, axis, up)
        after = lax.ppermute(initial, axis, down)
        array = jnp.concatenate([before, array, after], axis=dim)
    return array


def neighbor_sum(padded):
    total = padded[:, 2:, 1:-1, 1:-1] + padded[:, :-2, 1:-1, 1:-1]
    total = total + padded[:, 1:-1, 2:, 1:-1] + padded[:, 1:-1, :-2, 1:-1]
    return total + padded[:, 1:-1, 1:-1, 2:] + padded[:, 1:-1, 1:-1, :-2]


def inner(field):
    return field[:, 1:-1, 1:-1, 1:-1]


def flux_transpose(padded, owner_jac, neighbor_jac):
    psi = padded[:5]
    weights = padded[5:]
    center = inner(psi)
    total = jnp.zeros_like(center)
    for direction in range(3):
        lower = [slice(None), slice(1, -1), slice(1, -1), slice(1, -1)]
        upper = [slice(None), slice(1, -1), slice(1, -1), slice(1, -1)]
        lower[direction + 1] = slice(0, -2)
        upper[direction + 1] = slice(2, None)
        w_here = weights[direction, 1:-1, 1:-1, 1:-1]
        w_lower = weights[direction][tuple(lower[1:])]
        up_term = w_here[None] * (center - psi[tuple(upper)])
        down_term = w_lower[None] * (psi[tuple(lower)] - center)
        total = total + jnp.einsum(
            "uv,ukji->vkji", owner_jac[direction], up_term, precision=lax.Precision.HIGHEST
        )
        total = total + jnp.einsum(
            "uv,ukji->vkji", neighbor_jac[direction], down_term, precision=lax.Precision.HIGHEST
        )
    return total


def relax(mesh_pad, stiff_pad, force_pad):
    weighted = stiff_pad[None] * mesh_pad
    stiff_in = stiff_pad[1:-1, 1:-1, 1:-1]
    diag_term = 6.0 * stiff_in + 1.0
    mesh_in = inner(mesh_pad)
    return (
        mesh_in
        + 0.8
        * (inner(force_pad) - diag_term[None] * mesh_in + neighbor_sum(weighted))
        / diag_term[None]
    )


def run_sweeps(stiff_pad, force_pad):
    mesh_pad = 0.8 * force_pad / (6.0 * stiff_pad[None] + 1.0)
    for sweep in range(1, SWEEPS):
        mesh_pad = relax(mesh_pad, stiff_pad, force_pad)
        stiff_pad = stiff_pad[1:-1, 1:-1, 1:-1]
        force_pad = inner(force_pad)
    return mesh_pad


ORDER = ("circ", "normal", "span")
WRAP = {"circ": True, "normal": False, "span": False}


def edge(array, dim, side, width):
    length = array.shape[dim]
    start = length - width if side < 0 else 0
    return lax.slice_in_dim(array, start, start + width, axis=dim)


def pairs_for(offsets):
    axes = [a for a in ORDER if a in offsets]
    sizes = [lax.axis_size(a) for a in axes]
    pairs = []
    for source in itertools.product(*[range(n) for n in sizes]):
        target, inside = [], True
        for axis, q, n in zip(axes, source, sizes):
            t = q + offsets[axis]
            if WRAP[axis]:
                t %= n
            elif not 0 <= t < n:
                inside = False
            target.append(t)
        if inside:
            lin = lambda v: sum(x * math.prod(sizes[i + 1 :]) for i, x in enumerate(v))
            pairs.append((lin(source), lin(target)))
    return tuple(axes), pairs


def take(array, rel, dims, width):
    for axis, r in rel.items():
        if r:
            array = edge(array, dims[axis], r, width)
    return array


def receive(array, rel, dims, width):
    rel = {a: r for a, r in rel.items() if r}
    axes, pairs = pairs_for({a: -r for a, r in rel.items()})
    return lax.ppermute(take(array, rel, dims, width), axes, pairs)


def receive_pair(array, rel, axis, dims, width):
    low = dict(rel, **{axis: -1})
    high = dict(rel, **{axis: 1})
    if lax.axis_size(axis) != 2 or WRAP[axis]:
        return receive(array, low, dims, width), receive(array, high, dims, width)
    me = lax.axis_index(axis)
    sent = jnp.where(me == 0, take(array, low, dims, width), take(array, high, dims, width))
    low_nz = {a: r for a, r in low.items() if r}
    axes, pairs = pairs_for({a: -r for a, r in low_nz.items()})
    _, back = pairs_for({a: -r for a, r in dict(low_nz, **{axis: 1}).items()})
    got = lax.ppermute(sent, axes, pairs + back)
    zero = jnp.zeros_like(got)
    return jnp.where(me == 1, got, zero), jnp.where(me == 0, got, zero)


def face_halos(array, axis, dim, wrap):
    return receive_pair(array, {}, axis, {axis: dim}, 1)


def padded_sweeps(joined, width):
    dims = {"span": 1, "normal": 2, "circ": 3}
    before_c = receive(joined, {"circ": -1}, dims, width)
    after_c = receive(joined, {"circ": 1}, dims, width)
    low_n, high_n = receive_pair(joined, {}, "normal", dims, width)
    low_lc, high_lc = receive_pair(joined, {"circ": -1}, "normal", dims, width)
    low_hc, high_hc = receive_pair(joined, {"circ": 1}, "normal", dims, width)
    top = jnp.concatenate([low_lc, low_n, low_hc], axis=3)
    middle = jnp.concatenate([before_c, joined, after_c], axis=3)
    bottom = jnp.concatenate([high_lc, high_n, high_hc], axis=3)
    plane = jnp.concatenate([top, middle, bottom], axis=2)
    before_s = receive(plane, {"span": -1}, dims, width)
    after_s = receive(plane, {"span": 1}, dims, width)
    return jnp.concatenate([before_s, plane, after_s], axis=1)


def flux_faces(stacked, halos, owner_jac, neighbor_jac):
    center = stacked[:5]
    total = jnp.zeros_like(center)
    for direction in range(3):
        dim = direction + 1
        before, after = halos[direction]
        line = jnp.concatenate([before, stacked, after], axis=dim)
        length = line.shape[dim]
        upper = lax.slice_in_dim(line[:5], 2, length, axis=dim)
        lower = lax.slice_in_dim(line[:5], 0, length - 2, axis=dim)
        w_here = stacked[5 + direction]
        w_lower = lax.slice_in_dim(line[5 + direction], 0, length - 2, axis=direction)
        up_term = w_here[None] * (center - upper)
        down_term = w_lower[None] * (lower - center)
        total = total + jnp.einsum(
            "uv,ukji->vkji", owner_jac[direction], up_term, precision=lax.Precision.HIGHEST
        )
        total = total + jnp.einsum(
            "uv,ukji->vkji", neighbor_jac[direction], down_term, precision=lax.Precision.HIGHEST
        )
    return total


def on_device(
    adjoint,
    objective_grad,
    face_weights,
    owner_jac,
    neighbor_jac,
    coupling,
    stiffness,
    wall_kernel,
    panel_owner,
):
    stacked = jnp.concatenate([adjoint, face_weights], axis=0)
    halos = [
        face_halos(stacked, "span", 1, False),
        face_halos(stacked, "normal", 2, False),
        face_halos(stacked, "circ", 3, True),
    ]
    residual = flux_faces(stacked, halos, owner_jac, neighbor_jac) + adjoint - objective_grad
    forcing = jnp.einsum("mv,vkji->mkji", coupling, residual, precision=lax.Precision.HIGHEST)
    margin = SWEEPS - 1
    joined = jnp.concatenate([stiffness[None], forcing], axis=0)
    full_pad = padded_sweeps(joined, margin)
    mesh = run_sweeps(full_pad[0], full_pad[1:])
    wall_sens = jnp.sum(wall_kernel[None] * mesh, axis=2)
    span = lax.axis_index("span")
    first = (span - 1) * PANEL_DEV
    local = panel_owner - first
    onehot = (
        local[:, :, None] == jnp.arange(3 * PANEL_DEV, dtype=jnp.int32)[None, None, :]
    ).astype(jnp.float32)
    terms = jnp.einsum("mki,kip->mp", wall_sens, onehot, precision=lax.Precision.HIGHEST)
    terms = lax.psum(terms, ("circ", "normal"))
    peers = lax.axis_size("span")
    up = [(i, i + 1) for i in range(peers - 1)]
    down = [(j, i) for i, j in up]
    from_below = lax.ppermute(terms[:, 2 * PANEL_DEV :], "span", up)
    from_above = lax.ppermute(terms[:, :PANEL_DEV], "span", down)
    panels = terms[:, PANEL_DEV : 2 * PANEL_DEV] + from_below + from_above
    return (residual, mesh, panels)


def solution(mesh):
    placed = (
        P(None, "span", "normal", "circ"),
        P(None, "span", "normal", "circ"),
        P(None, "span", "normal", "circ"),
        P(),
        P(),
        P(),
        P("span", "normal", "circ"),
        P("span", "normal", "circ"),
        P("span", "circ"),
    )
    return jax.shard_map(
        on_device,
        mesh=mesh,
        in_specs=placed,
        out_specs=(
            P(None, "span", "normal", "circ"),
            P(None, "span", "normal", "circ"),
            P(None, "span"),
        ),
        check_vma=False,
    )
```

```python
import itertools
import math

import jax
import jax.numpy as jnp
from jax import lax
from jax.sharding import PartitionSpec as P

PANEL_DEV = 128
SWEEPS = 4


def padded_2(array, sides, width, wrap):
    for axis, dim in sides:
        peers, length = (lax.axis_size(axis), array.shape[dim])
        up = [(i, (i + 1) % peers) for i in range(peers if wrap else peers - 1)]
        down = [(j, i) for i, j in up]
        last = lax.slice_in_dim(array, length - width, length, axis=dim)
        initial = lax.slice_in_dim(array, 0, width, axis=dim)
        before = lax.ppermute(last, axis, up)
        after = lax.ppermute(initial, axis, down)
        array = jnp.concatenate([before, array, after], axis=dim)
    return array


def neighbor_sum(padded):
    total = padded[:, 2:, 1:-1, 1:-1] + padded[:, :-2, 1:-1, 1:-1]
    total = total + padded[:, 1:-1, 2:, 1:-1] + padded[:, 1:-1, :-2, 1:-1]
    return total + padded[:, 1:-1, 1:-1, 2:] + padded[:, 1:-1, 1:-1, :-2]


def inner(field):
    return field[:, 1:-1, 1:-1, 1:-1]


def flux_transpose(padded, owner_jac, neighbor_jac):
    psi = padded[:5]
    weights = padded[5:]
    center = inner(psi)
    total = jnp.zeros_like(center)
    for direction in range(3):
        lower = [slice(None), slice(1, -1), slice(1, -1), slice(1, -1)]
        upper = [slice(None), slice(1, -1), slice(1, -1), slice(1, -1)]
        lower[direction + 1] = slice(0, -2)
        upper[direction + 1] = slice(2, None)
        w_here = weights[direction, 1:-1, 1:-1, 1:-1]
        w_lower = weights[direction][tuple(lower[1:])]
        up_term = w_here[None] * (center - psi[tuple(upper)])
        down_term = w_lower[None] * (psi[tuple(lower)] - center)
        total = total + jnp.einsum(
            "uv,ukji->vkji", owner_jac[direction], up_term, precision=lax.Precision.HIGHEST
        )
        total = total + jnp.einsum(
            "uv,ukji->vkji", neighbor_jac[direction], down_term, precision=lax.Precision.HIGHEST
        )
    return total


def relax(mesh_pad, stiff_pad, force_pad):
    weighted = stiff_pad[None] * mesh_pad
    stiff_in = stiff_pad[1:-1, 1:-1, 1:-1]
    diag_term = 6.0 * stiff_in + 1.0
    mesh_in = inner(mesh_pad)
    return (
        mesh_in
        + 0.8
        * (inner(force_pad) - diag_term[None] * mesh_in + neighbor_sum(weighted))
        / diag_term[None]
    )


def run_sweeps(stiff_pad, force_pad):
    mesh_pad = 0.8 * force_pad / (6.0 * stiff_pad[None] + 1.0)
    for sweep in range(1, SWEEPS):
        mesh_pad = relax(mesh_pad, stiff_pad, force_pad)
        stiff_pad = stiff_pad[1:-1, 1:-1, 1:-1]
        force_pad = inner(force_pad)
    return mesh_pad


ORDER = ("circ", "normal", "span")
WRAP = {"circ": True, "normal": False, "span": False}


def edge(array, dim, side, width):
    length = array.shape[dim]
    start = length - width if side < 0 else 0
    return lax.slice_in_dim(array, start, start + width, axis=dim)


def pairs_for(offsets, wrap=()):
    axes = [a for a in ORDER if a in offsets]
    sizes = [lax.axis_size(a) for a in axes]
    pairs = []
    for source in itertools.product(*[range(n) for n in sizes]):
        target, inside = [], True
        for axis, q, n in zip(axes, source, sizes):
            t = q + offsets[axis]
            if WRAP[axis] or axis in wrap:
                t %= n
            elif not 0 <= t < n:
                inside = False
            target.append(t)
        if inside:
            lin = lambda v: sum(x * math.prod(sizes[i + 1 :]) for i, x in enumerate(v))
            pairs.append((lin(source), lin(target)))
    return tuple(axes), pairs


def take(array, rel, dims, width):
    for axis, r in rel.items():
        if r:
            array = edge(array, dims[axis], r, width)
    return array


def receive(array, rel, dims, width):
    rel = {a: r for a, r in rel.items() if r}
    axes, pairs = pairs_for({a: -r for a, r in rel.items()})
    return lax.ppermute(take(array, rel, dims, width), axes, pairs)


def receive_pair(array, rel, axis, dims, width):
    low = dict(rel, **{axis: -1})
    high = dict(rel, **{axis: 1})
    if lax.axis_size(axis) != 2 or WRAP[axis]:
        return receive(array, low, dims, width), receive(array, high, dims, width)
    me = lax.axis_index(axis)
    sent = jnp.where(me == 0, take(array, low, dims, width), take(array, high, dims, width))
    low_nz = {a: r for a, r in low.items() if r}
    axes, pairs = pairs_for({a: -r for a, r in low_nz.items()})
    _, back = pairs_for({a: -r for a, r in dict(low_nz, **{axis: 1}).items()})
    got = lax.ppermute(sent, axes, pairs + back)
    zero = jnp.zeros_like(got)
    return jnp.where(me == 1, got, zero), jnp.where(me == 0, got, zero)


def face_halos(array, axis, dim, wrap):
    return receive_pair(array, {}, axis, {axis: dim}, 1)


def padded_sweeps(joined, width):
    dims = {"span": 1, "normal": 2, "circ": 3}
    before_c = receive(joined, {"circ": -1}, dims, width)
    after_c = receive(joined, {"circ": 1}, dims, width)
    low_n, high_n = receive_pair(joined, {}, "normal", dims, width)
    low_lc, high_lc = receive_pair(joined, {"circ": -1}, "normal", dims, width)
    low_hc, high_hc = receive_pair(joined, {"circ": 1}, "normal", dims, width)
    top = jnp.concatenate([low_lc, low_n, low_hc], axis=3)
    middle = jnp.concatenate([before_c, joined, after_c], axis=3)
    bottom = jnp.concatenate([high_lc, high_n, high_hc], axis=3)
    plane = jnp.concatenate([top, middle, bottom], axis=2)
    before_s = receive(plane, {"span": -1}, dims, width)
    after_s = receive(plane, {"span": 1}, dims, width)
    return jnp.concatenate([before_s, plane, after_s], axis=1)


def flux_faces(stacked, halos, owner_jac, neighbor_jac):
    center = stacked[:5]
    total = jnp.zeros_like(center)
    for direction in range(3):
        dim = direction + 1
        before, after = halos[direction]
        line = jnp.concatenate([before, stacked, after], axis=dim)
        length = line.shape[dim]
        upper = lax.slice_in_dim(line[:5], 2, length, axis=dim)
        lower = lax.slice_in_dim(line[:5], 0, length - 2, axis=dim)
        w_here = stacked[5 + direction]
        w_lower = lax.slice_in_dim(line[5 + direction], 0, length - 2, axis=direction)
        up_term = w_here[None] * (center - upper)
        down_term = w_lower[None] * (lower - center)
        total = total + jnp.einsum(
            "uv,ukji->vkji", owner_jac[direction], up_term, precision=lax.Precision.HIGHEST
        )
        total = total + jnp.einsum(
            "uv,ukji->vkji", neighbor_jac[direction], down_term, precision=lax.Precision.HIGHEST
        )
    return total


def shifted(array, offsets):
    axes, pairs = pairs_for(offsets, ("normal",))
    return lax.ppermute(array, axes, pairs)


def reduce_panels(terms):
    below, own, above = (terms[:, i * PANEL_DEV : (i + 1) * PANEL_DEV] for i in range(3))
    if lax.axis_size("normal") != 2 or lax.axis_size("circ") > 4:
        own = lax.psum(own + shifted(above, {"span": 1}) + shifted(below, {"span": -1}), ("circ", "normal"))
        return own
    partner = {"normal": 1}
    total = own + shifted(above, {"span": 1}) + shifted(below, {"span": -1})
    total = total + shifted(own, partner)
    total = total + shifted(above, dict(partner, span=1)) + shifted(below, dict(partner, span=-1))
    summed = total
    for step in range(1, lax.axis_size("circ")):
        summed = summed + shifted(total, {"circ": step})
    return summed


def on_device(
    adjoint,
    objective_grad,
    face_weights,
    owner_jac,
    neighbor_jac,
    coupling,
    stiffness,
    wall_kernel,
    panel_owner,
):
    stacked = jnp.concatenate([adjoint, face_weights], axis=0)
    halos = [
        face_halos(stacked, "span", 1, False),
        face_halos(stacked, "normal", 2, False),
        face_halos(stacked, "circ", 3, True),
    ]
    residual = flux_faces(stacked, halos, owner_jac, neighbor_jac) + adjoint - objective_grad
    forcing = jnp.einsum("mv,vkji->mkji", coupling, residual, precision=lax.Precision.HIGHEST)
    margin = SWEEPS - 1
    joined = jnp.concatenate([stiffness[None], forcing], axis=0)
    full_pad = padded_sweeps(joined, margin)
    mesh = run_sweeps(full_pad[0], full_pad[1:])
    wall_sens = jnp.sum(wall_kernel[None] * mesh, axis=2)
    span = lax.axis_index("span")
    first = (span - 1) * PANEL_DEV
    local = panel_owner - first
    onehot = (
        local[:, :, None] == jnp.arange(3 * PANEL_DEV, dtype=jnp.int32)[None, None, :]
    ).astype(jnp.float32)
    terms = jnp.einsum("mki,kip->mp", wall_sens, onehot, precision=lax.Precision.HIGHEST)
    panels = reduce_panels(terms)
    return (residual, mesh, panels)


def solution(mesh):
    placed = (
        P(None, "span", "normal", "circ"),
        P(None, "span", "normal", "circ"),
        P(None, "span", "normal", "circ"),
        P(),
        P(),
        P(),
        P("span", "normal", "circ"),
        P("span", "normal", "circ"),
        P("span", "circ"),
    )
    return jax.shard_map(
        on_device,
        mesh=mesh,
        in_specs=placed,
        out_specs=(
            P(None, "span", "normal", "circ"),
            P(None, "span", "normal", "circ"),
            P(None, "span"),
        ),
        check_vma=False,
    )
```

```python
import itertools
import math

import jax
import jax.numpy as jnp
from jax import lax
from jax.sharding import PartitionSpec as P

PANEL_DEV = 128
SWEEPS = 4


def padded_2(array, sides, width, wrap):
    for axis, dim in sides:
        peers, length = (lax.axis_size(axis), array.shape[dim])
        up = [(i, (i + 1) % peers) for i in range(peers if wrap else peers - 1)]
        down = [(j, i) for i, j in up]
        last = lax.slice_in_dim(array, length - width, length, axis=dim)
        initial = lax.slice_in_dim(array, 0, width, axis=dim)
        before = lax.ppermute(last, axis, up)
        after = lax.ppermute(initial, axis, down)
        array = jnp.concatenate([before, array, after], axis=dim)
    return array


def neighbor_sum(padded):
    total = padded[:, 2:, 1:-1, 1:-1] + padded[:, :-2, 1:-1, 1:-1]
    total = total + padded[:, 1:-1, 2:, 1:-1] + padded[:, 1:-1, :-2, 1:-1]
    return total + padded[:, 1:-1, 1:-1, 2:] + padded[:, 1:-1, 1:-1, :-2]


def inner(field):
    return field[:, 1:-1, 1:-1, 1:-1]


def flux_transpose(padded, owner_jac, neighbor_jac):
    psi = padded[:5]
    weights = padded[5:]
    center = inner(psi)
    total = jnp.zeros_like(center)
    for direction in range(3):
        lower = [slice(None), slice(1, -1), slice(1, -1), slice(1, -1)]
        upper = [slice(None), slice(1, -1), slice(1, -1), slice(1, -1)]
        lower[direction + 1] = slice(0, -2)
        upper[direction + 1] = slice(2, None)
        w_here = weights[direction, 1:-1, 1:-1, 1:-1]
        w_lower = weights[direction][tuple(lower[1:])]
        up_term = w_here[None] * (center - psi[tuple(upper)])
        down_term = w_lower[None] * (psi[tuple(lower)] - center)
        total = total + jnp.einsum(
            "uv,ukji->vkji", owner_jac[direction], up_term, precision=lax.Precision.HIGHEST
        )
        total = total + jnp.einsum(
            "uv,ukji->vkji", neighbor_jac[direction], down_term, precision=lax.Precision.HIGHEST
        )
    return total


def relax(mesh_pad, stiff_pad, force_pad):
    weighted = stiff_pad[None] * mesh_pad
    stiff_in = stiff_pad[1:-1, 1:-1, 1:-1]
    diag_term = 6.0 * stiff_in + 1.0
    mesh_in = inner(mesh_pad)
    return (
        mesh_in
        + 0.8
        * (inner(force_pad) - diag_term[None] * mesh_in + neighbor_sum(weighted))
        / diag_term[None]
    )


def run_sweeps(stiff_pad, force_pad):
    mesh_pad = 0.8 * force_pad / (6.0 * stiff_pad[None] + 1.0)
    for sweep in range(1, SWEEPS):
        mesh_pad = relax(mesh_pad, stiff_pad, force_pad)
        stiff_pad = stiff_pad[1:-1, 1:-1, 1:-1]
        force_pad = inner(force_pad)
    return mesh_pad


ORDER = ("circ", "normal", "span")
WRAP = {"circ": True, "normal": False, "span": False}


def edge(array, dim, side, width):
    length = array.shape[dim]
    start = length - width if side < 0 else 0
    return lax.slice_in_dim(array, start, start + width, axis=dim)


def pairs_for(offsets, wrap=()):
    axes = [a for a in ORDER if a in offsets]
    sizes = [lax.axis_size(a) for a in axes]
    pairs = []
    for source in itertools.product(*[range(n) for n in sizes]):
        target, inside = [], True
        for axis, q, n in zip(axes, source, sizes):
            t = q + offsets[axis]
            if WRAP[axis] or axis in wrap:
                t %= n
            elif not 0 <= t < n:
                inside = False
            target.append(t)
        if inside:
            lin = lambda v: sum(x * math.prod(sizes[i + 1 :]) for i, x in enumerate(v))
            pairs.append((lin(source), lin(target)))
    return tuple(axes), pairs


def take(array, rel, dims, width):
    for axis, r in rel.items():
        if r:
            array = edge(array, dims[axis], r, width)
    return array


def receive(array, rel, dims, width):
    rel = {a: r for a, r in rel.items() if r}
    axes, pairs = pairs_for({a: -r for a, r in rel.items()})
    return lax.ppermute(take(array, rel, dims, width), axes, pairs)


def receive_pair(array, rel, axis, dims, width):
    low = dict(rel, **{axis: -1})
    high = dict(rel, **{axis: 1})
    if lax.axis_size(axis) != 2 or WRAP[axis]:
        return receive(array, low, dims, width), receive(array, high, dims, width)
    me = lax.axis_index(axis)
    sent = jnp.where(me == 0, take(array, low, dims, width), take(array, high, dims, width))
    low_nz = {a: r for a, r in low.items() if r}
    axes, pairs = pairs_for({a: -r for a, r in low_nz.items()})
    _, back = pairs_for({a: -r for a, r in dict(low_nz, **{axis: 1}).items()})
    got = lax.ppermute(sent, axes, pairs + back)
    zero = jnp.zeros_like(got)
    return jnp.where(me == 1, got, zero), jnp.where(me == 0, got, zero)


def face_halos(array, axis, dim, wrap):
    return receive_pair(array, {}, axis, {axis: dim}, 1)


def padded_sweeps(joined, width):
    dims = {"span": 1, "normal": 2, "circ": 3}
    before_c = receive(joined, {"circ": -1}, dims, width)
    after_c = receive(joined, {"circ": 1}, dims, width)
    low_n, high_n = receive_pair(joined, {}, "normal", dims, width)
    low_lc, high_lc = receive_pair(joined, {"circ": -1}, "normal", dims, width)
    low_hc, high_hc = receive_pair(joined, {"circ": 1}, "normal", dims, width)
    top = jnp.concatenate([low_lc, low_n, low_hc], axis=3)
    middle = jnp.concatenate([before_c, joined, after_c], axis=3)
    bottom = jnp.concatenate([high_lc, high_n, high_hc], axis=3)
    plane = jnp.concatenate([top, middle, bottom], axis=2)
    before_s = receive(plane, {"span": -1}, dims, width)
    after_s = receive(plane, {"span": 1}, dims, width)
    return jnp.concatenate([before_s, plane, after_s], axis=1)


def jac_apply(jac, term):
    return jnp.einsum("uv,ukji->vkji", jac, term, precision=lax.Precision.HIGHEST)


def flux_faces(stacked, halos, owner_jac, neighbor_jac):
    psi = stacked[:5]
    inner_terms = []
    for direction in range(3):
        dim = direction + 1
        length = stacked.shape[dim]
        low = lax.slice_in_dim(psi, 0, length - 1, axis=dim)
        high = lax.slice_in_dim(psi, 1, length, axis=dim)
        w_low = lax.slice_in_dim(stacked[5 + direction], 0, length - 1, axis=direction)
        between = w_low[None] * (low - high)
        inner_terms.append((jac_apply(owner_jac[direction], between), jac_apply(neighbor_jac[direction], between)))
    inner_terms = lax.optimization_barrier(inner_terms)
    total = jnp.zeros_like(psi)
    for direction in range(3):
        dim = direction + 1
        length = stacked.shape[dim]
        before, after = halos[direction]
        last = lax.slice_in_dim(psi, length - 1, length, axis=dim)
        first = lax.slice_in_dim(psi, 0, 1, axis=dim)
        w_last = lax.slice_in_dim(stacked[5 + direction], length - 1, length, axis=direction)
        up_edge = w_last[None] * (last - after[:5])
        down_edge = before[5 + direction][None] * (before[:5] - first)
        up_inner, down_inner = inner_terms[direction]
        up = jnp.concatenate([up_inner, jac_apply(owner_jac[direction], up_edge)], axis=dim)
        down = jnp.concatenate([jac_apply(neighbor_jac[direction], down_edge), down_inner], axis=dim)
        total = total + up
        total = total + down
    return total


def shifted(array, offsets):
    axes, pairs = pairs_for(offsets, ("normal",))
    return lax.ppermute(array, axes, pairs)


def reduce_panels(terms):
    below, own, above = (terms[:, i * PANEL_DEV : (i + 1) * PANEL_DEV] for i in range(3))
    if lax.axis_size("normal") != 2 or lax.axis_size("circ") > 4:
        own = lax.psum(own + shifted(above, {"span": 1}) + shifted(below, {"span": -1}), ("circ", "normal"))
        return own
    partner = {"normal": 1}
    total = own + shifted(above, {"span": 1}) + shifted(below, {"span": -1})
    total = total + shifted(own, partner)
    total = total + shifted(above, dict(partner, span=1)) + shifted(below, dict(partner, span=-1))
    summed = total
    for step in range(1, lax.axis_size("circ")):
        summed = summed + shifted(total, {"circ": step})
    return summed


def on_device(
    adjoint,
    objective_grad,
    face_weights,
    owner_jac,
    neighbor_jac,
    coupling,
    stiffness,
    wall_kernel,
    panel_owner,
):
    stacked = jnp.concatenate([adjoint, face_weights], axis=0)
    halos = [
        face_halos(stacked, "span", 1, False),
        face_halos(stacked, "normal", 2, False),
        face_halos(stacked, "circ", 3, True),
    ]
    residual = flux_faces(stacked, halos, owner_jac, neighbor_jac) + adjoint - objective_grad
    forcing = jnp.einsum("mv,vkji->mkji", coupling, residual, precision=lax.Precision.HIGHEST)
    margin = SWEEPS - 1
    joined = jnp.concatenate([stiffness[None], forcing], axis=0)
    full_pad = padded_sweeps(joined, margin)
    mesh = run_sweeps(full_pad[0], full_pad[1:])
    wall_sens = jnp.sum(wall_kernel[None] * mesh, axis=2)
    span = lax.axis_index("span")
    first = (span - 1) * PANEL_DEV
    local = panel_owner - first
    onehot = (
        local[:, :, None] == jnp.arange(3 * PANEL_DEV, dtype=jnp.int32)[None, None, :]
    ).astype(jnp.float32)
    terms = jnp.einsum("mki,kip->mp", wall_sens, onehot, precision=lax.Precision.HIGHEST)
    panels = reduce_panels(terms)
    return (residual, mesh, panels)


def solution(mesh):
    placed = (
        P(None, "span", "normal", "circ"),
        P(None, "span", "normal", "circ"),
        P(None, "span", "normal", "circ"),
        P(),
        P(),
        P(),
        P("span", "normal", "circ"),
        P("span", "normal", "circ"),
        P("span", "circ"),
    )
    return jax.shard_map(
        on_device,
        mesh=mesh,
        in_specs=placed,
        out_specs=(
            P(None, "span", "normal", "circ"),
            P(None, "span", "normal", "circ"),
            P(None, "span"),
        ),
        check_vma=False,
    )
```

```python
import itertools
import math

import jax
import jax.numpy as jnp
from jax import lax
from jax.sharding import PartitionSpec as P

PANEL_DEV = 128
SWEEPS = 4


def padded_2(array, sides, width, wrap):
    for axis, dim in sides:
        peers, length = (lax.axis_size(axis), array.shape[dim])
        up = [(i, (i + 1) % peers) for i in range(peers if wrap else peers - 1)]
        down = [(j, i) for i, j in up]
        last = lax.slice_in_dim(array, length - width, length, axis=dim)
        initial = lax.slice_in_dim(array, 0, width, axis=dim)
        before = lax.ppermute(last, axis, up)
        after = lax.ppermute(initial, axis, down)
        array = jnp.concatenate([before, array, after], axis=dim)
    return array


def neighbor_sum(padded):
    total = padded[:, 2:, 1:-1, 1:-1] + padded[:, :-2, 1:-1, 1:-1]
    total = total + padded[:, 1:-1, 2:, 1:-1] + padded[:, 1:-1, :-2, 1:-1]
    return total + padded[:, 1:-1, 1:-1, 2:] + padded[:, 1:-1, 1:-1, :-2]


def inner(field):
    return field[:, 1:-1, 1:-1, 1:-1]


def flux_transpose(padded, owner_jac, neighbor_jac):
    psi = padded[:5]
    weights = padded[5:]
    center = inner(psi)
    total = jnp.zeros_like(center)
    for direction in range(3):
        lower = [slice(None), slice(1, -1), slice(1, -1), slice(1, -1)]
        upper = [slice(None), slice(1, -1), slice(1, -1), slice(1, -1)]
        lower[direction + 1] = slice(0, -2)
        upper[direction + 1] = slice(2, None)
        w_here = weights[direction, 1:-1, 1:-1, 1:-1]
        w_lower = weights[direction][tuple(lower[1:])]
        up_term = w_here[None] * (center - psi[tuple(upper)])
        down_term = w_lower[None] * (psi[tuple(lower)] - center)
        total = total + jnp.einsum(
            "uv,ukji->vkji", owner_jac[direction], up_term, precision=lax.Precision.HIGHEST
        )
        total = total + jnp.einsum(
            "uv,ukji->vkji", neighbor_jac[direction], down_term, precision=lax.Precision.HIGHEST
        )
    return total


def relax(mesh_pad, stiff_pad, force_pad):
    weighted = stiff_pad[None] * mesh_pad
    stiff_in = stiff_pad[1:-1, 1:-1, 1:-1]
    diag_term = 6.0 * stiff_in + 1.0
    mesh_in = inner(mesh_pad)
    return (
        mesh_in
        + 0.8
        * (inner(force_pad) - diag_term[None] * mesh_in + neighbor_sum(weighted))
        / diag_term[None]
    )


def run_sweeps(stiff_pad, force_pad):
    mesh_pad = 0.8 * force_pad / (6.0 * stiff_pad[None] + 1.0)
    for sweep in range(1, SWEEPS):
        mesh_pad = relax(mesh_pad, stiff_pad, force_pad)
        stiff_pad = stiff_pad[1:-1, 1:-1, 1:-1]
        force_pad = inner(force_pad)
    return mesh_pad


ORDER = ("circ", "normal", "span")
WRAP = {"circ": True, "normal": False, "span": False}


def edge(array, dim, side, width):
    length = array.shape[dim]
    start = length - width if side < 0 else 0
    return lax.slice_in_dim(array, start, start + width, axis=dim)


def pairs_for(offsets, wrap=()):
    axes = [a for a in ORDER if a in offsets]
    sizes = [lax.axis_size(a) for a in axes]
    pairs = []
    for source in itertools.product(*[range(n) for n in sizes]):
        target, inside = [], True
        for axis, q, n in zip(axes, source, sizes):
            t = q + offsets[axis]
            if WRAP[axis] or axis in wrap:
                t %= n
            elif not 0 <= t < n:
                inside = False
            target.append(t)
        if inside:
            lin = lambda v: sum(x * math.prod(sizes[i + 1 :]) for i, x in enumerate(v))
            pairs.append((lin(source), lin(target)))
    return tuple(axes), pairs


def take(array, rel, dims, width):
    for axis, r in rel.items():
        if r:
            array = edge(array, dims[axis], r, width)
    return array


def receive(array, rel, dims, width):
    rel = {a: r for a, r in rel.items() if r}
    axes, pairs = pairs_for({a: -r for a, r in rel.items()})
    return lax.ppermute(take(array, rel, dims, width), axes, pairs)


def receive_pair(array, rel, axis, dims, width):
    low = dict(rel, **{axis: -1})
    high = dict(rel, **{axis: 1})
    if lax.axis_size(axis) != 2 or WRAP[axis]:
        return receive(array, low, dims, width), receive(array, high, dims, width)
    me = lax.axis_index(axis)
    sent = jnp.where(me == 0, take(array, low, dims, width), take(array, high, dims, width))
    low_nz = {a: r for a, r in low.items() if r}
    axes, pairs = pairs_for({a: -r for a, r in low_nz.items()})
    _, back = pairs_for({a: -r for a, r in dict(low_nz, **{axis: 1}).items()})
    got = lax.ppermute(sent, axes, pairs + back)
    zero = jnp.zeros_like(got)
    return jnp.where(me == 1, got, zero), jnp.where(me == 0, got, zero)


def face_halos(array, axis, dim, wrap):
    return receive_pair(array, {}, axis, {axis: dim}, 1)


def padded_sweeps(joined, width):
    dims = {"span": 1, "normal": 2, "circ": 3}
    before_c = receive(joined, {"circ": -1}, dims, width)
    after_c = receive(joined, {"circ": 1}, dims, width)
    low_n, high_n = receive_pair(joined, {}, "normal", dims, width)
    low_lc, high_lc = receive_pair(joined, {"circ": -1}, "normal", dims, width)
    low_hc, high_hc = receive_pair(joined, {"circ": 1}, "normal", dims, width)
    top = jnp.concatenate([low_lc, low_n, low_hc], axis=3)
    middle = jnp.concatenate([before_c, joined, after_c], axis=3)
    bottom = jnp.concatenate([high_lc, high_n, high_hc], axis=3)
    plane = jnp.concatenate([top, middle, bottom], axis=2)
    before_s = receive(plane, {"span": -1}, dims, width)
    after_s = receive(plane, {"span": 1}, dims, width)
    return jnp.concatenate([before_s, plane, after_s], axis=1)


def jac_apply(jac, term):
    rows = []
    for v in range(jac.shape[1]):
        acc = jac[0, v] * term[0]
        for u in range(1, jac.shape[0]):
            acc = acc + jac[u, v] * term[u]
        rows.append(acc)
    return jnp.stack(rows)


def flux_faces(stacked, halos, owner_jac, neighbor_jac):
    psi = stacked[:5]
    inner_terms = []
    for direction in range(3):
        dim = direction + 1
        length = stacked.shape[dim]
        low = lax.slice_in_dim(psi, 0, length - 1, axis=dim)
        high = lax.slice_in_dim(psi, 1, length, axis=dim)
        w_low = lax.slice_in_dim(stacked[5 + direction], 0, length - 1, axis=direction)
        between = w_low[None] * (low - high)
        inner_terms.append((jac_apply(owner_jac[direction], between), jac_apply(neighbor_jac[direction], between)))
    inner_terms = lax.optimization_barrier(inner_terms)
    total = jnp.zeros_like(psi)
    for direction in range(3):
        dim = direction + 1
        length = stacked.shape[dim]
        before, after = halos[direction]
        last = lax.slice_in_dim(psi, length - 1, length, axis=dim)
        first = lax.slice_in_dim(psi, 0, 1, axis=dim)
        w_last = lax.slice_in_dim(stacked[5 + direction], length - 1, length, axis=direction)
        up_edge = w_last[None] * (last - after[:5])
        down_edge = before[5 + direction][None] * (before[:5] - first)
        up_inner, down_inner = inner_terms[direction]
        up = jnp.concatenate([up_inner, jac_apply(owner_jac[direction], up_edge)], axis=dim)
        down = jnp.concatenate([jac_apply(neighbor_jac[direction], down_edge), down_inner], axis=dim)
        total = total + up
        total = total + down
    return total


def shifted(array, offsets):
    axes, pairs = pairs_for(offsets, ("normal",))
    return lax.ppermute(array, axes, pairs)


def reduce_panels(terms):
    below, own, above = (terms[:, i * PANEL_DEV : (i + 1) * PANEL_DEV] for i in range(3))
    if lax.axis_size("normal") != 2 or lax.axis_size("circ") > 4:
        own = lax.psum(own + shifted(above, {"span": 1}) + shifted(below, {"span": -1}), ("circ", "normal"))
        return own
    partner = {"normal": 1}
    total = own + shifted(above, {"span": 1}) + shifted(below, {"span": -1})
    total = total + shifted(own, partner)
    total = total + shifted(above, dict(partner, span=1)) + shifted(below, dict(partner, span=-1))
    summed = total
    for step in range(1, lax.axis_size("circ")):
        summed = summed + shifted(total, {"circ": step})
    return summed


def on_device(
    adjoint,
    objective_grad,
    face_weights,
    owner_jac,
    neighbor_jac,
    coupling,
    stiffness,
    wall_kernel,
    panel_owner,
):
    stacked = jnp.concatenate([adjoint, face_weights], axis=0)
    halos = [
        face_halos(stacked, "span", 1, False),
        face_halos(stacked, "normal", 2, False),
        face_halos(stacked, "circ", 3, True),
    ]
    residual = flux_faces(stacked, halos, owner_jac, neighbor_jac) + adjoint - objective_grad
    forcing = jac_apply(coupling.T, residual)
    margin = SWEEPS - 1
    joined = jnp.concatenate([stiffness[None], forcing], axis=0)
    full_pad = padded_sweeps(joined, margin)
    mesh = run_sweeps(full_pad[0], full_pad[1:])
    wall_sens = jnp.sum(wall_kernel[None] * mesh, axis=2)
    span = lax.axis_index("span")
    first = (span - 1) * PANEL_DEV
    local = panel_owner - first
    onehot = (
        local[:, :, None] == jnp.arange(3 * PANEL_DEV, dtype=jnp.int32)[None, None, :]
    ).astype(jnp.float32)
    terms = jnp.einsum("mki,kip->mp", wall_sens, onehot, precision=lax.Precision.HIGHEST)
    panels = reduce_panels(terms)
    return (residual, mesh, panels)


def solution(mesh):
    placed = (
        P(None, "span", "normal", "circ"),
        P(None, "span", "normal", "circ"),
        P(None, "span", "normal", "circ"),
        P(),
        P(),
        P(),
        P("span", "normal", "circ"),
        P("span", "normal", "circ"),
        P("span", "circ"),
    )
    return jax.shard_map(
        on_device,
        mesh=mesh,
        in_specs=placed,
        out_specs=(
            P(None, "span", "normal", "circ"),
            P(None, "span", "normal", "circ"),
            P(None, "span"),
        ),
        check_vma=False,
    )
```

```python
import itertools
import math

import jax
import jax.numpy as jnp
from jax import lax
from jax.sharding import PartitionSpec as P

PANEL_DEV = 128
SWEEPS = 4


def padded_2(array, sides, width, wrap):
    for axis, dim in sides:
        peers, length = (lax.axis_size(axis), array.shape[dim])
        up = [(i, (i + 1) % peers) for i in range(peers if wrap else peers - 1)]
        down = [(j, i) for i, j in up]
        last = lax.slice_in_dim(array, length - width, length, axis=dim)
        initial = lax.slice_in_dim(array, 0, width, axis=dim)
        before = lax.ppermute(last, axis, up)
        after = lax.ppermute(initial, axis, down)
        array = jnp.concatenate([before, array, after], axis=dim)
    return array


def neighbor_sum(padded):
    total = padded[:, 2:, 1:-1, 1:-1] + padded[:, :-2, 1:-1, 1:-1]
    total = total + padded[:, 1:-1, 2:, 1:-1] + padded[:, 1:-1, :-2, 1:-1]
    return total + padded[:, 1:-1, 1:-1, 2:] + padded[:, 1:-1, 1:-1, :-2]


def inner(field):
    return field[:, 1:-1, 1:-1, 1:-1]


def flux_transpose(padded, owner_jac, neighbor_jac):
    psi = padded[:5]
    weights = padded[5:]
    center = inner(psi)
    total = jnp.zeros_like(center)
    for direction in range(3):
        lower = [slice(None), slice(1, -1), slice(1, -1), slice(1, -1)]
        upper = [slice(None), slice(1, -1), slice(1, -1), slice(1, -1)]
        lower[direction + 1] = slice(0, -2)
        upper[direction + 1] = slice(2, None)
        w_here = weights[direction, 1:-1, 1:-1, 1:-1]
        w_lower = weights[direction][tuple(lower[1:])]
        up_term = w_here[None] * (center - psi[tuple(upper)])
        down_term = w_lower[None] * (psi[tuple(lower)] - center)
        total = total + jnp.einsum(
            "uv,ukji->vkji", owner_jac[direction], up_term, precision=lax.Precision.HIGHEST
        )
        total = total + jnp.einsum(
            "uv,ukji->vkji", neighbor_jac[direction], down_term, precision=lax.Precision.HIGHEST
        )
    return total


def relax(mesh_pad, stiff_pad, force_pad):
    weighted = stiff_pad[None] * mesh_pad
    stiff_in = stiff_pad[1:-1, 1:-1, 1:-1]
    diag_term = 6.0 * stiff_in + 1.0
    mesh_in = inner(mesh_pad)
    return (
        mesh_in
        + 0.8
        * (inner(force_pad) - diag_term[None] * mesh_in + neighbor_sum(weighted))
        / diag_term[None]
    )


def run_sweeps(stiff_pad, force_pad):
    mesh_pad = 0.8 * force_pad / (6.0 * stiff_pad[None] + 1.0)
    for sweep in range(1, SWEEPS):
        mesh_pad = relax(mesh_pad, stiff_pad, force_pad)
        stiff_pad = stiff_pad[1:-1, 1:-1, 1:-1]
        force_pad = inner(force_pad)
    return mesh_pad


ORDER = ("circ", "normal", "span")
WRAP = {"circ": True, "normal": False, "span": False}


def edge(array, dim, side, width):
    length = array.shape[dim]
    start = length - width if side < 0 else 0
    return lax.slice_in_dim(array, start, start + width, axis=dim)


def pairs_for(offsets, wrap=()):
    axes = [a for a in ORDER if a in offsets]
    sizes = [lax.axis_size(a) for a in axes]
    pairs = []
    for source in itertools.product(*[range(n) for n in sizes]):
        target, inside = [], True
        for axis, q, n in zip(axes, source, sizes):
            t = q + offsets[axis]
            if WRAP[axis] or axis in wrap:
                t %= n
            elif not 0 <= t < n:
                inside = False
            target.append(t)
        if inside:
            lin = lambda v: sum(x * math.prod(sizes[i + 1 :]) for i, x in enumerate(v))
            pairs.append((lin(source), lin(target)))
    return tuple(axes), pairs


def take(array, rel, dims, width):
    for axis, r in rel.items():
        if r:
            array = edge(array, dims[axis], r, width)
    return array


def receive(array, rel, dims, width):
    rel = {a: r for a, r in rel.items() if r}
    axes, pairs = pairs_for({a: -r for a, r in rel.items()})
    return lax.ppermute(take(array, rel, dims, width), axes, pairs)


def receive_pair(array, rel, axis, dims, width):
    low = dict(rel, **{axis: -1})
    high = dict(rel, **{axis: 1})
    if lax.axis_size(axis) != 2 or WRAP[axis]:
        return receive(array, low, dims, width), receive(array, high, dims, width)
    me = lax.axis_index(axis)
    sent = jnp.where(me == 0, take(array, low, dims, width), take(array, high, dims, width))
    low_nz = {a: r for a, r in low.items() if r}
    axes, pairs = pairs_for({a: -r for a, r in low_nz.items()})
    _, back = pairs_for({a: -r for a, r in dict(low_nz, **{axis: 1}).items()})
    got = lax.ppermute(sent, axes, pairs + back)
    zero = jnp.zeros_like(got)
    return jnp.where(me == 1, got, zero), jnp.where(me == 0, got, zero)


def face_halos(array, axis, dim, wrap):
    return receive_pair(array, {}, axis, {axis: dim}, 1)


def padded_sweeps(joined, width):
    dims = {"span": 1, "normal": 2, "circ": 3}
    before_c = receive(joined, {"circ": -1}, dims, width)
    after_c = receive(joined, {"circ": 1}, dims, width)
    low_n, high_n = receive_pair(joined, {}, "normal", dims, width)
    low_lc, high_lc = receive_pair(joined, {"circ": -1}, "normal", dims, width)
    low_hc, high_hc = receive_pair(joined, {"circ": 1}, "normal", dims, width)
    top = jnp.concatenate([low_lc, low_n, low_hc], axis=3)
    middle = jnp.concatenate([before_c, joined, after_c], axis=3)
    bottom = jnp.concatenate([high_lc, high_n, high_hc], axis=3)
    plane = jnp.concatenate([top, middle, bottom], axis=2)
    before_s = receive(plane, {"span": -1}, dims, width)
    after_s = receive(plane, {"span": 1}, dims, width)
    return jnp.concatenate([before_s, plane, after_s], axis=1)


def jac_apply(jac, term):
    spread = (slice(None), slice(None)) + (None,) * (term.ndim - 1)
    return jnp.sum(jac[spread] * term[:, None], axis=0)


def flux_faces(stacked, halos, owner_jac, neighbor_jac):
    psi = stacked[:5]
    inner_terms = []
    for direction in range(3):
        dim = direction + 1
        length = stacked.shape[dim]
        low = lax.slice_in_dim(psi, 0, length - 1, axis=dim)
        high = lax.slice_in_dim(psi, 1, length, axis=dim)
        w_low = lax.slice_in_dim(stacked[5 + direction], 0, length - 1, axis=direction)
        between = w_low[None] * (low - high)
        inner_terms.append((jac_apply(owner_jac[direction], between), jac_apply(neighbor_jac[direction], between)))
    inner_terms = lax.optimization_barrier(inner_terms)
    total = jnp.zeros_like(psi)
    for direction in range(3):
        dim = direction + 1
        length = stacked.shape[dim]
        before, after = halos[direction]
        last = lax.slice_in_dim(psi, length - 1, length, axis=dim)
        first = lax.slice_in_dim(psi, 0, 1, axis=dim)
        w_last = lax.slice_in_dim(stacked[5 + direction], length - 1, length, axis=direction)
        up_edge = w_last[None] * (last - after[:5])
        down_edge = before[5 + direction][None] * (before[:5] - first)
        up_inner, down_inner = inner_terms[direction]
        up = jnp.concatenate([up_inner, jac_apply(owner_jac[direction], up_edge)], axis=dim)
        down = jnp.concatenate([jac_apply(neighbor_jac[direction], down_edge), down_inner], axis=dim)
        total = total + up
        total = total + down
    return total


def shifted(array, offsets):
    axes, pairs = pairs_for(offsets, ("normal",))
    return lax.ppermute(array, axes, pairs)


def reduce_panels(terms):
    below, own, above = (terms[:, i * PANEL_DEV : (i + 1) * PANEL_DEV] for i in range(3))
    if lax.axis_size("normal") != 2 or lax.axis_size("circ") > 4:
        own = lax.psum(own + shifted(above, {"span": 1}) + shifted(below, {"span": -1}), ("circ", "normal"))
        return own
    partner = {"normal": 1}
    total = own + shifted(above, {"span": 1}) + shifted(below, {"span": -1})
    total = total + shifted(own, partner)
    total = total + shifted(above, dict(partner, span=1)) + shifted(below, dict(partner, span=-1))
    summed = total
    for step in range(1, lax.axis_size("circ")):
        summed = summed + shifted(total, {"circ": step})
    return summed


def on_device(
    adjoint,
    objective_grad,
    face_weights,
    owner_jac,
    neighbor_jac,
    coupling,
    stiffness,
    wall_kernel,
    panel_owner,
):
    stacked = jnp.concatenate([adjoint, face_weights], axis=0)
    halos = [
        face_halos(stacked, "span", 1, False),
        face_halos(stacked, "normal", 2, False),
        face_halos(stacked, "circ", 3, True),
    ]
    residual = flux_faces(stacked, halos, owner_jac, neighbor_jac) + adjoint - objective_grad
    forcing = jac_apply(coupling.T, residual)
    margin = SWEEPS - 1
    joined = jnp.concatenate([stiffness[None], forcing], axis=0)
    full_pad = padded_sweeps(joined, margin)
    mesh = run_sweeps(full_pad[0], full_pad[1:])
    wall_sens = jnp.sum(wall_kernel[None] * mesh, axis=2)
    span = lax.axis_index("span")
    first = (span - 1) * PANEL_DEV
    local = panel_owner - first
    onehot = (
        local[:, :, None] == jnp.arange(3 * PANEL_DEV, dtype=jnp.int32)[None, None, :]
    ).astype(jnp.float32)
    terms = jnp.einsum("mki,kip->mp", wall_sens, onehot, precision=lax.Precision.HIGHEST)
    panels = reduce_panels(terms)
    return (residual, mesh, panels)


def solution(mesh):
    placed = (
        P(None, "span", "normal", "circ"),
        P(None, "span", "normal", "circ"),
        P(None, "span", "normal", "circ"),
        P(),
        P(),
        P(),
        P("span", "normal", "circ"),
        P("span", "normal", "circ"),
        P("span", "circ"),
    )
    return jax.shard_map(
        on_device,
        mesh=mesh,
        in_specs=placed,
        out_specs=(
            P(None, "span", "normal", "circ"),
            P(None, "span", "normal", "circ"),
            P(None, "span"),
        ),
        check_vma=False,
    )
```

```python
import itertools
import math

import jax
import jax.numpy as jnp
from jax import lax
from jax.sharding import PartitionSpec as P

PANEL_DEV = 128
SWEEPS = 4


def padded_2(array, sides, width, wrap):
    for axis, dim in sides:
        peers, length = (lax.axis_size(axis), array.shape[dim])
        up = [(i, (i + 1) % peers) for i in range(peers if wrap else peers - 1)]
        down = [(j, i) for i, j in up]
        last = lax.slice_in_dim(array, length - width, length, axis=dim)
        initial = lax.slice_in_dim(array, 0, width, axis=dim)
        before = lax.ppermute(last, axis, up)
        after = lax.ppermute(initial, axis, down)
        array = jnp.concatenate([before, array, after], axis=dim)
    return array


def neighbor_sum(padded):
    total = padded[:, 2:, 1:-1, 1:-1] + padded[:, :-2, 1:-1, 1:-1]
    total = total + padded[:, 1:-1, 2:, 1:-1] + padded[:, 1:-1, :-2, 1:-1]
    return total + padded[:, 1:-1, 1:-1, 2:] + padded[:, 1:-1, 1:-1, :-2]


def inner(field):
    return field[:, 1:-1, 1:-1, 1:-1]


def flux_transpose(padded, owner_jac, neighbor_jac):
    psi = padded[:5]
    weights = padded[5:]
    center = inner(psi)
    total = jnp.zeros_like(center)
    for direction in range(3):
        lower = [slice(None), slice(1, -1), slice(1, -1), slice(1, -1)]
        upper = [slice(None), slice(1, -1), slice(1, -1), slice(1, -1)]
        lower[direction + 1] = slice(0, -2)
        upper[direction + 1] = slice(2, None)
        w_here = weights[direction, 1:-1, 1:-1, 1:-1]
        w_lower = weights[direction][tuple(lower[1:])]
        up_term = w_here[None] * (center - psi[tuple(upper)])
        down_term = w_lower[None] * (psi[tuple(lower)] - center)
        total = total + jnp.einsum(
            "uv,ukji->vkji", owner_jac[direction], up_term, precision=lax.Precision.HIGHEST
        )
        total = total + jnp.einsum(
            "uv,ukji->vkji", neighbor_jac[direction], down_term, precision=lax.Precision.HIGHEST
        )
    return total


def relax(mesh_pad, stiff_pad, force_pad):
    weighted = stiff_pad[None] * mesh_pad
    stiff_in = stiff_pad[1:-1, 1:-1, 1:-1]
    diag_term = 6.0 * stiff_in + 1.0
    mesh_in = inner(mesh_pad)
    return (
        mesh_in
        + 0.8
        * (inner(force_pad) - diag_term[None] * mesh_in + neighbor_sum(weighted))
        / diag_term[None]
    )


def run_sweeps(stiff_pad, force_pad):
    mesh_pad = 0.8 * force_pad / (6.0 * stiff_pad[None] + 1.0)
    for sweep in range(1, SWEEPS):
        mesh_pad = relax(mesh_pad, stiff_pad, force_pad)
        stiff_pad = stiff_pad[1:-1, 1:-1, 1:-1]
        force_pad = inner(force_pad)
    return mesh_pad


ORDER = ("circ", "normal", "span")
WRAP = {"circ": True, "normal": False, "span": False}


def edge(array, dim, side, width):
    length = array.shape[dim]
    start = length - width if side < 0 else 0
    return lax.slice_in_dim(array, start, start + width, axis=dim)


def pairs_for(offsets, wrap=()):
    axes = [a for a in ORDER if a in offsets]
    sizes = [lax.axis_size(a) for a in axes]
    pairs = []
    for source in itertools.product(*[range(n) for n in sizes]):
        target, inside = [], True
        for axis, q, n in zip(axes, source, sizes):
            t = q + offsets[axis]
            if WRAP[axis] or axis in wrap:
                t %= n
            elif not 0 <= t < n:
                inside = False
            target.append(t)
        if inside:
            lin = lambda v: sum(x * math.prod(sizes[i + 1 :]) for i, x in enumerate(v))
            pairs.append((lin(source), lin(target)))
    return tuple(axes), pairs


def take(array, rel, dims, width):
    for axis, r in rel.items():
        if r:
            array = edge(array, dims[axis], r, width)
    return array


def receive(array, rel, dims, width):
    rel = {a: r for a, r in rel.items() if r}
    axes, pairs = pairs_for({a: -r for a, r in rel.items()})
    return lax.ppermute(take(array, rel, dims, width), axes, pairs)


def receive_pair(array, rel, axis, dims, width):
    low = dict(rel, **{axis: -1})
    high = dict(rel, **{axis: 1})
    if lax.axis_size(axis) != 2 or WRAP[axis]:
        return receive(array, low, dims, width), receive(array, high, dims, width)
    me = lax.axis_index(axis)
    sent = jnp.where(me == 0, take(array, low, dims, width), take(array, high, dims, width))
    low_nz = {a: r for a, r in low.items() if r}
    axes, pairs = pairs_for({a: -r for a, r in low_nz.items()})
    _, back = pairs_for({a: -r for a, r in dict(low_nz, **{axis: 1}).items()})
    got = lax.ppermute(sent, axes, pairs + back)
    zero = jnp.zeros_like(got)
    return jnp.where(me == 1, got, zero), jnp.where(me == 0, got, zero)


def face_halos(fields, axis, dim, wrap):
    thin = jnp.concatenate(
        [jnp.concatenate([edge(f, dim, 1, 1), edge(f, dim, -1, 1)], axis=dim) for f in fields], axis=0
    )
    return receive_pair(thin, {}, axis, {axis: dim}, 1)


def padded_sweeps(joined, width):
    dims = {"span": 1, "normal": 2, "circ": 3}
    before_c = receive(joined, {"circ": -1}, dims, width)
    after_c = receive(joined, {"circ": 1}, dims, width)
    low_n, high_n = receive_pair(joined, {}, "normal", dims, width)
    low_lc, high_lc = receive_pair(joined, {"circ": -1}, "normal", dims, width)
    low_hc, high_hc = receive_pair(joined, {"circ": 1}, "normal", dims, width)
    top = jnp.concatenate([low_lc, low_n, low_hc], axis=3)
    middle = jnp.concatenate([before_c, joined, after_c], axis=3)
    bottom = jnp.concatenate([high_lc, high_n, high_hc], axis=3)
    plane = jnp.concatenate([top, middle, bottom], axis=2)
    before_s = receive(plane, {"span": -1}, dims, width)
    after_s = receive(plane, {"span": 1}, dims, width)
    return jnp.concatenate([before_s, plane, after_s], axis=1)


def jac_apply(jac, term):
    spread = (slice(None), slice(None)) + (None,) * (term.ndim - 1)
    return jnp.sum(jac[spread] * term[:, None], axis=0)


def flux_faces(psi, weights, halos, owner_jac, neighbor_jac):
    inner_terms = []
    for direction in range(3):
        dim = direction + 1
        length = psi.shape[dim]
        low = lax.slice_in_dim(psi, 0, length - 1, axis=dim)
        high = lax.slice_in_dim(psi, 1, length, axis=dim)
        w_low = lax.slice_in_dim(weights[direction], 0, length - 1, axis=direction)
        between = w_low[None] * (low - high)
        inner_terms.append((jac_apply(owner_jac[direction], between), jac_apply(neighbor_jac[direction], between)))
    inner_terms = lax.optimization_barrier(inner_terms)
    total = jnp.zeros_like(psi)
    for direction in range(3):
        dim = direction + 1
        length = psi.shape[dim]
        before, after = halos[direction]
        last = lax.slice_in_dim(psi, length - 1, length, axis=dim)
        first = lax.slice_in_dim(psi, 0, 1, axis=dim)
        w_last = lax.slice_in_dim(weights[direction], length - 1, length, axis=direction)
        up_edge = w_last[None] * (last - after[:5])
        down_edge = before[5 + direction][None] * (before[:5] - first)
        up_inner, down_inner = inner_terms[direction]
        up = jnp.concatenate([up_inner, jac_apply(owner_jac[direction], up_edge)], axis=dim)
        down = jnp.concatenate([jac_apply(neighbor_jac[direction], down_edge), down_inner], axis=dim)
        total = total + up
        total = total + down
    return total


def shifted(array, offsets):
    axes, pairs = pairs_for(offsets, ("normal",))
    return lax.ppermute(array, axes, pairs)


def reduce_panels(terms):
    below, own, above = (terms[:, i * PANEL_DEV : (i + 1) * PANEL_DEV] for i in range(3))
    if lax.axis_size("normal") != 2 or lax.axis_size("circ") > 4:
        own = lax.psum(own + shifted(above, {"span": 1}) + shifted(below, {"span": -1}), ("circ", "normal"))
        return own
    partner = {"normal": 1}
    total = own + shifted(above, {"span": 1}) + shifted(below, {"span": -1})
    total = total + shifted(own, partner)
    total = total + shifted(above, dict(partner, span=1)) + shifted(below, dict(partner, span=-1))
    summed = total
    for step in range(1, lax.axis_size("circ")):
        summed = summed + shifted(total, {"circ": step})
    return summed


def on_device(
    adjoint,
    objective_grad,
    face_weights,
    owner_jac,
    neighbor_jac,
    coupling,
    stiffness,
    wall_kernel,
    panel_owner,
):
    fields = (adjoint, face_weights)
    halos = [
        face_halos(fields, "span", 1, False),
        face_halos(fields, "normal", 2, False),
        face_halos(fields, "circ", 3, True),
    ]
    residual = flux_faces(adjoint, face_weights, halos, owner_jac, neighbor_jac) + adjoint - objective_grad
    forcing = jac_apply(coupling.T, residual)
    margin = SWEEPS - 1
    joined = jnp.concatenate([stiffness[None], forcing], axis=0)
    full_pad = padded_sweeps(joined, margin)
    mesh = run_sweeps(full_pad[0], full_pad[1:])
    wall_sens = jnp.sum(wall_kernel[None] * mesh, axis=2)
    span = lax.axis_index("span")
    first = (span - 1) * PANEL_DEV
    local = panel_owner - first
    onehot = (
        local[:, :, None] == jnp.arange(3 * PANEL_DEV, dtype=jnp.int32)[None, None, :]
    ).astype(jnp.float32)
    terms = jnp.einsum("mki,kip->mp", wall_sens, onehot, precision=lax.Precision.HIGHEST)
    panels = reduce_panels(terms)
    return (residual, mesh, panels)


def solution(mesh):
    placed = (
        P(None, "span", "normal", "circ"),
        P(None, "span", "normal", "circ"),
        P(None, "span", "normal", "circ"),
        P(),
        P(),
        P(),
        P("span", "normal", "circ"),
        P("span", "normal", "circ"),
        P("span", "circ"),
    )
    return jax.shard_map(
        on_device,
        mesh=mesh,
        in_specs=placed,
        out_specs=(
            P(None, "span", "normal", "circ"),
            P(None, "span", "normal", "circ"),
            P(None, "span"),
        ),
        check_vma=False,
    )
```

```python
import itertools
import math

import jax
import jax.numpy as jnp
from jax import lax
from jax.sharding import PartitionSpec as P

PANEL_DEV = 128
SWEEPS = 4


def padded_2(array, sides, width, wrap):
    for axis, dim in sides:
        peers, length = (lax.axis_size(axis), array.shape[dim])
        up = [(i, (i + 1) % peers) for i in range(peers if wrap else peers - 1)]
        down = [(j, i) for i, j in up]
        last = lax.slice_in_dim(array, length - width, length, axis=dim)
        initial = lax.slice_in_dim(array, 0, width, axis=dim)
        before = lax.ppermute(last, axis, up)
        after = lax.ppermute(initial, axis, down)
        array = jnp.concatenate([before, array, after], axis=dim)
    return array


def neighbor_sum(padded):
    total = padded[:, 2:, 1:-1, 1:-1] + padded[:, :-2, 1:-1, 1:-1]
    total = total + padded[:, 1:-1, 2:, 1:-1] + padded[:, 1:-1, :-2, 1:-1]
    return total + padded[:, 1:-1, 1:-1, 2:] + padded[:, 1:-1, 1:-1, :-2]


def inner(field):
    return field[:, 1:-1, 1:-1, 1:-1]


def flux_transpose(padded, owner_jac, neighbor_jac):
    psi = padded[:5]
    weights = padded[5:]
    center = inner(psi)
    total = jnp.zeros_like(center)
    for direction in range(3):
        lower = [slice(None), slice(1, -1), slice(1, -1), slice(1, -1)]
        upper = [slice(None), slice(1, -1), slice(1, -1), slice(1, -1)]
        lower[direction + 1] = slice(0, -2)
        upper[direction + 1] = slice(2, None)
        w_here = weights[direction, 1:-1, 1:-1, 1:-1]
        w_lower = weights[direction][tuple(lower[1:])]
        up_term = w_here[None] * (center - psi[tuple(upper)])
        down_term = w_lower[None] * (psi[tuple(lower)] - center)
        total = total + jnp.einsum(
            "uv,ukji->vkji", owner_jac[direction], up_term, precision=lax.Precision.HIGHEST
        )
        total = total + jnp.einsum(
            "uv,ukji->vkji", neighbor_jac[direction], down_term, precision=lax.Precision.HIGHEST
        )
    return total


def relax(mesh_pad, stiff_pad, force_pad):
    weighted = stiff_pad[None] * mesh_pad
    stiff_in = stiff_pad[1:-1, 1:-1, 1:-1]
    diag_term = 6.0 * stiff_in + 1.0
    mesh_in = inner(mesh_pad)
    return (
        mesh_in
        + 0.8
        * (inner(force_pad) - diag_term[None] * mesh_in + neighbor_sum(weighted))
        / diag_term[None]
    )


def run_sweeps(stiff_pad, force_pad):
    mesh_pad = 0.8 * force_pad / (6.0 * stiff_pad[None] + 1.0)
    for sweep in range(1, SWEEPS):
        mesh_pad = relax(mesh_pad, stiff_pad, force_pad)
        stiff_pad = stiff_pad[1:-1, 1:-1, 1:-1]
        force_pad = inner(force_pad)
    return mesh_pad


ORDER = ("circ", "normal", "span")
WRAP = {"circ": True, "normal": False, "span": False}


def edge(array, dim, side, width):
    length = array.shape[dim]
    start = length - width if side < 0 else 0
    return lax.slice_in_dim(array, start, start + width, axis=dim)


def pairs_for(offsets, wrap=()):
    axes = [a for a in ORDER if a in offsets]
    sizes = [lax.axis_size(a) for a in axes]
    pairs = []
    for source in itertools.product(*[range(n) for n in sizes]):
        target, inside = [], True
        for axis, q, n in zip(axes, source, sizes):
            t = q + offsets[axis]
            if WRAP[axis] or axis in wrap:
                t %= n
            elif not 0 <= t < n:
                inside = False
            target.append(t)
        if inside:
            lin = lambda v: sum(x * math.prod(sizes[i + 1 :]) for i, x in enumerate(v))
            pairs.append((lin(source), lin(target)))
    return tuple(axes), pairs


def take(array, rel, dims, width):
    for axis, r in rel.items():
        if r:
            array = edge(array, dims[axis], r, width)
    return array


def permute(array, axes, pairs, pack):
    if not pack:
        return lax.ppermute(array, axes, pairs)
    size = array.size
    rows = -(-size // 1024) * 8
    flat = jnp.pad(array.reshape(-1), (0, rows * 128 - size)).reshape(rows, 128)
    got = lax.ppermute(flat, axes, pairs)
    return got.reshape(-1)[:size].reshape(array.shape)


def receive(array, rel, dims, width, pack=False):
    rel = {a: r for a, r in rel.items() if r}
    axes, pairs = pairs_for({a: -r for a, r in rel.items()})
    return permute(take(array, rel, dims, width), axes, pairs, pack)


def receive_pair(array, rel, axis, dims, width, pack=False):
    low = dict(rel, **{axis: -1})
    high = dict(rel, **{axis: 1})
    if lax.axis_size(axis) != 2 or WRAP[axis]:
        return receive(array, low, dims, width, pack), receive(array, high, dims, width, pack)
    me = lax.axis_index(axis)
    sent = jnp.where(me == 0, take(array, low, dims, width), take(array, high, dims, width))
    low_nz = {a: r for a, r in low.items() if r}
    axes, pairs = pairs_for({a: -r for a, r in low_nz.items()})
    _, back = pairs_for({a: -r for a, r in dict(low_nz, **{axis: 1}).items()})
    got = permute(sent, axes, pairs + back, pack)
    zero = jnp.zeros_like(got)
    return jnp.where(me == 1, got, zero), jnp.where(me == 0, got, zero)


def face_halos(fields, axis, dim, wrap):
    thin = jnp.concatenate(
        [jnp.concatenate([edge(f, dim, 1, 1), edge(f, dim, -1, 1)], axis=dim) for f in fields], axis=0
    )
    return receive_pair(thin, {}, axis, {axis: dim}, 1)


def padded_sweeps(joined, width):
    dims = {"span": 1, "normal": 2, "circ": 3}
    before_c = receive(joined, {"circ": -1}, dims, width, True)
    after_c = receive(joined, {"circ": 1}, dims, width, True)
    low_n, high_n = receive_pair(joined, {}, "normal", dims, width, True)
    low_lc, high_lc = receive_pair(joined, {"circ": -1}, "normal", dims, width, True)
    low_hc, high_hc = receive_pair(joined, {"circ": 1}, "normal", dims, width, True)
    top = jnp.concatenate([low_lc, low_n, low_hc], axis=3)
    middle = jnp.concatenate([before_c, joined, after_c], axis=3)
    bottom = jnp.concatenate([high_lc, high_n, high_hc], axis=3)
    plane = jnp.concatenate([top, middle, bottom], axis=2)
    before_s = receive(plane, {"span": -1}, dims, width, True)
    after_s = receive(plane, {"span": 1}, dims, width, True)
    return jnp.concatenate([before_s, plane, after_s], axis=1)


def jac_apply(jac, term):
    spread = (slice(None), slice(None)) + (None,) * (term.ndim - 1)
    return jnp.sum(jac[spread] * term[:, None], axis=0)


def flux_faces(psi, weights, halos, owner_jac, neighbor_jac):
    inner_terms = []
    for direction in range(3):
        dim = direction + 1
        length = psi.shape[dim]
        low = lax.slice_in_dim(psi, 0, length - 1, axis=dim)
        high = lax.slice_in_dim(psi, 1, length, axis=dim)
        w_low = lax.slice_in_dim(weights[direction], 0, length - 1, axis=direction)
        between = w_low[None] * (low - high)
        inner_terms.append((jac_apply(owner_jac[direction], between), jac_apply(neighbor_jac[direction], between)))
    inner_terms = lax.optimization_barrier(inner_terms)
    total = jnp.zeros_like(psi)
    for direction in range(3):
        dim = direction + 1
        length = psi.shape[dim]
        before, after = halos[direction]
        last = lax.slice_in_dim(psi, length - 1, length, axis=dim)
        first = lax.slice_in_dim(psi, 0, 1, axis=dim)
        w_last = lax.slice_in_dim(weights[direction], length - 1, length, axis=direction)
        up_edge = w_last[None] * (last - after[:5])
        down_edge = before[5 + direction][None] * (before[:5] - first)
        up_inner, down_inner = inner_terms[direction]
        up = jnp.concatenate([up_inner, jac_apply(owner_jac[direction], up_edge)], axis=dim)
        down = jnp.concatenate([jac_apply(neighbor_jac[direction], down_edge), down_inner], axis=dim)
        total = total + up
        total = total + down
    return total


def shifted(array, offsets):
    axes, pairs = pairs_for(offsets, ("normal",))
    return lax.ppermute(array, axes, pairs)


def reduce_panels(terms):
    below, own, above = (terms[:, i * PANEL_DEV : (i + 1) * PANEL_DEV] for i in range(3))
    if lax.axis_size("normal") != 2 or lax.axis_size("circ") > 4:
        own = lax.psum(own + shifted(above, {"span": 1}) + shifted(below, {"span": -1}), ("circ", "normal"))
        return own
    partner = {"normal": 1}
    total = own + shifted(above, {"span": 1}) + shifted(below, {"span": -1})
    total = total + shifted(own, partner)
    total = total + shifted(above, dict(partner, span=1)) + shifted(below, dict(partner, span=-1))
    summed = total
    for step in range(1, lax.axis_size("circ")):
        summed = summed + shifted(total, {"circ": step})
    return summed


def on_device(
    adjoint,
    objective_grad,
    face_weights,
    owner_jac,
    neighbor_jac,
    coupling,
    stiffness,
    wall_kernel,
    panel_owner,
):
    fields = (adjoint, face_weights)
    halos = [
        face_halos(fields, "span", 1, False),
        face_halos(fields, "normal", 2, False),
        face_halos(fields, "circ", 3, True),
    ]
    residual = flux_faces(adjoint, face_weights, halos, owner_jac, neighbor_jac) + adjoint - objective_grad
    forcing = jac_apply(coupling.T, residual)
    margin = SWEEPS - 1
    joined = jnp.concatenate([stiffness[None], forcing], axis=0)
    full_pad = padded_sweeps(joined, margin)
    mesh = run_sweeps(full_pad[0], full_pad[1:])
    wall_sens = jnp.sum(wall_kernel[None] * mesh, axis=2)
    span = lax.axis_index("span")
    first = (span - 1) * PANEL_DEV
    local = panel_owner - first
    onehot = (
        local[:, :, None] == jnp.arange(3 * PANEL_DEV, dtype=jnp.int32)[None, None, :]
    ).astype(jnp.float32)
    terms = jnp.einsum("mki,kip->mp", wall_sens, onehot, precision=lax.Precision.HIGHEST)
    panels = reduce_panels(terms)
    return (residual, mesh, panels)


def solution(mesh):
    placed = (
        P(None, "span", "normal", "circ"),
        P(None, "span", "normal", "circ"),
        P(None, "span", "normal", "circ"),
        P(),
        P(),
        P(),
        P("span", "normal", "circ"),
        P("span", "normal", "circ"),
        P("span", "circ"),
    )
    return jax.shard_map(
        on_device,
        mesh=mesh,
        in_specs=placed,
        out_specs=(
            P(None, "span", "normal", "circ"),
            P(None, "span", "normal", "circ"),
            P(None, "span"),
        ),
        check_vma=False,
    )
```

```python
import itertools
import math

import jax
import jax.numpy as jnp
from jax import lax
from jax.sharding import PartitionSpec as P

PANEL_DEV = 128
SWEEPS = 4


def padded_2(array, sides, width, wrap):
    for axis, dim in sides:
        peers, length = (lax.axis_size(axis), array.shape[dim])
        up = [(i, (i + 1) % peers) for i in range(peers if wrap else peers - 1)]
        down = [(j, i) for i, j in up]
        last = lax.slice_in_dim(array, length - width, length, axis=dim)
        initial = lax.slice_in_dim(array, 0, width, axis=dim)
        before = lax.ppermute(last, axis, up)
        after = lax.ppermute(initial, axis, down)
        array = jnp.concatenate([before, array, after], axis=dim)
    return array


def neighbor_sum(padded):
    total = padded[:, 2:, 1:-1, 1:-1] + padded[:, :-2, 1:-1, 1:-1]
    total = total + padded[:, 1:-1, 2:, 1:-1] + padded[:, 1:-1, :-2, 1:-1]
    return total + padded[:, 1:-1, 1:-1, 2:] + padded[:, 1:-1, 1:-1, :-2]


def inner(field):
    return field[:, 1:-1, 1:-1, 1:-1]


def flux_transpose(padded, owner_jac, neighbor_jac):
    psi = padded[:5]
    weights = padded[5:]
    center = inner(psi)
    total = jnp.zeros_like(center)
    for direction in range(3):
        lower = [slice(None), slice(1, -1), slice(1, -1), slice(1, -1)]
        upper = [slice(None), slice(1, -1), slice(1, -1), slice(1, -1)]
        lower[direction + 1] = slice(0, -2)
        upper[direction + 1] = slice(2, None)
        w_here = weights[direction, 1:-1, 1:-1, 1:-1]
        w_lower = weights[direction][tuple(lower[1:])]
        up_term = w_here[None] * (center - psi[tuple(upper)])
        down_term = w_lower[None] * (psi[tuple(lower)] - center)
        total = total + jnp.einsum(
            "uv,ukji->vkji", owner_jac[direction], up_term, precision=lax.Precision.HIGHEST
        )
        total = total + jnp.einsum(
            "uv,ukji->vkji", neighbor_jac[direction], down_term, precision=lax.Precision.HIGHEST
        )
    return total


def relax(mesh_pad, stiff_pad, force_pad):
    weighted = stiff_pad[None] * mesh_pad
    stiff_in = stiff_pad[1:-1, 1:-1, 1:-1]
    diag_term = 6.0 * stiff_in + 1.0
    mesh_in = inner(mesh_pad)
    return (
        mesh_in
        + 0.8
        * (inner(force_pad) - diag_term[None] * mesh_in + neighbor_sum(weighted))
        / diag_term[None]
    )


def run_sweeps(stiff_pad, force_pad):
    mesh_pad = 0.8 * force_pad / (6.0 * stiff_pad[None] + 1.0)
    for sweep in range(1, SWEEPS):
        mesh_pad = relax(mesh_pad, stiff_pad, force_pad)
        stiff_pad = stiff_pad[1:-1, 1:-1, 1:-1]
        force_pad = inner(force_pad)
    return mesh_pad


ORDER = ("circ", "normal", "span")
WRAP = {"circ": True, "normal": False, "span": False}


def edge(array, dim, side, width):
    length = array.shape[dim]
    start = length - width if side < 0 else 0
    return lax.slice_in_dim(array, start, start + width, axis=dim)


def pairs_for(offsets, wrap=()):
    axes = [a for a in ORDER if a in offsets]
    sizes = [lax.axis_size(a) for a in axes]
    pairs = []
    for source in itertools.product(*[range(n) for n in sizes]):
        target, inside = [], True
        for axis, q, n in zip(axes, source, sizes):
            t = q + offsets[axis]
            if WRAP[axis] or axis in wrap:
                t %= n
            elif not 0 <= t < n:
                inside = False
            target.append(t)
        if inside:
            lin = lambda v: sum(x * math.prod(sizes[i + 1 :]) for i, x in enumerate(v))
            pairs.append((lin(source), lin(target)))
    return tuple(axes), pairs


def take(array, rel, dims, width):
    for axis, r in rel.items():
        if r:
            array = edge(array, dims[axis], r, width)
    return array


def receive(array, rel, dims, width):
    rel = {a: r for a, r in rel.items() if r}
    axes, pairs = pairs_for({a: -r for a, r in rel.items()})
    return lax.ppermute(take(array, rel, dims, width), axes, pairs)


def receive_pair(array, rel, axis, dims, width):
    low = dict(rel, **{axis: -1})
    high = dict(rel, **{axis: 1})
    if lax.axis_size(axis) != 2 or WRAP[axis]:
        return receive(array, low, dims, width), receive(array, high, dims, width)
    me = lax.axis_index(axis)
    sent = jnp.where(me == 0, take(array, low, dims, width), take(array, high, dims, width))
    low_nz = {a: r for a, r in low.items() if r}
    axes, pairs = pairs_for({a: -r for a, r in low_nz.items()})
    _, back = pairs_for({a: -r for a, r in dict(low_nz, **{axis: 1}).items()})
    got = lax.ppermute(sent, axes, pairs + back)
    zero = jnp.zeros_like(got)
    return jnp.where(me == 1, got, zero), jnp.where(me == 0, got, zero)


def face_halos(fields, axis, dim, wrap):
    thin = jnp.concatenate(
        [jnp.concatenate([edge(f, dim, 1, 1), edge(f, dim, -1, 1)], axis=dim) for f in fields], axis=0
    )
    return receive_pair(thin, {}, axis, {axis: dim}, 1)


def padded_sweeps(joined, width):
    dims = {"span": 1, "normal": 2, "circ": 3}
    before_c = receive(joined, {"circ": -1}, dims, width)
    after_c = receive(joined, {"circ": 1}, dims, width)
    low_n, high_n = receive_pair(joined, {}, "normal", dims, width)
    low_lc, high_lc = receive_pair(joined, {"circ": -1}, "normal", dims, width)
    low_hc, high_hc = receive_pair(joined, {"circ": 1}, "normal", dims, width)
    top = jnp.concatenate([low_lc, low_n, low_hc], axis=3)
    middle = jnp.concatenate([before_c, joined, after_c], axis=3)
    bottom = jnp.concatenate([high_lc, high_n, high_hc], axis=3)
    plane = jnp.concatenate([top, middle, bottom], axis=2)
    before_s = receive(plane, {"span": -1}, dims, width)
    after_s = receive(plane, {"span": 1}, dims, width)
    return jnp.concatenate([before_s, plane, after_s], axis=1)


def jac_apply(jac, term):
    spread = (slice(None), slice(None)) + (None,) * (term.ndim - 1)
    return jnp.sum(jac[spread] * term[:, None], axis=0)


def flux_faces(psi, weights, halos, owner_jac, neighbor_jac, base, stiffness):
    inner_terms = []
    for direction in range(3):
        dim = direction + 1
        length = psi.shape[dim]
        low = lax.slice_in_dim(psi, 0, length - 1, axis=dim)
        high = lax.slice_in_dim(psi, 1, length, axis=dim)
        w_low = lax.slice_in_dim(weights[direction], 0, length - 1, axis=direction)
        between = w_low[None] * (low - high)
        inner_terms.append((jac_apply(owner_jac[direction], between), jac_apply(neighbor_jac[direction], between)))
    inner_terms, total, stiffness = lax.optimization_barrier((inner_terms, base, stiffness))
    for direction in range(3):
        dim = direction + 1
        length = psi.shape[dim]
        before, after = halos[direction]
        last = lax.slice_in_dim(psi, length - 1, length, axis=dim)
        first = lax.slice_in_dim(psi, 0, 1, axis=dim)
        w_last = lax.slice_in_dim(weights[direction], length - 1, length, axis=direction)
        up_edge = w_last[None] * (last - after[:5])
        down_edge = before[5 + direction][None] * (before[:5] - first)
        up_inner, down_inner = inner_terms[direction]
        up = jnp.concatenate([up_inner, jac_apply(owner_jac[direction], up_edge)], axis=dim)
        down = jnp.concatenate([jac_apply(neighbor_jac[direction], down_edge), down_inner], axis=dim)
        total = total + up
        total = total + down
    return total, stiffness


def shifted(array, offsets):
    axes, pairs = pairs_for(offsets, ("normal",))
    return lax.ppermute(array, axes, pairs)


def reduce_panels(terms):
    below, own, above = (terms[:, i * PANEL_DEV : (i + 1) * PANEL_DEV] for i in range(3))
    if lax.axis_size("normal") != 2 or lax.axis_size("circ") > 4:
        own = lax.psum(own + shifted(above, {"span": 1}) + shifted(below, {"span": -1}), ("circ", "normal"))
        return own
    partner = {"normal": 1}
    total = own + shifted(above, {"span": 1}) + shifted(below, {"span": -1})
    total = total + shifted(own, partner)
    total = total + shifted(above, dict(partner, span=1)) + shifted(below, dict(partner, span=-1))
    summed = total
    for step in range(1, lax.axis_size("circ")):
        summed = summed + shifted(total, {"circ": step})
    return summed


def on_device(
    adjoint,
    objective_grad,
    face_weights,
    owner_jac,
    neighbor_jac,
    coupling,
    stiffness,
    wall_kernel,
    panel_owner,
):
    fields = (adjoint, face_weights)
    halos = [
        face_halos(fields, "span", 1, False),
        face_halos(fields, "normal", 2, False),
        face_halos(fields, "circ", 3, True),
    ]
    residual, stiffness = flux_faces(
        adjoint, face_weights, halos, owner_jac, neighbor_jac, adjoint - objective_grad, stiffness
    )
    forcing = jac_apply(coupling.T, residual)
    margin = SWEEPS - 1
    joined = jnp.concatenate([stiffness[None], forcing], axis=0)
    full_pad = padded_sweeps(joined, margin)
    mesh = run_sweeps(full_pad[0], full_pad[1:])
    wall_sens = jnp.sum(wall_kernel[None] * mesh, axis=2)
    span = lax.axis_index("span")
    first = (span - 1) * PANEL_DEV
    local = panel_owner - first
    onehot = (
        local[:, :, None] == jnp.arange(3 * PANEL_DEV, dtype=jnp.int32)[None, None, :]
    ).astype(jnp.float32)
    terms = jnp.einsum("mki,kip->mp", wall_sens, onehot, precision=lax.Precision.HIGHEST)
    panels = reduce_panels(terms)
    return (residual, mesh, panels)


def solution(mesh):
    placed = (
        P(None, "span", "normal", "circ"),
        P(None, "span", "normal", "circ"),
        P(None, "span", "normal", "circ"),
        P(),
        P(),
        P(),
        P("span", "normal", "circ"),
        P("span", "normal", "circ"),
        P("span", "circ"),
    )
    return jax.shard_map(
        on_device,
        mesh=mesh,
        in_specs=placed,
        out_specs=(
            P(None, "span", "normal", "circ"),
            P(None, "span", "normal", "circ"),
            P(None, "span"),
        ),
        check_vma=False,
    )
```

```python
import itertools
import math

import jax
import jax.numpy as jnp
from jax import lax
from jax.sharding import PartitionSpec as P

PANEL_DEV = 128
SWEEPS = 4


def padded_2(array, sides, width, wrap):
    for axis, dim in sides:
        peers, length = (lax.axis_size(axis), array.shape[dim])
        up = [(i, (i + 1) % peers) for i in range(peers if wrap else peers - 1)]
        down = [(j, i) for i, j in up]
        last = lax.slice_in_dim(array, length - width, length, axis=dim)
        initial = lax.slice_in_dim(array, 0, width, axis=dim)
        before = lax.ppermute(last, axis, up)
        after = lax.ppermute(initial, axis, down)
        array = jnp.concatenate([before, array, after], axis=dim)
    return array


def neighbor_sum(padded):
    total = padded[:, 2:, 1:-1, 1:-1] + padded[:, :-2, 1:-1, 1:-1]
    total = total + padded[:, 1:-1, 2:, 1:-1] + padded[:, 1:-1, :-2, 1:-1]
    return total + padded[:, 1:-1, 1:-1, 2:] + padded[:, 1:-1, 1:-1, :-2]


def inner(field):
    return field[:, 1:-1, 1:-1, 1:-1]


def flux_transpose(padded, owner_jac, neighbor_jac):
    psi = padded[:5]
    weights = padded[5:]
    center = inner(psi)
    total = jnp.zeros_like(center)
    for direction in range(3):
        lower = [slice(None), slice(1, -1), slice(1, -1), slice(1, -1)]
        upper = [slice(None), slice(1, -1), slice(1, -1), slice(1, -1)]
        lower[direction + 1] = slice(0, -2)
        upper[direction + 1] = slice(2, None)
        w_here = weights[direction, 1:-1, 1:-1, 1:-1]
        w_lower = weights[direction][tuple(lower[1:])]
        up_term = w_here[None] * (center - psi[tuple(upper)])
        down_term = w_lower[None] * (psi[tuple(lower)] - center)
        total = total + jnp.einsum(
            "uv,ukji->vkji", owner_jac[direction], up_term, precision=lax.Precision.HIGHEST
        )
        total = total + jnp.einsum(
            "uv,ukji->vkji", neighbor_jac[direction], down_term, precision=lax.Precision.HIGHEST
        )
    return total


def relax(mesh_pad, stiff_pad, force_pad):
    weighted = stiff_pad[None] * mesh_pad
    stiff_in = stiff_pad[1:-1, 1:-1, 1:-1]
    diag_term = 6.0 * stiff_in + 1.0
    mesh_in = inner(mesh_pad)
    return (
        mesh_in
        + 0.8
        * (inner(force_pad) - diag_term[None] * mesh_in + neighbor_sum(weighted))
        / diag_term[None]
    )


def run_sweeps(stiff_pad, force_pad):
    mesh_pad = 0.8 * force_pad / (6.0 * stiff_pad[None] + 1.0)
    for sweep in range(1, SWEEPS):
        mesh_pad = relax(mesh_pad, stiff_pad, force_pad)
        stiff_pad = stiff_pad[1:-1, 1:-1, 1:-1]
        force_pad = inner(force_pad)
    return mesh_pad


ORDER = ("circ", "normal", "span")
WRAP = {"circ": True, "normal": False, "span": False}


def edge(array, dim, side, width):
    length = array.shape[dim]
    start = length - width if side < 0 else 0
    return lax.slice_in_dim(array, start, start + width, axis=dim)


def pairs_for(offsets, wrap=()):
    axes = [a for a in ORDER if a in offsets]
    sizes = [lax.axis_size(a) for a in axes]
    pairs = []
    for source in itertools.product(*[range(n) for n in sizes]):
        target, inside = [], True
        for axis, q, n in zip(axes, source, sizes):
            t = q + offsets[axis]
            if WRAP[axis] or axis in wrap:
                t %= n
            elif not 0 <= t < n:
                inside = False
            target.append(t)
        if inside:
            lin = lambda v: sum(x * math.prod(sizes[i + 1 :]) for i, x in enumerate(v))
            pairs.append((lin(source), lin(target)))
    return tuple(axes), pairs


def take(array, rel, dims, width):
    for axis, r in rel.items():
        if r:
            array = edge(array, dims[axis], r, width)
    return array


def receive(array, rel, dims, width):
    rel = {a: r for a, r in rel.items() if r}
    axes, pairs = pairs_for({a: -r for a, r in rel.items()})
    return lax.ppermute(take(array, rel, dims, width), axes, pairs)


def receive_pair(array, rel, axis, dims, width):
    low = dict(rel, **{axis: -1})
    high = dict(rel, **{axis: 1})
    if lax.axis_size(axis) != 2 or WRAP[axis]:
        return receive(array, low, dims, width), receive(array, high, dims, width)
    me = lax.axis_index(axis)
    sent = jnp.where(me == 0, take(array, low, dims, width), take(array, high, dims, width))
    low_nz = {a: r for a, r in low.items() if r}
    axes, pairs = pairs_for({a: -r for a, r in low_nz.items()})
    _, back = pairs_for({a: -r for a, r in dict(low_nz, **{axis: 1}).items()})
    got = lax.ppermute(sent, axes, pairs + back)
    zero = jnp.zeros_like(got)
    return jnp.where(me == 1, got, zero), jnp.where(me == 0, got, zero)


def face_halos(fields, axis, dim, wrap):
    thin = jnp.concatenate(
        [jnp.concatenate([edge(f, dim, 1, 1), edge(f, dim, -1, 1)], axis=dim) for f in fields], axis=0
    )
    return receive_pair(thin, {}, axis, {axis: dim}, 1)


def padded_sweeps(joined, width):
    dims = {"span": 1, "normal": 2, "circ": 3}
    before_c = receive(joined, {"circ": -1}, dims, width)
    after_c = receive(joined, {"circ": 1}, dims, width)
    low_n, high_n = receive_pair(joined, {}, "normal", dims, width)
    low_lc, high_lc = receive_pair(joined, {"circ": -1}, "normal", dims, width)
    low_hc, high_hc = receive_pair(joined, {"circ": 1}, "normal", dims, width)
    top = jnp.concatenate([low_lc, low_n, low_hc], axis=3)
    middle = jnp.concatenate([before_c, joined, after_c], axis=3)
    bottom = jnp.concatenate([high_lc, high_n, high_hc], axis=3)
    plane = jnp.concatenate([top, middle, bottom], axis=2)
    before_s = receive(plane, {"span": -1}, dims, width)
    after_s = receive(plane, {"span": 1}, dims, width)
    return jnp.concatenate([before_s, plane, after_s], axis=1)


def jac_apply(jac, term):
    spread = (slice(None), slice(None)) + (None,) * (term.ndim - 1)
    return jnp.sum(jac[spread] * term[:, None], axis=0)


def flux_faces(psi, weights, halos, owner_jac, neighbor_jac):
    inner_terms = []
    for direction in range(3):
        dim = direction + 1
        length = psi.shape[dim]
        low = lax.slice_in_dim(psi, 0, length - 1, axis=dim)
        high = lax.slice_in_dim(psi, 1, length, axis=dim)
        w_low = lax.slice_in_dim(weights[direction], 0, length - 1, axis=direction)
        between = w_low[None] * (low - high)
        inner_terms.append((jac_apply(owner_jac[direction], between), jac_apply(neighbor_jac[direction], between)))
    inner_terms = lax.optimization_barrier(inner_terms)
    total = jnp.zeros_like(psi)
    for direction in range(3):
        dim = direction + 1
        length = psi.shape[dim]
        before, after = halos[direction]
        last = lax.slice_in_dim(psi, length - 1, length, axis=dim)
        first = lax.slice_in_dim(psi, 0, 1, axis=dim)
        w_last = lax.slice_in_dim(weights[direction], length - 1, length, axis=direction)
        up_edge = w_last[None] * (last - after[:5])
        down_edge = before[5 + direction][None] * (before[:5] - first)
        up_inner, down_inner = inner_terms[direction]
        up = jnp.concatenate([up_inner, jac_apply(owner_jac[direction], up_edge)], axis=dim)
        down = jnp.concatenate([jac_apply(neighbor_jac[direction], down_edge), down_inner], axis=dim)
        total = total + up
        total = total + down
    return total


def shifted(array, offsets):
    axes, pairs = pairs_for(offsets, ("normal",))
    return lax.ppermute(array, axes, pairs)


def reduce_panels(terms):
    below, own, above = (terms[:, i * PANEL_DEV : (i + 1) * PANEL_DEV] for i in range(3))
    devices = math.prod(lax.axis_size(a) for a in ORDER)
    if devices <= 64:
        spans = lax.axis_size("span")
        relative = jnp.arange(devices, dtype=jnp.int32) % spans - lax.axis_index("span") + 1
        chunks = jnp.zeros((devices,) + own.shape, own.dtype)
        for index, block in enumerate((below, own, above)):
            chunks = jnp.where((relative == index)[:, None, None], block[None], chunks)
        return jnp.sum(lax.all_to_all(chunks, ORDER, 0, 0, tiled=False), axis=0)
    if lax.axis_size("normal") != 2 or lax.axis_size("circ") > 4:
        own = lax.psum(own + shifted(above, {"span": 1}) + shifted(below, {"span": -1}), ("circ", "normal"))
        return own
    partner = {"normal": 1}
    total = own + shifted(above, {"span": 1}) + shifted(below, {"span": -1})
    total = total + shifted(own, partner)
    total = total + shifted(above, dict(partner, span=1)) + shifted(below, dict(partner, span=-1))
    summed = total
    for step in range(1, lax.axis_size("circ")):
        summed = summed + shifted(total, {"circ": step})
    return summed


def on_device(
    adjoint,
    objective_grad,
    face_weights,
    owner_jac,
    neighbor_jac,
    coupling,
    stiffness,
    wall_kernel,
    panel_owner,
):
    fields = (adjoint, face_weights)
    halos = [
        face_halos(fields, "span", 1, False),
        face_halos(fields, "normal", 2, False),
        face_halos(fields, "circ", 3, True),
    ]
    residual = flux_faces(adjoint, face_weights, halos, owner_jac, neighbor_jac) + adjoint - objective_grad
    forcing = jac_apply(coupling.T, residual)
    margin = SWEEPS - 1
    joined = jnp.concatenate([stiffness[None], forcing], axis=0)
    full_pad = padded_sweeps(joined, margin)
    mesh = run_sweeps(full_pad[0], full_pad[1:])
    wall_sens = jnp.sum(wall_kernel[None] * mesh, axis=2)
    span = lax.axis_index("span")
    first = (span - 1) * PANEL_DEV
    local = panel_owner - first
    onehot = (
        local[:, :, None] == jnp.arange(3 * PANEL_DEV, dtype=jnp.int32)[None, None, :]
    ).astype(jnp.float32)
    terms = jnp.einsum("mki,kip->mp", wall_sens, onehot, precision=lax.Precision.HIGHEST)
    panels = reduce_panels(terms)
    return (residual, mesh, panels)


def solution(mesh):
    placed = (
        P(None, "span", "normal", "circ"),
        P(None, "span", "normal", "circ"),
        P(None, "span", "normal", "circ"),
        P(),
        P(),
        P(),
        P("span", "normal", "circ"),
        P("span", "normal", "circ"),
        P("span", "circ"),
    )
    return jax.shard_map(
        on_device,
        mesh=mesh,
        in_specs=placed,
        out_specs=(
            P(None, "span", "normal", "circ"),
            P(None, "span", "normal", "circ"),
            P(None, "span"),
        ),
        check_vma=False,
    )
```

```python
import itertools
import math

import jax
import jax.numpy as jnp
from jax import lax
from jax.sharding import PartitionSpec as P

PANEL_DEV = 128
SWEEPS = 4


def padded_2(array, sides, width, wrap):
    for axis, dim in sides:
        peers, length = (lax.axis_size(axis), array.shape[dim])
        up = [(i, (i + 1) % peers) for i in range(peers if wrap else peers - 1)]
        down = [(j, i) for i, j in up]
        last = lax.slice_in_dim(array, length - width, length, axis=dim)
        initial = lax.slice_in_dim(array, 0, width, axis=dim)
        before = lax.ppermute(last, axis, up)
        after = lax.ppermute(initial, axis, down)
        array = jnp.concatenate([before, array, after], axis=dim)
    return array


def neighbor_sum(padded):
    total = padded[:, 2:, 1:-1, 1:-1] + padded[:, :-2, 1:-1, 1:-1]
    total = total + padded[:, 1:-1, 2:, 1:-1] + padded[:, 1:-1, :-2, 1:-1]
    return total + padded[:, 1:-1, 1:-1, 2:] + padded[:, 1:-1, 1:-1, :-2]


def inner(field):
    return field[:, 1:-1, 1:-1, 1:-1]


def flux_transpose(padded, owner_jac, neighbor_jac):
    psi = padded[:5]
    weights = padded[5:]
    center = inner(psi)
    total = jnp.zeros_like(center)
    for direction in range(3):
        lower = [slice(None), slice(1, -1), slice(1, -1), slice(1, -1)]
        upper = [slice(None), slice(1, -1), slice(1, -1), slice(1, -1)]
        lower[direction + 1] = slice(0, -2)
        upper[direction + 1] = slice(2, None)
        w_here = weights[direction, 1:-1, 1:-1, 1:-1]
        w_lower = weights[direction][tuple(lower[1:])]
        up_term = w_here[None] * (center - psi[tuple(upper)])
        down_term = w_lower[None] * (psi[tuple(lower)] - center)
        total = total + jnp.einsum(
            "uv,ukji->vkji", owner_jac[direction], up_term, precision=lax.Precision.HIGHEST
        )
        total = total + jnp.einsum(
            "uv,ukji->vkji", neighbor_jac[direction], down_term, precision=lax.Precision.HIGHEST
        )
    return total


def relax(mesh_pad, stiff_pad, force_pad):
    weighted = stiff_pad[None] * mesh_pad
    stiff_in = stiff_pad[1:-1, 1:-1, 1:-1]
    diag_term = 6.0 * stiff_in + 1.0
    mesh_in = inner(mesh_pad)
    return (
        mesh_in
        + 0.8
        * (inner(force_pad) - diag_term[None] * mesh_in + neighbor_sum(weighted))
        / diag_term[None]
    )


def run_sweeps(stiff_pad, force_pad):
    mesh_pad = 0.8 * force_pad / (6.0 * stiff_pad[None] + 1.0)
    for sweep in range(1, SWEEPS):
        mesh_pad = relax(mesh_pad, stiff_pad, force_pad)
        stiff_pad = stiff_pad[1:-1, 1:-1, 1:-1]
        force_pad = inner(force_pad)
    return mesh_pad


ORDER = ("circ", "normal", "span")
WRAP = {"circ": True, "normal": False, "span": False}


def edge(array, dim, side, width):
    length = array.shape[dim]
    start = length - width if side < 0 else 0
    return lax.slice_in_dim(array, start, start + width, axis=dim)


def pairs_for(offsets, wrap=()):
    axes = [a for a in ORDER if a in offsets]
    sizes = [lax.axis_size(a) for a in axes]
    pairs = []
    for source in itertools.product(*[range(n) for n in sizes]):
        target, inside = [], True
        for axis, q, n in zip(axes, source, sizes):
            t = q + offsets[axis]
            if WRAP[axis] or axis in wrap:
                t %= n
            elif not 0 <= t < n:
                inside = False
            target.append(t)
        if inside:
            lin = lambda v: sum(x * math.prod(sizes[i + 1 :]) for i, x in enumerate(v))
            pairs.append((lin(source), lin(target)))
    return tuple(axes), pairs


def take(array, rel, dims, width):
    for axis, r in rel.items():
        if r:
            array = edge(array, dims[axis], r, width)
    return array


def receive(array, rel, dims, width):
    rel = {a: r for a, r in rel.items() if r}
    axes, pairs = pairs_for({a: -r for a, r in rel.items()})
    return lax.ppermute(take(array, rel, dims, width), axes, pairs)


def receive_pair(array, rel, axis, dims, width):
    low = dict(rel, **{axis: -1})
    high = dict(rel, **{axis: 1})
    if lax.axis_size(axis) != 2 or WRAP[axis]:
        return receive(array, low, dims, width), receive(array, high, dims, width)
    me = lax.axis_index(axis)
    sent = jnp.where(me == 0, take(array, low, dims, width), take(array, high, dims, width))
    low_nz = {a: r for a, r in low.items() if r}
    axes, pairs = pairs_for({a: -r for a, r in low_nz.items()})
    _, back = pairs_for({a: -r for a, r in dict(low_nz, **{axis: 1}).items()})
    got = lax.ppermute(sent, axes, pairs + back)
    zero = jnp.zeros_like(got)
    return jnp.where(me == 1, got, zero), jnp.where(me == 0, got, zero)


def face_halos(fields, axis, dim, wrap):
    thin = jnp.concatenate(
        [jnp.concatenate([edge(f, dim, 1, 1), edge(f, dim, -1, 1)], axis=dim) for f in fields], axis=0
    )
    return receive_pair(thin, {}, axis, {axis: dim}, 1)


def padded_sweeps(joined, width):
    dims = {"span": 1, "normal": 2, "circ": 3}
    before_c = receive(joined, {"circ": -1}, dims, width)
    after_c = receive(joined, {"circ": 1}, dims, width)
    low_n, high_n = receive_pair(joined, {}, "normal", dims, width)
    low_lc, high_lc = receive_pair(joined, {"circ": -1}, "normal", dims, width)
    low_hc, high_hc = receive_pair(joined, {"circ": 1}, "normal", dims, width)
    top = jnp.concatenate([low_lc, low_n, low_hc], axis=3)
    middle = jnp.concatenate([before_c, joined, after_c], axis=3)
    bottom = jnp.concatenate([high_lc, high_n, high_hc], axis=3)
    plane = jnp.concatenate([top, middle, bottom], axis=2)
    before_s = receive(plane, {"span": -1}, dims, width)
    after_s = receive(plane, {"span": 1}, dims, width)
    return jnp.concatenate([before_s, plane, after_s], axis=1)


def padded_sweeps_a2a(joined, width):
    dims = {"span": 1, "normal": 2, "circ": 3}
    ring = lax.axis_size("circ")
    c, n = lax.axis_index("circ"), lax.axis_index("normal")
    rows = {side: take(joined, {"normal": side}, dims, width) for side in (-1, 1)}
    facing = jnp.where(n == 0, rows[-1], rows[1])
    pieces = {
        (1, 0): take(joined, {"circ": -1}, dims, width),
        (ring - 1, 0): take(joined, {"circ": 1}, dims, width),
        (0, 1): facing,
        (1, 1): take(facing, {"circ": -1}, dims, width),
        (ring - 1, 1): take(facing, {"circ": 1}, dims, width),
    }
    size = max(p.size for p in pieces.values())
    table = jnp.zeros((ring, 2, size), joined.dtype)
    for (dc, dn), piece in pieces.items():
        flat = jnp.pad(piece.reshape(-1), (0, size - piece.size))
        table = table.at[dc, dn].set(flat)
    table = jnp.roll(jnp.roll(table, c, axis=0), n, axis=1).reshape(ring * 2, size)
    got = lax.all_to_all(table, ("circ", "normal"), 0, 0, tiled=False).reshape(ring, 2, size)
    got = jnp.roll(jnp.roll(got, -c, axis=0), -n, axis=1)

    def unpack(dc, dn, like):
        return got[dc, dn, : like.size].reshape(like.shape)

    before_c = unpack(ring - 1, 0, pieces[(1, 0)])
    after_c = unpack(1, 0, pieces[(ring - 1, 0)])
    zero_rows = jnp.zeros_like(facing)
    partner = unpack(0, 1, facing)
    low_n, high_n = jnp.where(n == 1, partner, zero_rows), jnp.where(n == 0, partner, zero_rows)
    corner = pieces[(1, 1)]
    zero_corner = jnp.zeros_like(corner)
    from_lc = unpack(ring - 1, 1, corner)
    from_hc = unpack(1, 1, corner)
    low_lc, high_lc = jnp.where(n == 1, from_lc, zero_corner), jnp.where(n == 0, from_lc, zero_corner)
    low_hc, high_hc = jnp.where(n == 1, from_hc, zero_corner), jnp.where(n == 0, from_hc, zero_corner)
    top = jnp.concatenate([low_lc, low_n, low_hc], axis=3)
    middle = jnp.concatenate([before_c, joined, after_c], axis=3)
    bottom = jnp.concatenate([high_lc, high_n, high_hc], axis=3)
    plane = jnp.concatenate([top, middle, bottom], axis=2)
    before_s = receive(plane, {"span": -1}, dims, width)
    after_s = receive(plane, {"span": 1}, dims, width)
    return jnp.concatenate([before_s, plane, after_s], axis=1)


def jac_apply(jac, term):
    spread = (slice(None), slice(None)) + (None,) * (term.ndim - 1)
    return jnp.sum(jac[spread] * term[:, None], axis=0)


def flux_faces(psi, weights, halos, owner_jac, neighbor_jac):
    inner_terms = []
    for direction in range(3):
        dim = direction + 1
        length = psi.shape[dim]
        low = lax.slice_in_dim(psi, 0, length - 1, axis=dim)
        high = lax.slice_in_dim(psi, 1, length, axis=dim)
        w_low = lax.slice_in_dim(weights[direction], 0, length - 1, axis=direction)
        between = w_low[None] * (low - high)
        inner_terms.append((jac_apply(owner_jac[direction], between), jac_apply(neighbor_jac[direction], between)))
    inner_terms = lax.optimization_barrier(inner_terms)
    total = jnp.zeros_like(psi)
    for direction in range(3):
        dim = direction + 1
        length = psi.shape[dim]
        before, after = halos[direction]
        last = lax.slice_in_dim(psi, length - 1, length, axis=dim)
        first = lax.slice_in_dim(psi, 0, 1, axis=dim)
        w_last = lax.slice_in_dim(weights[direction], length - 1, length, axis=direction)
        up_edge = w_last[None] * (last - after[:5])
        down_edge = before[5 + direction][None] * (before[:5] - first)
        up_inner, down_inner = inner_terms[direction]
        up = jnp.concatenate([up_inner, jac_apply(owner_jac[direction], up_edge)], axis=dim)
        down = jnp.concatenate([jac_apply(neighbor_jac[direction], down_edge), down_inner], axis=dim)
        total = total + up
        total = total + down
    return total


def shifted(array, offsets):
    axes, pairs = pairs_for(offsets, ("normal",))
    return lax.ppermute(array, axes, pairs)


def reduce_panels(terms):
    below, own, above = (terms[:, i * PANEL_DEV : (i + 1) * PANEL_DEV] for i in range(3))
    devices = math.prod(lax.axis_size(a) for a in ORDER)
    if devices <= 64:
        spans = lax.axis_size("span")
        relative = jnp.arange(devices, dtype=jnp.int32) % spans - lax.axis_index("span") + 1
        chunks = jnp.zeros((devices,) + own.shape, own.dtype)
        for index, block in enumerate((below, own, above)):
            chunks = jnp.where((relative == index)[:, None, None], block[None], chunks)
        return jnp.sum(lax.all_to_all(chunks, ORDER, 0, 0, tiled=False), axis=0)
    if lax.axis_size("normal") != 2 or lax.axis_size("circ") > 4:
        own = lax.psum(own + shifted(above, {"span": 1}) + shifted(below, {"span": -1}), ("circ", "normal"))
        return own
    partner = {"normal": 1}
    total = own + shifted(above, {"span": 1}) + shifted(below, {"span": -1})
    total = total + shifted(own, partner)
    total = total + shifted(above, dict(partner, span=1)) + shifted(below, dict(partner, span=-1))
    summed = total
    for step in range(1, lax.axis_size("circ")):
        summed = summed + shifted(total, {"circ": step})
    return summed


def on_device(
    adjoint,
    objective_grad,
    face_weights,
    owner_jac,
    neighbor_jac,
    coupling,
    stiffness,
    wall_kernel,
    panel_owner,
):
    fields = (adjoint, face_weights)
    halos = [
        face_halos(fields, "span", 1, False),
        face_halos(fields, "normal", 2, False),
        face_halos(fields, "circ", 3, True),
    ]
    residual = flux_faces(adjoint, face_weights, halos, owner_jac, neighbor_jac) + adjoint - objective_grad
    forcing = jac_apply(coupling.T, residual)
    margin = SWEEPS - 1
    joined = jnp.concatenate([stiffness[None], forcing], axis=0)
    if lax.axis_size("normal") == 2 and 3 <= lax.axis_size("circ") <= 4:
        full_pad = padded_sweeps_a2a(joined, margin)
    else:
        full_pad = padded_sweeps(joined, margin)
    mesh = run_sweeps(full_pad[0], full_pad[1:])
    wall_sens = jnp.sum(wall_kernel[None] * mesh, axis=2)
    span = lax.axis_index("span")
    first = (span - 1) * PANEL_DEV
    local = panel_owner - first
    onehot = (
        local[:, :, None] == jnp.arange(3 * PANEL_DEV, dtype=jnp.int32)[None, None, :]
    ).astype(jnp.float32)
    terms = jnp.einsum("mki,kip->mp", wall_sens, onehot, precision=lax.Precision.HIGHEST)
    panels = reduce_panels(terms)
    return (residual, mesh, panels)


def solution(mesh):
    placed = (
        P(None, "span", "normal", "circ"),
        P(None, "span", "normal", "circ"),
        P(None, "span", "normal", "circ"),
        P(),
        P(),
        P(),
        P("span", "normal", "circ"),
        P("span", "normal", "circ"),
        P("span", "circ"),
    )
    return jax.shard_map(
        on_device,
        mesh=mesh,
        in_specs=placed,
        out_specs=(
            P(None, "span", "normal", "circ"),
            P(None, "span", "normal", "circ"),
            P(None, "span"),
        ),
        check_vma=False,
    )
```

```python
import itertools
import math

import jax
import jax.numpy as jnp
from jax import lax
from jax.sharding import PartitionSpec as P

PANEL_DEV = 128
SWEEPS = 4


def padded_2(array, sides, width, wrap):
    for axis, dim in sides:
        peers, length = (lax.axis_size(axis), array.shape[dim])
        up = [(i, (i + 1) % peers) for i in range(peers if wrap else peers - 1)]
        down = [(j, i) for i, j in up]
        last = lax.slice_in_dim(array, length - width, length, axis=dim)
        initial = lax.slice_in_dim(array, 0, width, axis=dim)
        before = lax.ppermute(last, axis, up)
        after = lax.ppermute(initial, axis, down)
        array = jnp.concatenate([before, array, after], axis=dim)
    return array


def neighbor_sum(padded):
    total = padded[:, 2:, 1:-1, 1:-1] + padded[:, :-2, 1:-1, 1:-1]
    total = total + padded[:, 1:-1, 2:, 1:-1] + padded[:, 1:-1, :-2, 1:-1]
    return total + padded[:, 1:-1, 1:-1, 2:] + padded[:, 1:-1, 1:-1, :-2]


def inner(field):
    return field[:, 1:-1, 1:-1, 1:-1]


def flux_transpose(padded, owner_jac, neighbor_jac):
    psi = padded[:5]
    weights = padded[5:]
    center = inner(psi)
    total = jnp.zeros_like(center)
    for direction in range(3):
        lower = [slice(None), slice(1, -1), slice(1, -1), slice(1, -1)]
        upper = [slice(None), slice(1, -1), slice(1, -1), slice(1, -1)]
        lower[direction + 1] = slice(0, -2)
        upper[direction + 1] = slice(2, None)
        w_here = weights[direction, 1:-1, 1:-1, 1:-1]
        w_lower = weights[direction][tuple(lower[1:])]
        up_term = w_here[None] * (center - psi[tuple(upper)])
        down_term = w_lower[None] * (psi[tuple(lower)] - center)
        total = total + jnp.einsum(
            "uv,ukji->vkji", owner_jac[direction], up_term, precision=lax.Precision.HIGHEST
        )
        total = total + jnp.einsum(
            "uv,ukji->vkji", neighbor_jac[direction], down_term, precision=lax.Precision.HIGHEST
        )
    return total


def relax(mesh_pad, stiff_pad, force_pad):
    weighted = stiff_pad[None] * mesh_pad
    stiff_in = stiff_pad[1:-1, 1:-1, 1:-1]
    diag_term = 6.0 * stiff_in + 1.0
    mesh_in = inner(mesh_pad)
    return (
        mesh_in
        + 0.8
        * (inner(force_pad) - diag_term[None] * mesh_in + neighbor_sum(weighted))
        / diag_term[None]
    )


def run_sweeps(stiff_pad, force_pad):
    mesh_pad = 0.8 * force_pad / (6.0 * stiff_pad[None] + 1.0)
    for sweep in range(1, SWEEPS):
        mesh_pad = relax(mesh_pad, stiff_pad, force_pad)
        stiff_pad = stiff_pad[1:-1, 1:-1, 1:-1]
        force_pad = inner(force_pad)
    return mesh_pad


ORDER = ("circ", "normal", "span")
WRAP = {"circ": True, "normal": False, "span": False}


def edge(array, dim, side, width):
    length = array.shape[dim]
    start = length - width if side < 0 else 0
    return lax.slice_in_dim(array, start, start + width, axis=dim)


def pairs_for(offsets, wrap=()):
    axes = [a for a in ORDER if a in offsets]
    sizes = [lax.axis_size(a) for a in axes]
    pairs = []
    for source in itertools.product(*[range(n) for n in sizes]):
        target, inside = [], True
        for axis, q, n in zip(axes, source, sizes):
            t = q + offsets[axis]
            if WRAP[axis] or axis in wrap:
                t %= n
            elif not 0 <= t < n:
                inside = False
            target.append(t)
        if inside:
            lin = lambda v: sum(x * math.prod(sizes[i + 1 :]) for i, x in enumerate(v))
            pairs.append((lin(source), lin(target)))
    return tuple(axes), pairs


def take(array, rel, dims, width):
    for axis, r in rel.items():
        if r:
            array = edge(array, dims[axis], r, width)
    return array


def receive(array, rel, dims, width):
    rel = {a: r for a, r in rel.items() if r}
    axes, pairs = pairs_for({a: -r for a, r in rel.items()})
    return lax.ppermute(take(array, rel, dims, width), axes, pairs)


def receive_pair(array, rel, axis, dims, width):
    low = dict(rel, **{axis: -1})
    high = dict(rel, **{axis: 1})
    if lax.axis_size(axis) != 2 or WRAP[axis]:
        return receive(array, low, dims, width), receive(array, high, dims, width)
    me = lax.axis_index(axis)
    sent = jnp.where(me == 0, take(array, low, dims, width), take(array, high, dims, width))
    low_nz = {a: r for a, r in low.items() if r}
    axes, pairs = pairs_for({a: -r for a, r in low_nz.items()})
    _, back = pairs_for({a: -r for a, r in dict(low_nz, **{axis: 1}).items()})
    got = lax.ppermute(sent, axes, pairs + back)
    zero = jnp.zeros_like(got)
    return jnp.where(me == 1, got, zero), jnp.where(me == 0, got, zero)


def face_halos(fields, axis, dim, wrap):
    thin = jnp.concatenate(
        [jnp.concatenate([edge(f, dim, 1, 1), edge(f, dim, -1, 1)], axis=dim) for f in fields], axis=0
    )
    return receive_pair(thin, {}, axis, {axis: dim}, 1)


def padded_sweeps(joined, width):
    dims = {"span": 1, "normal": 2, "circ": 3}
    before_c = receive(joined, {"circ": -1}, dims, width)
    after_c = receive(joined, {"circ": 1}, dims, width)
    low_n, high_n = receive_pair(joined, {}, "normal", dims, width)
    low_lc, high_lc = receive_pair(joined, {"circ": -1}, "normal", dims, width)
    low_hc, high_hc = receive_pair(joined, {"circ": 1}, "normal", dims, width)
    top = jnp.concatenate([low_lc, low_n, low_hc], axis=3)
    middle = jnp.concatenate([before_c, joined, after_c], axis=3)
    bottom = jnp.concatenate([high_lc, high_n, high_hc], axis=3)
    plane = jnp.concatenate([top, middle, bottom], axis=2)
    before_s = receive(plane, {"span": -1}, dims, width)
    after_s = receive(plane, {"span": 1}, dims, width)
    return jnp.concatenate([before_s, plane, after_s], axis=1)


def jac_apply(jac, term):
    spread = (slice(None), slice(None)) + (None,) * (term.ndim - 1)
    return jnp.sum(jac[spread] * term[:, None], axis=0)


def flux_faces(psi, weights, halos, owner_jac, neighbor_jac):
    inner_terms = []
    for direction in range(3):
        dim = direction + 1
        length = psi.shape[dim]
        low = lax.slice_in_dim(psi, 0, length - 1, axis=dim)
        high = lax.slice_in_dim(psi, 1, length, axis=dim)
        w_low = lax.slice_in_dim(weights[direction], 0, length - 1, axis=direction)
        between = w_low[None] * (low - high)
        inner_terms.append((jac_apply(owner_jac[direction], between), jac_apply(neighbor_jac[direction], between)))
    inner_terms = lax.optimization_barrier(inner_terms)
    total = jnp.zeros_like(psi)
    for direction in range(3):
        dim = direction + 1
        length = psi.shape[dim]
        before, after = halos[direction]
        last = lax.slice_in_dim(psi, length - 1, length, axis=dim)
        first = lax.slice_in_dim(psi, 0, 1, axis=dim)
        w_last = lax.slice_in_dim(weights[direction], length - 1, length, axis=direction)
        up_edge = w_last[None] * (last - after[:5])
        down_edge = before[5 + direction][None] * (before[:5] - first)
        up_inner, down_inner = inner_terms[direction]
        up = jnp.concatenate([up_inner, jac_apply(owner_jac[direction], up_edge)], axis=dim)
        down = jnp.concatenate([jac_apply(neighbor_jac[direction], down_edge), down_inner], axis=dim)
        total = total + up
        total = total + down
    return total


def shifted(array, offsets):
    axes, pairs = pairs_for(offsets, ("normal",))
    return lax.ppermute(array, axes, pairs)


def reduce_panels(terms):
    below, own, above = (terms[:, i * PANEL_DEV : (i + 1) * PANEL_DEV] for i in range(3))
    devices = math.prod(lax.axis_size(a) for a in ORDER)
    if devices <= 64:
        spans = lax.axis_size("span")
        relative = jnp.arange(devices, dtype=jnp.int32) % spans - lax.axis_index("span") + 1
        chunks = jnp.zeros((devices,) + own.shape, own.dtype)
        for index, block in enumerate((below, own, above)):
            chunks = jnp.where((relative == index)[:, None, None], block[None], chunks)
        return jnp.sum(lax.all_to_all(chunks, ORDER, 0, 0, tiled=False), axis=0)
    if lax.axis_size("normal") != 2 or lax.axis_size("circ") > 4:
        own = lax.psum(own + shifted(above, {"span": 1}) + shifted(below, {"span": -1}), ("circ", "normal"))
        return own
    partner = {"normal": 1}
    total = own + shifted(above, {"span": 1}) + shifted(below, {"span": -1})
    total = total + shifted(own, partner)
    total = total + shifted(above, dict(partner, span=1)) + shifted(below, dict(partner, span=-1))
    summed = total
    for step in range(1, lax.axis_size("circ")):
        summed = summed + shifted(total, {"circ": step})
    return summed


def on_device(
    adjoint,
    objective_grad,
    face_weights,
    owner_jac,
    neighbor_jac,
    coupling,
    stiffness,
    wall_kernel,
    panel_owner,
):
    fields = (adjoint, face_weights)
    halos = [
        face_halos(fields, "span", 1, False),
        face_halos(fields, "normal", 2, False),
        face_halos(fields, "circ", 3, True),
    ]
    residual = flux_faces(adjoint, face_weights, halos, owner_jac, neighbor_jac) + adjoint - objective_grad
    forcing = jac_apply(coupling.T, residual)
    margin = SWEEPS - 1
    joined = jnp.concatenate([stiffness[None], forcing], axis=0)
    full_pad = padded_sweeps(joined, margin)
    mesh = run_sweeps(full_pad[0], full_pad[1:])
    wall_sens = jnp.sum(wall_kernel[None] * mesh, axis=2)
    span = lax.axis_index("span")
    first = (span - 1) * PANEL_DEV
    local = panel_owner - first
    onehot = (
        local[:, :, None] == jnp.arange(3 * PANEL_DEV, dtype=jnp.int32)[None, None, :]
    ).astype(jnp.float32)
    terms = jnp.einsum("mki,kip->mp", wall_sens, onehot, precision=lax.Precision.HIGHEST)
    panels = reduce_panels(terms)
    return (residual, mesh, panels)


def joined_inputs(coeffs, loads, *rest):
    coeffs, loads = lax.optimization_barrier((coeffs, loads))
    jac = coeffs[: 2 * JAC].reshape(2, 3, 5, 5)
    coupling = coeffs[2 * JAC :].reshape(3, 5)
    return on_device(rest[0], loads[:5], rest[1], jac[0], jac[1], coupling, loads[5], rest[2], rest[3])


JAC = 75


def solution(mesh):
    field = P(None, "span", "normal", "circ")
    inner = jax.shard_map(
        joined_inputs,
        mesh=mesh,
        in_specs=(P(), field, field, field, P("span", "normal", "circ"), P("span", "circ")),
        out_specs=(field, field, P(None, "span")),
        check_vma=False,
    )

    def run(adjoint, objective_grad, face_weights, owner_jac, neighbor_jac, coupling, stiffness, wall_kernel, panel_owner):
        coeffs = jnp.concatenate([owner_jac.reshape(-1), neighbor_jac.reshape(-1), coupling.reshape(-1)])
        loads = jnp.concatenate([objective_grad, stiffness[None]], axis=0)
        return inner(coeffs, loads, adjoint, face_weights, wall_kernel, panel_owner)

    return run
```

```python
import itertools
import math

import jax
import jax.numpy as jnp
from jax import lax
from jax.sharding import PartitionSpec as P

PANEL_DEV = 128
SWEEPS = 4


def padded_2(array, sides, width, wrap):
    for axis, dim in sides:
        peers, length = (lax.axis_size(axis), array.shape[dim])
        up = [(i, (i + 1) % peers) for i in range(peers if wrap else peers - 1)]
        down = [(j, i) for i, j in up]
        last = lax.slice_in_dim(array, length - width, length, axis=dim)
        initial = lax.slice_in_dim(array, 0, width, axis=dim)
        before = lax.ppermute(last, axis, up)
        after = lax.ppermute(initial, axis, down)
        array = jnp.concatenate([before, array, after], axis=dim)
    return array


def neighbor_sum(padded):
    total = padded[:, 2:, 1:-1, 1:-1] + padded[:, :-2, 1:-1, 1:-1]
    total = total + padded[:, 1:-1, 2:, 1:-1] + padded[:, 1:-1, :-2, 1:-1]
    return total + padded[:, 1:-1, 1:-1, 2:] + padded[:, 1:-1, 1:-1, :-2]


def inner(field):
    return field[:, 1:-1, 1:-1, 1:-1]


def flux_transpose(padded, owner_jac, neighbor_jac):
    psi = padded[:5]
    weights = padded[5:]
    center = inner(psi)
    total = jnp.zeros_like(center)
    for direction in range(3):
        lower = [slice(None), slice(1, -1), slice(1, -1), slice(1, -1)]
        upper = [slice(None), slice(1, -1), slice(1, -1), slice(1, -1)]
        lower[direction + 1] = slice(0, -2)
        upper[direction + 1] = slice(2, None)
        w_here = weights[direction, 1:-1, 1:-1, 1:-1]
        w_lower = weights[direction][tuple(lower[1:])]
        up_term = w_here[None] * (center - psi[tuple(upper)])
        down_term = w_lower[None] * (psi[tuple(lower)] - center)
        total = total + jnp.einsum(
            "uv,ukji->vkji", owner_jac[direction], up_term, precision=lax.Precision.HIGHEST
        )
        total = total + jnp.einsum(
            "uv,ukji->vkji", neighbor_jac[direction], down_term, precision=lax.Precision.HIGHEST
        )
    return total


def relax(mesh_pad, stiff_pad, force_pad, scale_pad):
    weighted = stiff_pad[None] * mesh_pad
    stiff_in = stiff_pad[1:-1, 1:-1, 1:-1]
    diag_term = 6.0 * stiff_in + 1.0
    mesh_in = inner(mesh_pad)
    scale = scale_pad[1:-1, 1:-1, 1:-1]
    return mesh_in + scale[None] * (inner(force_pad) - diag_term[None] * mesh_in + neighbor_sum(weighted))


def run_sweeps(stiff_pad, force_pad):
    scale_pad = 0.8 / (6.0 * stiff_pad + 1.0)
    mesh_pad = force_pad * scale_pad[None]
    for sweep in range(1, SWEEPS):
        mesh_pad = relax(mesh_pad, stiff_pad, force_pad, scale_pad)
        stiff_pad = stiff_pad[1:-1, 1:-1, 1:-1]
        scale_pad = scale_pad[1:-1, 1:-1, 1:-1]
        force_pad = inner(force_pad)
    return mesh_pad


ORDER = ("circ", "normal", "span")
WRAP = {"circ": True, "normal": False, "span": False}


def edge(array, dim, side, width):
    length = array.shape[dim]
    start = length - width if side < 0 else 0
    return lax.slice_in_dim(array, start, start + width, axis=dim)


def pairs_for(offsets, wrap=()):
    axes = [a for a in ORDER if a in offsets]
    sizes = [lax.axis_size(a) for a in axes]
    pairs = []
    for source in itertools.product(*[range(n) for n in sizes]):
        target, inside = [], True
        for axis, q, n in zip(axes, source, sizes):
            t = q + offsets[axis]
            if WRAP[axis] or axis in wrap:
                t %= n
            elif not 0 <= t < n:
                inside = False
            target.append(t)
        if inside:
            lin = lambda v: sum(x * math.prod(sizes[i + 1 :]) for i, x in enumerate(v))
            pairs.append((lin(source), lin(target)))
    return tuple(axes), pairs


def take(array, rel, dims, width):
    for axis, r in rel.items():
        if r:
            array = edge(array, dims[axis], r, width)
    return array


def receive(array, rel, dims, width):
    rel = {a: r for a, r in rel.items() if r}
    axes, pairs = pairs_for({a: -r for a, r in rel.items()})
    return lax.ppermute(take(array, rel, dims, width), axes, pairs)


def receive_pair(array, rel, axis, dims, width):
    low = dict(rel, **{axis: -1})
    high = dict(rel, **{axis: 1})
    if lax.axis_size(axis) != 2 or WRAP[axis]:
        return receive(array, low, dims, width), receive(array, high, dims, width)
    me = lax.axis_index(axis)
    sent = jnp.where(me == 0, take(array, low, dims, width), take(array, high, dims, width))
    low_nz = {a: r for a, r in low.items() if r}
    axes, pairs = pairs_for({a: -r for a, r in low_nz.items()})
    _, back = pairs_for({a: -r for a, r in dict(low_nz, **{axis: 1}).items()})
    got = lax.ppermute(sent, axes, pairs + back)
    zero = jnp.zeros_like(got)
    return jnp.where(me == 1, got, zero), jnp.where(me == 0, got, zero)


def face_halos(fields, axis, dim, wrap):
    thin = jnp.concatenate(
        [jnp.concatenate([edge(f, dim, 1, 1), edge(f, dim, -1, 1)], axis=dim) for f in fields], axis=0
    )
    return receive_pair(thin, {}, axis, {axis: dim}, 1)


def padded_sweeps(joined, width):
    dims = {"span": 1, "normal": 2, "circ": 3}
    before_c = receive(joined, {"circ": -1}, dims, width)
    after_c = receive(joined, {"circ": 1}, dims, width)
    low_n, high_n = receive_pair(joined, {}, "normal", dims, width)
    low_lc, high_lc = receive_pair(joined, {"circ": -1}, "normal", dims, width)
    low_hc, high_hc = receive_pair(joined, {"circ": 1}, "normal", dims, width)
    top = jnp.concatenate([low_lc, low_n, low_hc], axis=3)
    middle = jnp.concatenate([before_c, joined, after_c], axis=3)
    bottom = jnp.concatenate([high_lc, high_n, high_hc], axis=3)
    plane = jnp.concatenate([top, middle, bottom], axis=2)
    before_s = receive(plane, {"span": -1}, dims, width)
    after_s = receive(plane, {"span": 1}, dims, width)
    return jnp.concatenate([before_s, plane, after_s], axis=1)


def jac_apply(jac, term):
    spread = (slice(None), slice(None)) + (None,) * (term.ndim - 1)
    return jnp.sum(jac[spread] * term[:, None], axis=0)


def flux_faces(psi, weights, halos, owner_jac, neighbor_jac):
    inner_terms = []
    for direction in range(3):
        dim = direction + 1
        length = psi.shape[dim]
        low = lax.slice_in_dim(psi, 0, length - 1, axis=dim)
        high = lax.slice_in_dim(psi, 1, length, axis=dim)
        w_low = lax.slice_in_dim(weights[direction], 0, length - 1, axis=direction)
        between = w_low[None] * (low - high)
        inner_terms.append((jac_apply(owner_jac[direction], between), jac_apply(neighbor_jac[direction], between)))
    inner_terms = lax.optimization_barrier(inner_terms)
    total = jnp.zeros_like(psi)
    for direction in range(3):
        dim = direction + 1
        length = psi.shape[dim]
        before, after = halos[direction]
        last = lax.slice_in_dim(psi, length - 1, length, axis=dim)
        first = lax.slice_in_dim(psi, 0, 1, axis=dim)
        w_last = lax.slice_in_dim(weights[direction], length - 1, length, axis=direction)
        up_edge = w_last[None] * (last - after[:5])
        down_edge = before[5 + direction][None] * (before[:5] - first)
        up_inner, down_inner = inner_terms[direction]
        up = jnp.concatenate([up_inner, jac_apply(owner_jac[direction], up_edge)], axis=dim)
        down = jnp.concatenate([jac_apply(neighbor_jac[direction], down_edge), down_inner], axis=dim)
        total = total + up
        total = total + down
    return total


def shifted(array, offsets):
    axes, pairs = pairs_for(offsets, ("normal",))
    return lax.ppermute(array, axes, pairs)


def reduce_panels(terms):
    below, own, above = (terms[:, i * PANEL_DEV : (i + 1) * PANEL_DEV] for i in range(3))
    devices = math.prod(lax.axis_size(a) for a in ORDER)
    if devices <= 64:
        spans = lax.axis_size("span")
        relative = jnp.arange(devices, dtype=jnp.int32) % spans - lax.axis_index("span") + 1
        chunks = jnp.zeros((devices,) + own.shape, own.dtype)
        for index, block in enumerate((below, own, above)):
            chunks = jnp.where((relative == index)[:, None, None], block[None], chunks)
        return jnp.sum(lax.all_to_all(chunks, ORDER, 0, 0, tiled=False), axis=0)
    if lax.axis_size("normal") != 2 or lax.axis_size("circ") > 4:
        own = lax.psum(own + shifted(above, {"span": 1}) + shifted(below, {"span": -1}), ("circ", "normal"))
        return own
    partner = {"normal": 1}
    total = own + shifted(above, {"span": 1}) + shifted(below, {"span": -1})
    total = total + shifted(own, partner)
    total = total + shifted(above, dict(partner, span=1)) + shifted(below, dict(partner, span=-1))
    summed = total
    for step in range(1, lax.axis_size("circ")):
        summed = summed + shifted(total, {"circ": step})
    return summed


def on_device(
    adjoint,
    objective_grad,
    face_weights,
    owner_jac,
    neighbor_jac,
    coupling,
    stiffness,
    wall_kernel,
    panel_owner,
):
    fields = (adjoint, face_weights)
    halos = [
        face_halos(fields, "span", 1, False),
        face_halos(fields, "normal", 2, False),
        face_halos(fields, "circ", 3, True),
    ]
    residual = flux_faces(adjoint, face_weights, halos, owner_jac, neighbor_jac) + adjoint - objective_grad
    forcing = jac_apply(coupling.T, residual)
    margin = SWEEPS - 1
    joined = jnp.concatenate([stiffness[None], forcing], axis=0)
    full_pad = padded_sweeps(joined, margin)
    mesh = run_sweeps(full_pad[0], full_pad[1:])
    wall_sens = jnp.sum(wall_kernel[None] * mesh, axis=2)
    span = lax.axis_index("span")
    first = (span - 1) * PANEL_DEV
    local = panel_owner - first
    onehot = (
        local[:, :, None] == jnp.arange(3 * PANEL_DEV, dtype=jnp.int32)[None, None, :]
    ).astype(jnp.float32)
    terms = jnp.einsum("mki,kip->mp", wall_sens, onehot, precision=lax.Precision.HIGHEST)
    panels = reduce_panels(terms)
    return (residual, mesh, panels)


def solution(mesh):
    placed = (
        P(None, "span", "normal", "circ"),
        P(None, "span", "normal", "circ"),
        P(None, "span", "normal", "circ"),
        P(),
        P(),
        P(),
        P("span", "normal", "circ"),
        P("span", "normal", "circ"),
        P("span", "circ"),
    )
    return jax.shard_map(
        on_device,
        mesh=mesh,
        in_specs=placed,
        out_specs=(
            P(None, "span", "normal", "circ"),
            P(None, "span", "normal", "circ"),
            P(None, "span"),
        ),
        check_vma=False,
    )
```

```python
import itertools
import math

import jax
import jax.numpy as jnp
from jax import lax
from jax.sharding import PartitionSpec as P

PANEL_DEV = 128
SWEEPS = 4


def padded_2(array, sides, width, wrap):
    for axis, dim in sides:
        peers, length = (lax.axis_size(axis), array.shape[dim])
        up = [(i, (i + 1) % peers) for i in range(peers if wrap else peers - 1)]
        down = [(j, i) for i, j in up]
        last = lax.slice_in_dim(array, length - width, length, axis=dim)
        initial = lax.slice_in_dim(array, 0, width, axis=dim)
        before = lax.ppermute(last, axis, up)
        after = lax.ppermute(initial, axis, down)
        array = jnp.concatenate([before, array, after], axis=dim)
    return array


def neighbor_sum(padded):
    total = padded[:, 2:, 1:-1, 1:-1] + padded[:, :-2, 1:-1, 1:-1]
    total = total + padded[:, 1:-1, 2:, 1:-1] + padded[:, 1:-1, :-2, 1:-1]
    return total + padded[:, 1:-1, 1:-1, 2:] + padded[:, 1:-1, 1:-1, :-2]


def inner(field):
    return field[:, 1:-1, 1:-1, 1:-1]


def flux_transpose(padded, owner_jac, neighbor_jac):
    psi = padded[:5]
    weights = padded[5:]
    center = inner(psi)
    total = jnp.zeros_like(center)
    for direction in range(3):
        lower = [slice(None), slice(1, -1), slice(1, -1), slice(1, -1)]
        upper = [slice(None), slice(1, -1), slice(1, -1), slice(1, -1)]
        lower[direction + 1] = slice(0, -2)
        upper[direction + 1] = slice(2, None)
        w_here = weights[direction, 1:-1, 1:-1, 1:-1]
        w_lower = weights[direction][tuple(lower[1:])]
        up_term = w_here[None] * (center - psi[tuple(upper)])
        down_term = w_lower[None] * (psi[tuple(lower)] - center)
        total = total + jnp.einsum(
            "uv,ukji->vkji", owner_jac[direction], up_term, precision=lax.Precision.HIGHEST
        )
        total = total + jnp.einsum(
            "uv,ukji->vkji", neighbor_jac[direction], down_term, precision=lax.Precision.HIGHEST
        )
    return total


def relax(mesh_pad, stiff_pad, force_pad):
    weighted = stiff_pad[None] * mesh_pad
    stiff_in = stiff_pad[1:-1, 1:-1, 1:-1]
    diag_term = 6.0 * stiff_in + 1.0
    mesh_in = inner(mesh_pad)
    return (
        mesh_in
        + 0.8
        * (inner(force_pad) - diag_term[None] * mesh_in + neighbor_sum(weighted))
        / diag_term[None]
    )


def run_sweeps(stiff_pad, force_pad):
    mesh_pad = 0.8 * force_pad / (6.0 * stiff_pad[None] + 1.0)
    for sweep in range(1, SWEEPS):
        mesh_pad = relax(mesh_pad, stiff_pad, force_pad)
        stiff_pad = stiff_pad[1:-1, 1:-1, 1:-1]
        force_pad = inner(force_pad)
    return mesh_pad


ORDER = ("circ", "normal", "span")
WRAP = {"circ": True, "normal": False, "span": False}


def edge(array, dim, side, width):
    length = array.shape[dim]
    start = length - width if side < 0 else 0
    return lax.slice_in_dim(array, start, start + width, axis=dim)


def pairs_for(offsets, wrap=()):
    axes = [a for a in ORDER if a in offsets]
    sizes = [lax.axis_size(a) for a in axes]
    pairs = []
    for source in itertools.product(*[range(n) for n in sizes]):
        target, inside = [], True
        for axis, q, n in zip(axes, source, sizes):
            t = q + offsets[axis]
            if WRAP[axis] or axis in wrap:
                t %= n
            elif not 0 <= t < n:
                inside = False
            target.append(t)
        if inside:
            lin = lambda v: sum(x * math.prod(sizes[i + 1 :]) for i, x in enumerate(v))
            pairs.append((lin(source), lin(target)))
    return tuple(axes), pairs


def take(array, rel, dims, width):
    for axis, r in rel.items():
        if r:
            array = edge(array, dims[axis], r, width)
    return array


def receive(array, rel, dims, width):
    rel = {a: r for a, r in rel.items() if r}
    axes, pairs = pairs_for({a: -r for a, r in rel.items()})
    return lax.ppermute(take(array, rel, dims, width), axes, pairs)


def receive_pair(array, rel, axis, dims, width):
    low = dict(rel, **{axis: -1})
    high = dict(rel, **{axis: 1})
    if lax.axis_size(axis) != 2 or WRAP[axis]:
        return receive(array, low, dims, width), receive(array, high, dims, width)
    me = lax.axis_index(axis)
    sent = jnp.where(me == 0, take(array, low, dims, width), take(array, high, dims, width))
    low_nz = {a: r for a, r in low.items() if r}
    axes, pairs = pairs_for({a: -r for a, r in low_nz.items()})
    _, back = pairs_for({a: -r for a, r in dict(low_nz, **{axis: 1}).items()})
    got = lax.ppermute(sent, axes, pairs + back)
    zero = jnp.zeros_like(got)
    return jnp.where(me == 1, got, zero), jnp.where(me == 0, got, zero)


def face_halos(fields, axis, dim, wrap):
    thin = jnp.concatenate(
        [jnp.concatenate([edge(f, dim, 1, 1), edge(f, dim, -1, 1)], axis=dim) for f in fields], axis=0
    )
    return receive_pair(thin, {}, axis, {axis: dim}, 1)


def padded_sweeps(joined, width):
    dims = {"span": 1, "normal": 2, "circ": 3}
    before_c = receive(joined, {"circ": -1}, dims, width)
    after_c = receive(joined, {"circ": 1}, dims, width)
    low_n, high_n = receive_pair(joined, {}, "normal", dims, width)
    low_lc, high_lc = receive_pair(joined, {"circ": -1}, "normal", dims, width)
    low_hc, high_hc = receive_pair(joined, {"circ": 1}, "normal", dims, width)
    top = jnp.concatenate([low_lc, low_n, low_hc], axis=3)
    middle = jnp.concatenate([before_c, joined, after_c], axis=3)
    bottom = jnp.concatenate([high_lc, high_n, high_hc], axis=3)
    plane = jnp.concatenate([top, middle, bottom], axis=2)
    before_s = receive(plane, {"span": -1}, dims, width)
    after_s = receive(plane, {"span": 1}, dims, width)
    return jnp.concatenate([before_s, plane, after_s], axis=1)


def jac_apply(jac, term):
    spread = (slice(None), slice(None)) + (None,) * (term.ndim - 1)
    return jnp.sum(jac[spread] * term[:, None], axis=0)


def flux_faces(psi, weights, halos, owner_jac, neighbor_jac):
    inner_terms = []
    for direction in range(3):
        dim = direction + 1
        length = psi.shape[dim]
        low = lax.slice_in_dim(psi, 0, length - 1, axis=dim)
        high = lax.slice_in_dim(psi, 1, length, axis=dim)
        w_low = lax.slice_in_dim(weights[direction], 0, length - 1, axis=direction)
        between = w_low[None] * (low - high)
        inner_terms.append((jac_apply(owner_jac[direction], between), jac_apply(neighbor_jac[direction], between)))
    inner_terms = lax.optimization_barrier(inner_terms)
    total = jnp.zeros_like(psi)
    for direction in range(3):
        dim = direction + 1
        length = psi.shape[dim]
        before, after = halos[direction]
        last = lax.slice_in_dim(psi, length - 1, length, axis=dim)
        first = lax.slice_in_dim(psi, 0, 1, axis=dim)
        w_last = lax.slice_in_dim(weights[direction], length - 1, length, axis=direction)
        up_edge = w_last[None] * (last - after[:5])
        down_edge = before[5 + direction][None] * (before[:5] - first)
        up_inner, down_inner = inner_terms[direction]
        up = jnp.concatenate([up_inner, jac_apply(owner_jac[direction], up_edge)], axis=dim)
        down = jnp.concatenate([jac_apply(neighbor_jac[direction], down_edge), down_inner], axis=dim)
        total = total + up
        total = total + down
    return total


def shifted(array, offsets):
    axes, pairs = pairs_for(offsets, ("normal",))
    return lax.ppermute(array, axes, pairs)


def reduce_panels(terms):
    below, own, above = (terms[:, i * PANEL_DEV : (i + 1) * PANEL_DEV] for i in range(3))
    devices = math.prod(lax.axis_size(a) for a in ORDER)
    if devices <= 64:
        spans = lax.axis_size("span")
        relative = jnp.arange(devices, dtype=jnp.int32) // (devices // spans) - lax.axis_index("span") + 1
        chunks = jnp.zeros((devices,) + own.shape, own.dtype)
        for index, block in enumerate((below, own, above)):
            chunks = jnp.where((relative == index)[:, None, None], block[None], chunks)
        return jnp.sum(lax.all_to_all(chunks, ORDER[::-1], 0, 0, tiled=False), axis=0)
    if lax.axis_size("normal") != 2 or lax.axis_size("circ") > 4:
        own = lax.psum(own + shifted(above, {"span": 1}) + shifted(below, {"span": -1}), ("circ", "normal"))
        return own
    partner = {"normal": 1}
    total = own + shifted(above, {"span": 1}) + shifted(below, {"span": -1})
    total = total + shifted(own, partner)
    total = total + shifted(above, dict(partner, span=1)) + shifted(below, dict(partner, span=-1))
    summed = total
    for step in range(1, lax.axis_size("circ")):
        summed = summed + shifted(total, {"circ": step})
    return summed


def on_device(
    adjoint,
    objective_grad,
    face_weights,
    owner_jac,
    neighbor_jac,
    coupling,
    stiffness,
    wall_kernel,
    panel_owner,
):
    fields = (adjoint, face_weights)
    halos = [
        face_halos(fields, "span", 1, False),
        face_halos(fields, "normal", 2, False),
        face_halos(fields, "circ", 3, True),
    ]
    residual = flux_faces(adjoint, face_weights, halos, owner_jac, neighbor_jac) + adjoint - objective_grad
    forcing = jac_apply(coupling.T, residual)
    margin = SWEEPS - 1
    joined = jnp.concatenate([stiffness[None], forcing], axis=0)
    full_pad = padded_sweeps(joined, margin)
    mesh = run_sweeps(full_pad[0], full_pad[1:])
    wall_sens = jnp.sum(wall_kernel[None] * mesh, axis=2)
    span = lax.axis_index("span")
    first = (span - 1) * PANEL_DEV
    local = panel_owner - first
    onehot = (
        local[:, :, None] == jnp.arange(3 * PANEL_DEV, dtype=jnp.int32)[None, None, :]
    ).astype(jnp.float32)
    terms = jnp.einsum("mki,kip->mp", wall_sens, onehot, precision=lax.Precision.HIGHEST)
    panels = reduce_panels(terms)
    return (residual, mesh, panels)


def solution(mesh):
    placed = (
        P(None, "span", "normal", "circ"),
        P(None, "span", "normal", "circ"),
        P(None, "span", "normal", "circ"),
        P(),
        P(),
        P(),
        P("span", "normal", "circ"),
        P("span", "normal", "circ"),
        P("span", "circ"),
    )
    return jax.shard_map(
        on_device,
        mesh=mesh,
        in_specs=placed,
        out_specs=(
            P(None, "span", "normal", "circ"),
            P(None, "span", "normal", "circ"),
            P(None, "span"),
        ),
        check_vma=False,
    )
```

```python
import itertools
import math

import jax
import jax.numpy as jnp
from jax import lax
from jax.sharding import PartitionSpec as P

PANEL_DEV = 128
SWEEPS = 4


def padded_2(array, sides, width, wrap):
    for axis, dim in sides:
        peers, length = (lax.axis_size(axis), array.shape[dim])
        up = [(i, (i + 1) % peers) for i in range(peers if wrap else peers - 1)]
        down = [(j, i) for i, j in up]
        last = lax.slice_in_dim(array, length - width, length, axis=dim)
        initial = lax.slice_in_dim(array, 0, width, axis=dim)
        before = lax.ppermute(last, axis, up)
        after = lax.ppermute(initial, axis, down)
        array = jnp.concatenate([before, array, after], axis=dim)
    return array


def neighbor_sum(padded):
    total = padded[:, 2:, 1:-1, 1:-1] + padded[:, :-2, 1:-1, 1:-1]
    total = total + padded[:, 1:-1, 2:, 1:-1] + padded[:, 1:-1, :-2, 1:-1]
    return total + padded[:, 1:-1, 1:-1, 2:] + padded[:, 1:-1, 1:-1, :-2]


def inner(field):
    return field[:, 1:-1, 1:-1, 1:-1]


def flux_transpose(padded, owner_jac, neighbor_jac):
    psi = padded[:5]
    weights = padded[5:]
    center = inner(psi)
    total = jnp.zeros_like(center)
    for direction in range(3):
        lower = [slice(None), slice(1, -1), slice(1, -1), slice(1, -1)]
        upper = [slice(None), slice(1, -1), slice(1, -1), slice(1, -1)]
        lower[direction + 1] = slice(0, -2)
        upper[direction + 1] = slice(2, None)
        w_here = weights[direction, 1:-1, 1:-1, 1:-1]
        w_lower = weights[direction][tuple(lower[1:])]
        up_term = w_here[None] * (center - psi[tuple(upper)])
        down_term = w_lower[None] * (psi[tuple(lower)] - center)
        total = total + jnp.einsum(
            "uv,ukji->vkji", owner_jac[direction], up_term, precision=lax.Precision.HIGHEST
        )
        total = total + jnp.einsum(
            "uv,ukji->vkji", neighbor_jac[direction], down_term, precision=lax.Precision.HIGHEST
        )
    return total


def relax(mesh_pad, stiff_pad, force_pad):
    weighted = stiff_pad[None] * mesh_pad
    stiff_in = stiff_pad[1:-1, 1:-1, 1:-1]
    diag_term = 6.0 * stiff_in + 1.0
    mesh_in = inner(mesh_pad)
    return (
        mesh_in
        + 0.8
        * (inner(force_pad) - diag_term[None] * mesh_in + neighbor_sum(weighted))
        / diag_term[None]
    )


def run_sweeps(stiff_pad, force_pad):
    mesh_pad = 0.8 * force_pad / (6.0 * stiff_pad[None] + 1.0)
    for sweep in range(1, SWEEPS):
        mesh_pad = relax(mesh_pad, stiff_pad, force_pad)
        stiff_pad = stiff_pad[1:-1, 1:-1, 1:-1]
        force_pad = inner(force_pad)
    return mesh_pad


ORDER = ("circ", "normal", "span")
WRAP = {"circ": True, "normal": False, "span": False}


def edge(array, dim, side, width):
    length = array.shape[dim]
    start = length - width if side < 0 else 0
    return lax.slice_in_dim(array, start, start + width, axis=dim)


def pairs_for(offsets, wrap=()):
    axes = [a for a in ORDER if a in offsets]
    sizes = [lax.axis_size(a) for a in axes]
    pairs = []
    for source in itertools.product(*[range(n) for n in sizes]):
        target, inside = [], True
        for axis, q, n in zip(axes, source, sizes):
            t = q + offsets[axis]
            if WRAP[axis] or axis in wrap:
                t %= n
            elif not 0 <= t < n:
                inside = False
            target.append(t)
        if inside:
            lin = lambda v: sum(x * math.prod(sizes[i + 1 :]) for i, x in enumerate(v))
            pairs.append((lin(source), lin(target)))
    return tuple(axes), pairs


def take(array, rel, dims, width):
    for axis, r in rel.items():
        if r:
            array = edge(array, dims[axis], r, width)
    return array


def receive(array, rel, dims, width):
    rel = {a: r for a, r in rel.items() if r}
    axes, pairs = pairs_for({a: -r for a, r in rel.items()})
    return lax.ppermute(take(array, rel, dims, width), axes, pairs)


def receive_pair(array, rel, axis, dims, width):
    low = dict(rel, **{axis: -1})
    high = dict(rel, **{axis: 1})
    if lax.axis_size(axis) != 2 or WRAP[axis]:
        return receive(array, low, dims, width), receive(array, high, dims, width)
    me = lax.axis_index(axis)
    sent = jnp.where(me == 0, take(array, low, dims, width), take(array, high, dims, width))
    low_nz = {a: r for a, r in low.items() if r}
    axes, pairs = pairs_for({a: -r for a, r in low_nz.items()})
    _, back = pairs_for({a: -r for a, r in dict(low_nz, **{axis: 1}).items()})
    got = lax.ppermute(sent, axes, pairs + back)
    zero = jnp.zeros_like(got)
    return jnp.where(me == 1, got, zero), jnp.where(me == 0, got, zero)


def tile_halos(fields, axis, dim, length):
    rows = 8
    me = lax.axis_index(axis)
    start = (1 - me) * (length - rows)
    sent = jnp.concatenate([lax.dynamic_slice_in_dim(f, start, rows, axis=dim) for f in fields], axis=0)
    got = lax.ppermute(sent, axis, [(0, 1), (1, 0)])
    low = lax.slice_in_dim(got, rows - 1, rows, axis=dim)
    high = lax.slice_in_dim(got, 0, 1, axis=dim)
    zero = jnp.zeros_like(low)
    return jnp.where(me == 1, low, zero), jnp.where(me == 0, high, zero)


def face_halos(fields, axis, dim, wrap):
    length = fields[0].shape[dim]
    if axis == "normal" and lax.axis_size(axis) == 2 and length >= 8:
        return tile_halos(fields, axis, dim, length)
    thin = jnp.concatenate(
        [jnp.concatenate([edge(f, dim, 1, 1), edge(f, dim, -1, 1)], axis=dim) for f in fields], axis=0
    )
    return receive_pair(thin, {}, axis, {axis: dim}, 1)


def padded_sweeps(joined, width):
    dims = {"span": 1, "normal": 2, "circ": 3}
    before_c = receive(joined, {"circ": -1}, dims, width)
    after_c = receive(joined, {"circ": 1}, dims, width)
    low_n, high_n = receive_pair(joined, {}, "normal", dims, width)
    low_lc, high_lc = receive_pair(joined, {"circ": -1}, "normal", dims, width)
    low_hc, high_hc = receive_pair(joined, {"circ": 1}, "normal", dims, width)
    top = jnp.concatenate([low_lc, low_n, low_hc], axis=3)
    middle = jnp.concatenate([before_c, joined, after_c], axis=3)
    bottom = jnp.concatenate([high_lc, high_n, high_hc], axis=3)
    plane = jnp.concatenate([top, middle, bottom], axis=2)
    before_s = receive(plane, {"span": -1}, dims, width)
    after_s = receive(plane, {"span": 1}, dims, width)
    return jnp.concatenate([before_s, plane, after_s], axis=1)


def jac_apply(jac, term):
    spread = (slice(None), slice(None)) + (None,) * (term.ndim - 1)
    return jnp.sum(jac[spread] * term[:, None], axis=0)


def flux_faces(psi, weights, halos, owner_jac, neighbor_jac):
    inner_terms = []
    for direction in range(3):
        dim = direction + 1
        length = psi.shape[dim]
        low = lax.slice_in_dim(psi, 0, length - 1, axis=dim)
        high = lax.slice_in_dim(psi, 1, length, axis=dim)
        w_low = lax.slice_in_dim(weights[direction], 0, length - 1, axis=direction)
        between = w_low[None] * (low - high)
        inner_terms.append((jac_apply(owner_jac[direction], between), jac_apply(neighbor_jac[direction], between)))
    inner_terms = lax.optimization_barrier(inner_terms)
    total = jnp.zeros_like(psi)
    for direction in range(3):
        dim = direction + 1
        length = psi.shape[dim]
        before, after = halos[direction]
        last = lax.slice_in_dim(psi, length - 1, length, axis=dim)
        first = lax.slice_in_dim(psi, 0, 1, axis=dim)
        w_last = lax.slice_in_dim(weights[direction], length - 1, length, axis=direction)
        up_edge = w_last[None] * (last - after[:5])
        down_edge = before[5 + direction][None] * (before[:5] - first)
        up_inner, down_inner = inner_terms[direction]
        up = jnp.concatenate([up_inner, jac_apply(owner_jac[direction], up_edge)], axis=dim)
        down = jnp.concatenate([jac_apply(neighbor_jac[direction], down_edge), down_inner], axis=dim)
        total = total + up
        total = total + down
    return total


def shifted(array, offsets):
    axes, pairs = pairs_for(offsets, ("normal",))
    return lax.ppermute(array, axes, pairs)


def reduce_panels(terms):
    below, own, above = (terms[:, i * PANEL_DEV : (i + 1) * PANEL_DEV] for i in range(3))
    devices = math.prod(lax.axis_size(a) for a in ORDER)
    if devices <= 64:
        spans = lax.axis_size("span")
        relative = jnp.arange(devices, dtype=jnp.int32) // (devices // spans) - lax.axis_index("span") + 1
        chunks = jnp.zeros((devices,) + own.shape, own.dtype)
        for index, block in enumerate((below, own, above)):
            chunks = jnp.where((relative == index)[:, None, None], block[None], chunks)
        return jnp.sum(lax.all_to_all(chunks, ORDER[::-1], 0, 0, tiled=False), axis=0)
    if lax.axis_size("normal") != 2 or lax.axis_size("circ") > 4:
        own = lax.psum(own + shifted(above, {"span": 1}) + shifted(below, {"span": -1}), ("circ", "normal"))
        return own
    partner = {"normal": 1}
    total = own + shifted(above, {"span": 1}) + shifted(below, {"span": -1})
    total = total + shifted(own, partner)
    total = total + shifted(above, dict(partner, span=1)) + shifted(below, dict(partner, span=-1))
    summed = total
    for step in range(1, lax.axis_size("circ")):
        summed = summed + shifted(total, {"circ": step})
    return summed


def on_device(
    adjoint,
    objective_grad,
    face_weights,
    owner_jac,
    neighbor_jac,
    coupling,
    stiffness,
    wall_kernel,
    panel_owner,
):
    fields = (adjoint, face_weights)
    halos = [
        face_halos(fields, "span", 1, False),
        face_halos(fields, "normal", 2, False),
        face_halos(fields, "circ", 3, True),
    ]
    residual = flux_faces(adjoint, face_weights, halos, owner_jac, neighbor_jac) + adjoint - objective_grad
    forcing = jac_apply(coupling.T, residual)
    margin = SWEEPS - 1
    joined = jnp.concatenate([stiffness[None], forcing], axis=0)
    full_pad = padded_sweeps(joined, margin)
    mesh = run_sweeps(full_pad[0], full_pad[1:])
    wall_sens = jnp.sum(wall_kernel[None] * mesh, axis=2)
    span = lax.axis_index("span")
    first = (span - 1) * PANEL_DEV
    local = panel_owner - first
    onehot = (
        local[:, :, None] == jnp.arange(3 * PANEL_DEV, dtype=jnp.int32)[None, None, :]
    ).astype(jnp.float32)
    terms = jnp.einsum("mki,kip->mp", wall_sens, onehot, precision=lax.Precision.HIGHEST)
    panels = reduce_panels(terms)
    return (residual, mesh, panels)


def solution(mesh):
    placed = (
        P(None, "span", "normal", "circ"),
        P(None, "span", "normal", "circ"),
        P(None, "span", "normal", "circ"),
        P(),
        P(),
        P(),
        P("span", "normal", "circ"),
        P("span", "normal", "circ"),
        P("span", "circ"),
    )
    return jax.shard_map(
        on_device,
        mesh=mesh,
        in_specs=placed,
        out_specs=(
            P(None, "span", "normal", "circ"),
            P(None, "span", "normal", "circ"),
            P(None, "span"),
        ),
        check_vma=False,
    )
```

```python
import itertools
import math

import jax
import jax.numpy as jnp
from jax import lax
from jax.sharding import PartitionSpec as P

PANEL_DEV = 128
SWEEPS = 4


def padded_2(array, sides, width, wrap):
    for axis, dim in sides:
        peers, length = (lax.axis_size(axis), array.shape[dim])
        up = [(i, (i + 1) % peers) for i in range(peers if wrap else peers - 1)]
        down = [(j, i) for i, j in up]
        last = lax.slice_in_dim(array, length - width, length, axis=dim)
        initial = lax.slice_in_dim(array, 0, width, axis=dim)
        before = lax.ppermute(last, axis, up)
        after = lax.ppermute(initial, axis, down)
        array = jnp.concatenate([before, array, after], axis=dim)
    return array


def neighbor_sum(padded):
    total = padded[:, 2:, 1:-1, 1:-1] + padded[:, :-2, 1:-1, 1:-1]
    total = total + padded[:, 1:-1, 2:, 1:-1] + padded[:, 1:-1, :-2, 1:-1]
    return total + padded[:, 1:-1, 1:-1, 2:] + padded[:, 1:-1, 1:-1, :-2]


def inner(field):
    return field[:, 1:-1, 1:-1, 1:-1]


def flux_transpose(padded, owner_jac, neighbor_jac):
    psi = padded[:5]
    weights = padded[5:]
    center = inner(psi)
    total = jnp.zeros_like(center)
    for direction in range(3):
        lower = [slice(None), slice(1, -1), slice(1, -1), slice(1, -1)]
        upper = [slice(None), slice(1, -1), slice(1, -1), slice(1, -1)]
        lower[direction + 1] = slice(0, -2)
        upper[direction + 1] = slice(2, None)
        w_here = weights[direction, 1:-1, 1:-1, 1:-1]
        w_lower = weights[direction][tuple(lower[1:])]
        up_term = w_here[None] * (center - psi[tuple(upper)])
        down_term = w_lower[None] * (psi[tuple(lower)] - center)
        total = total + jnp.einsum(
            "uv,ukji->vkji", owner_jac[direction], up_term, precision=lax.Precision.HIGHEST
        )
        total = total + jnp.einsum(
            "uv,ukji->vkji", neighbor_jac[direction], down_term, precision=lax.Precision.HIGHEST
        )
    return total


def relax(mesh_pad, stiff_pad, force_pad):
    weighted = stiff_pad[None] * mesh_pad
    stiff_in = stiff_pad[1:-1, 1:-1, 1:-1]
    diag_term = 6.0 * stiff_in + 1.0
    mesh_in = inner(mesh_pad)
    return (
        mesh_in
        + 0.8
        * (inner(force_pad) - diag_term[None] * mesh_in + neighbor_sum(weighted))
        / diag_term[None]
    )


def run_sweeps(stiff_pad, force_pad):
    mesh_pad = 0.8 * force_pad / (6.0 * stiff_pad[None] + 1.0)
    for sweep in range(1, SWEEPS):
        mesh_pad = relax(mesh_pad, stiff_pad, force_pad)
        stiff_pad = stiff_pad[1:-1, 1:-1, 1:-1]
        force_pad = inner(force_pad)
    return mesh_pad


ORDER = ("circ", "normal", "span")
WRAP = {"circ": True, "normal": False, "span": False}


def edge(array, dim, side, width):
    length = array.shape[dim]
    start = length - width if side < 0 else 0
    return lax.slice_in_dim(array, start, start + width, axis=dim)


def pairs_for(offsets, wrap=()):
    axes = [a for a in ORDER if a in offsets]
    sizes = [lax.axis_size(a) for a in axes]
    pairs = []
    for source in itertools.product(*[range(n) for n in sizes]):
        target, inside = [], True
        for axis, q, n in zip(axes, source, sizes):
            t = q + offsets[axis]
            if WRAP[axis] or axis in wrap:
                t %= n
            elif not 0 <= t < n:
                inside = False
            target.append(t)
        if inside:
            lin = lambda v: sum(x * math.prod(sizes[i + 1 :]) for i, x in enumerate(v))
            pairs.append((lin(source), lin(target)))
    return tuple(axes), pairs


def take(array, rel, dims, width):
    for axis, r in rel.items():
        if r:
            array = edge(array, dims[axis], r, width)
    return array


def receive(array, rel, dims, width):
    rel = {a: r for a, r in rel.items() if r}
    axes, pairs = pairs_for({a: -r for a, r in rel.items()})
    return lax.ppermute(take(array, rel, dims, width), axes, pairs)


def receive_pair(array, rel, axis, dims, width):
    low = dict(rel, **{axis: -1})
    high = dict(rel, **{axis: 1})
    if lax.axis_size(axis) != 2 or WRAP[axis]:
        return receive(array, low, dims, width), receive(array, high, dims, width)
    me = lax.axis_index(axis)
    sent = jnp.where(me == 0, take(array, low, dims, width), take(array, high, dims, width))
    low_nz = {a: r for a, r in low.items() if r}
    axes, pairs = pairs_for({a: -r for a, r in low_nz.items()})
    _, back = pairs_for({a: -r for a, r in dict(low_nz, **{axis: 1}).items()})
    got = lax.ppermute(sent, axes, pairs + back)
    zero = jnp.zeros_like(got)
    return jnp.where(me == 1, got, zero), jnp.where(me == 0, got, zero)


def tile_halos(fields, axis, dim, length):
    rows = 8
    me = lax.axis_index(axis)
    start = (1 - me) * (length - rows)
    sent = jnp.concatenate([lax.dynamic_slice_in_dim(f, start, rows, axis=dim) for f in fields], axis=0)
    got = lax.ppermute(sent, axis, [(0, 1), (1, 0)])
    low = lax.slice_in_dim(got, rows - 1, rows, axis=dim)
    high = lax.slice_in_dim(got, 0, 1, axis=dim)
    zero = jnp.zeros_like(low)
    return jnp.where(me == 1, low, zero), jnp.where(me == 0, high, zero)


def face_halos(fields, axis, dim, wrap):
    length = fields[0].shape[dim]
    if axis == "normal" and lax.axis_size(axis) == 2 and length >= 8:
        return tile_halos(fields, axis, dim, length)
    thin = jnp.concatenate(
        [jnp.concatenate([edge(f, dim, 1, 1), edge(f, dim, -1, 1)], axis=dim) for f in fields], axis=0
    )
    return receive_pair(thin, {}, axis, {axis: dim}, 1)


def padded_sweeps(joined, width):
    dims = {"span": 1, "normal": 2, "circ": 3}
    before_c = receive(joined, {"circ": -1}, dims, width)
    after_c = receive(joined, {"circ": 1}, dims, width)
    low_n, high_n = receive_pair(joined, {}, "normal", dims, width)
    low_lc, high_lc = receive_pair(joined, {"circ": -1}, "normal", dims, width)
    low_hc, high_hc = receive_pair(joined, {"circ": 1}, "normal", dims, width)
    top = jnp.concatenate([low_lc, low_n, low_hc], axis=3)
    middle = jnp.concatenate([before_c, joined, after_c], axis=3)
    bottom = jnp.concatenate([high_lc, high_n, high_hc], axis=3)
    plane = jnp.concatenate([top, middle, bottom], axis=2)
    before_s = receive(plane, {"span": -1}, dims, width)
    after_s = receive(plane, {"span": 1}, dims, width)
    return jnp.concatenate([before_s, plane, after_s], axis=1)


def jac_apply(jac, term):
    spread = (slice(None), slice(None)) + (None,) * (term.ndim - 1)
    return jnp.sum(jac[spread] * term[:, None], axis=0)


def flux_faces(psi, weights, halos, owner_jac, neighbor_jac):
    inner_terms = []
    for direction in range(3):
        dim = direction + 1
        length = psi.shape[dim]
        low = lax.slice_in_dim(psi, 0, length - 1, axis=dim)
        high = lax.slice_in_dim(psi, 1, length, axis=dim)
        w_low = lax.slice_in_dim(weights[direction], 0, length - 1, axis=direction)
        between = w_low[None] * (low - high)
        inner_terms.append((jac_apply(owner_jac[direction], between), jac_apply(neighbor_jac[direction], between)))
    inner_terms = lax.optimization_barrier(inner_terms)
    total = jnp.zeros_like(psi)
    for direction in range(3):
        dim = direction + 1
        length = psi.shape[dim]
        before, after = halos[direction]
        last = lax.slice_in_dim(psi, length - 1, length, axis=dim)
        first = lax.slice_in_dim(psi, 0, 1, axis=dim)
        w_last = lax.slice_in_dim(weights[direction], length - 1, length, axis=direction)
        up_edge = w_last[None] * (last - after[:5])
        down_edge = before[5 + direction][None] * (before[:5] - first)
        up_inner, down_inner = inner_terms[direction]
        up = jnp.concatenate([up_inner, jac_apply(owner_jac[direction], up_edge)], axis=dim)
        down = jnp.concatenate([jac_apply(neighbor_jac[direction], down_edge), down_inner], axis=dim)
        total = total + up
        total = total + down
    return total


def shifted(array, offsets):
    axes, pairs = pairs_for(offsets, ("normal",))
    return lax.ppermute(array, axes, pairs)


def reduce_panels(terms):
    below, own, above = (terms[:, i * PANEL_DEV : (i + 1) * PANEL_DEV] for i in range(3))
    devices = math.prod(lax.axis_size(a) for a in ORDER)
    if devices <= 64:
        spans = lax.axis_size("span")
        relative = jnp.arange(devices, dtype=jnp.int32) // (devices // spans) - lax.axis_index("span") + 1
        chunks = jnp.zeros((devices,) + own.shape, own.dtype)
        for index, block in enumerate((below, own, above)):
            chunks = jnp.where((relative == index)[:, None, None], block[None], chunks)
        return jnp.sum(lax.all_to_all(chunks, ORDER[::-1], 0, 0, tiled=False), axis=0)
    if lax.axis_size("normal") != 2 or lax.axis_size("circ") > 4:
        own = lax.psum(own + shifted(above, {"span": 1}) + shifted(below, {"span": -1}), ("circ", "normal"))
        return own
    partner = {"normal": 1}
    total = own + shifted(above, {"span": 1}) + shifted(below, {"span": -1})
    total = total + shifted(own, partner)
    total = total + shifted(above, dict(partner, span=1)) + shifted(below, dict(partner, span=-1))
    summed = total
    for step in range(1, lax.axis_size("circ")):
        summed = summed + shifted(total, {"circ": step})
    return summed


def on_device(
    adjoint,
    objective_grad,
    face_weights,
    owner_jac,
    neighbor_jac,
    coupling,
    stiffness,
    wall_kernel,
    panel_owner,
):
    fields = (adjoint, face_weights)
    halos = [
        face_halos(fields, "span", 1, False),
        face_halos(fields, "normal", 2, False),
        face_halos(fields, "circ", 3, True),
    ]
    residual = flux_faces(adjoint, face_weights, halos, owner_jac, neighbor_jac) + adjoint - objective_grad
    forcing = jac_apply(coupling.T, residual)
    margin = SWEEPS - 1
    joined = jnp.concatenate([stiffness[None], forcing], axis=0)
    full_pad = padded_sweeps(joined, margin)
    mesh = run_sweeps(full_pad[0], full_pad[1:])
    wall_sens = jnp.sum(wall_kernel[None] * mesh, axis=2)
    span = lax.axis_index("span")
    first = (span - 1) * PANEL_DEV
    local = panel_owner - first
    onehot = (
        local[:, :, None] == jnp.arange(3 * PANEL_DEV, dtype=jnp.int32)[None, None, :]
    ).astype(jnp.float32)
    terms = jnp.einsum("mki,kip->mp", wall_sens, onehot, precision=lax.Precision.HIGHEST)
    panels = reduce_panels(terms)
    return (residual, mesh, panels)


def joined_inputs(coeffs, loads, *rest):
    coeffs, loads = lax.optimization_barrier((coeffs, loads))
    jac = coeffs[: 2 * JAC].reshape(2, 3, 5, 5)
    coupling = coeffs[2 * JAC :].reshape(3, 5)
    return on_device(rest[0], loads[:5], rest[1], jac[0], jac[1], coupling, loads[5], rest[2], rest[3])


JAC = 75


def solution(mesh):
    field = P(None, "span", "normal", "circ")
    inner = jax.shard_map(
        joined_inputs,
        mesh=mesh,
        in_specs=(P(), field, field, field, P("span", "normal", "circ"), P("span", "circ")),
        out_specs=(field, field, P(None, "span")),
        check_vma=False,
    )

    def run(adjoint, objective_grad, face_weights, owner_jac, neighbor_jac, coupling, stiffness, wall_kernel, panel_owner):
        coeffs = jnp.concatenate([owner_jac.reshape(-1), neighbor_jac.reshape(-1), coupling.reshape(-1)])
        loads = jnp.concatenate([objective_grad, stiffness[None]], axis=0)
        return inner(coeffs, loads, adjoint, face_weights, wall_kernel, panel_owner)

    return run
```

```python
import itertools
import math

import jax
import jax.numpy as jnp
from jax import lax
from jax.sharding import PartitionSpec as P

PANEL_DEV = 128
SWEEPS = 4


def padded_2(array, sides, width, wrap):
    for axis, dim in sides:
        peers, length = (lax.axis_size(axis), array.shape[dim])
        up = [(i, (i + 1) % peers) for i in range(peers if wrap else peers - 1)]
        down = [(j, i) for i, j in up]
        last = lax.slice_in_dim(array, length - width, length, axis=dim)
        initial = lax.slice_in_dim(array, 0, width, axis=dim)
        before = lax.ppermute(last, axis, up)
        after = lax.ppermute(initial, axis, down)
        array = jnp.concatenate([before, array, after], axis=dim)
    return array


def neighbor_sum(padded):
    total = padded[:, 2:, 1:-1, 1:-1] + padded[:, :-2, 1:-1, 1:-1]
    total = total + padded[:, 1:-1, 2:, 1:-1] + padded[:, 1:-1, :-2, 1:-1]
    return total + padded[:, 1:-1, 1:-1, 2:] + padded[:, 1:-1, 1:-1, :-2]


def inner(field):
    return field[:, 1:-1, 1:-1, 1:-1]


def flux_transpose(padded, owner_jac, neighbor_jac):
    psi = padded[:5]
    weights = padded[5:]
    center = inner(psi)
    total = jnp.zeros_like(center)
    for direction in range(3):
        lower = [slice(None), slice(1, -1), slice(1, -1), slice(1, -1)]
        upper = [slice(None), slice(1, -1), slice(1, -1), slice(1, -1)]
        lower[direction + 1] = slice(0, -2)
        upper[direction + 1] = slice(2, None)
        w_here = weights[direction, 1:-1, 1:-1, 1:-1]
        w_lower = weights[direction][tuple(lower[1:])]
        up_term = w_here[None] * (center - psi[tuple(upper)])
        down_term = w_lower[None] * (psi[tuple(lower)] - center)
        total = total + jnp.einsum(
            "uv,ukji->vkji", owner_jac[direction], up_term, precision=lax.Precision.HIGHEST
        )
        total = total + jnp.einsum(
            "uv,ukji->vkji", neighbor_jac[direction], down_term, precision=lax.Precision.HIGHEST
        )
    return total


def relax(mesh_pad, stiff_pad, force_pad):
    weighted = stiff_pad[None] * mesh_pad
    stiff_in = stiff_pad[1:-1, 1:-1, 1:-1]
    diag_term = 6.0 * stiff_in + 1.0
    mesh_in = inner(mesh_pad)
    return (
        mesh_in
        + 0.8
        * (inner(force_pad) - diag_term[None] * mesh_in + neighbor_sum(weighted))
        / diag_term[None]
    )


def run_sweeps(stiff_pad, force_pad):
    mesh_pad = 0.8 * force_pad / (6.0 * stiff_pad[None] + 1.0)
    for sweep in range(1, SWEEPS):
        mesh_pad = relax(mesh_pad, stiff_pad, force_pad)
        stiff_pad = stiff_pad[1:-1, 1:-1, 1:-1]
        force_pad = inner(force_pad)
    return mesh_pad


ORDER = ("circ", "normal", "span")
WRAP = {"circ": True, "normal": False, "span": False}


def edge(array, dim, side, width):
    length = array.shape[dim]
    start = length - width if side < 0 else 0
    return lax.slice_in_dim(array, start, start + width, axis=dim)


def pairs_for(offsets, wrap=()):
    axes = [a for a in ORDER if a in offsets]
    sizes = [lax.axis_size(a) for a in axes]
    pairs = []
    for source in itertools.product(*[range(n) for n in sizes]):
        target, inside = [], True
        for axis, q, n in zip(axes, source, sizes):
            t = q + offsets[axis]
            if WRAP[axis] or axis in wrap:
                t %= n
            elif not 0 <= t < n:
                inside = False
            target.append(t)
        if inside:
            lin = lambda v: sum(x * math.prod(sizes[i + 1 :]) for i, x in enumerate(v))
            pairs.append((lin(source), lin(target)))
    return tuple(axes), pairs


def take(array, rel, dims, width):
    for axis, r in rel.items():
        if r:
            array = edge(array, dims[axis], r, width)
    return array


def receive(array, rel, dims, width):
    rel = {a: r for a, r in rel.items() if r}
    axes, pairs = pairs_for({a: -r for a, r in rel.items()})
    return lax.ppermute(take(array, rel, dims, width), axes, pairs)


def receive_pair(array, rel, axis, dims, width):
    low = dict(rel, **{axis: -1})
    high = dict(rel, **{axis: 1})
    if lax.axis_size(axis) != 2 or WRAP[axis]:
        return receive(array, low, dims, width), receive(array, high, dims, width)
    me = lax.axis_index(axis)
    sent = jnp.where(me == 0, take(array, low, dims, width), take(array, high, dims, width))
    low_nz = {a: r for a, r in low.items() if r}
    axes, pairs = pairs_for({a: -r for a, r in low_nz.items()})
    _, back = pairs_for({a: -r for a, r in dict(low_nz, **{axis: 1}).items()})
    got = lax.ppermute(sent, axes, pairs + back)
    zero = jnp.zeros_like(got)
    return jnp.where(me == 1, got, zero), jnp.where(me == 0, got, zero)


def tile_halos(fields, axis, dim, length):
    rows = 8
    me = lax.axis_index(axis)
    start = (1 - me) * (length - rows)
    sent = jnp.concatenate([lax.dynamic_slice_in_dim(f, start, rows, axis=dim) for f in fields], axis=0)
    got = lax.ppermute(sent, axis, [(0, 1), (1, 0)])
    low = lax.slice_in_dim(got, rows - 1, rows, axis=dim)
    high = lax.slice_in_dim(got, 0, 1, axis=dim)
    zero = jnp.zeros_like(low)
    return jnp.where(me == 1, low, zero), jnp.where(me == 0, high, zero)


def face_halos(fields, axis, dim, wrap):
    length = fields[0].shape[dim]
    if axis == "normal" and lax.axis_size(axis) == 2 and length >= 8:
        return tile_halos(fields, axis, dim, length)
    thin = jnp.concatenate(
        [jnp.concatenate([edge(f, dim, 1, 1), edge(f, dim, -1, 1)], axis=dim) for f in fields], axis=0
    )
    return receive_pair(thin, {}, axis, {axis: dim}, 1)


def padded_sweeps(joined, width):
    dims = {"span": 1, "normal": 2, "circ": 3}
    before_c = receive(joined, {"circ": -1}, dims, width)
    after_c = receive(joined, {"circ": 1}, dims, width)
    low_n, high_n = receive_pair(joined, {}, "normal", dims, width)
    low_lc, high_lc = receive_pair(joined, {"circ": -1}, "normal", dims, width)
    low_hc, high_hc = receive_pair(joined, {"circ": 1}, "normal", dims, width)
    top = jnp.concatenate([low_lc, low_n, low_hc], axis=3)
    middle = jnp.concatenate([before_c, joined, after_c], axis=3)
    bottom = jnp.concatenate([high_lc, high_n, high_hc], axis=3)
    plane = jnp.concatenate([top, middle, bottom], axis=2)
    before_s = receive(plane, {"span": -1}, dims, width)
    after_s = receive(plane, {"span": 1}, dims, width)
    return jnp.concatenate([before_s, plane, after_s], axis=1)


def jac_apply(jac, term):
    spread = (slice(None), slice(None)) + (None,) * (term.ndim - 1)
    return jnp.sum(jac[spread] * term[:, None], axis=0)


def flux_faces(psi, weights, halos, owner_jac, neighbor_jac):
    inner_terms = []
    for direction in range(3):
        dim = direction + 1
        length = psi.shape[dim]
        low = lax.slice_in_dim(psi, 0, length - 1, axis=dim)
        high = lax.slice_in_dim(psi, 1, length, axis=dim)
        w_low = lax.slice_in_dim(weights[direction], 0, length - 1, axis=direction)
        between = w_low[None] * (low - high)
        inner_terms.append((jac_apply(owner_jac[direction], between), jac_apply(neighbor_jac[direction], between)))
    inner_terms = lax.optimization_barrier(inner_terms)
    total = jnp.zeros_like(psi)
    for direction in range(3):
        dim = direction + 1
        length = psi.shape[dim]
        before, after = halos[direction]
        last = lax.slice_in_dim(psi, length - 1, length, axis=dim)
        first = lax.slice_in_dim(psi, 0, 1, axis=dim)
        w_last = lax.slice_in_dim(weights[direction], length - 1, length, axis=direction)
        up_edge = w_last[None] * (last - after[:5])
        down_edge = before[5][None] * (before[:5] - first)
        up_inner, down_inner = inner_terms[direction]
        up = jnp.concatenate([up_inner, jac_apply(owner_jac[direction], up_edge)], axis=dim)
        down = jnp.concatenate([jac_apply(neighbor_jac[direction], down_edge), down_inner], axis=dim)
        total = total + up
        total = total + down
    return total


def shifted(array, offsets):
    axes, pairs = pairs_for(offsets, ("normal",))
    return lax.ppermute(array, axes, pairs)


def reduce_panels(terms):
    below, own, above = (terms[:, i * PANEL_DEV : (i + 1) * PANEL_DEV] for i in range(3))
    devices = math.prod(lax.axis_size(a) for a in ORDER)
    if devices <= 64:
        spans = lax.axis_size("span")
        relative = jnp.arange(devices, dtype=jnp.int32) // (devices // spans) - lax.axis_index("span") + 1
        chunks = jnp.zeros((devices,) + own.shape, own.dtype)
        for index, block in enumerate((below, own, above)):
            chunks = jnp.where((relative == index)[:, None, None], block[None], chunks)
        return jnp.sum(lax.all_to_all(chunks, ORDER[::-1], 0, 0, tiled=False), axis=0)
    if lax.axis_size("normal") != 2 or lax.axis_size("circ") > 4:
        own = lax.psum(own + shifted(above, {"span": 1}) + shifted(below, {"span": -1}), ("circ", "normal"))
        return own
    partner = {"normal": 1}
    total = own + shifted(above, {"span": 1}) + shifted(below, {"span": -1})
    total = total + shifted(own, partner)
    total = total + shifted(above, dict(partner, span=1)) + shifted(below, dict(partner, span=-1))
    summed = total
    for step in range(1, lax.axis_size("circ")):
        summed = summed + shifted(total, {"circ": step})
    return summed


def on_device(
    adjoint,
    objective_grad,
    face_weights,
    owner_jac,
    neighbor_jac,
    coupling,
    stiffness,
    wall_kernel,
    panel_owner,
):
    halos = [
        face_halos((adjoint, face_weights[d : d + 1]), axis, d + 1, False)
        for d, axis in enumerate(("span", "normal", "circ"))
    ]
    residual = flux_faces(adjoint, face_weights, halos, owner_jac, neighbor_jac) + adjoint - objective_grad
    forcing = jac_apply(coupling.T, residual)
    margin = SWEEPS - 1
    joined = jnp.concatenate([stiffness[None], forcing], axis=0)
    full_pad = padded_sweeps(joined, margin)
    mesh = run_sweeps(full_pad[0], full_pad[1:])
    wall_sens = jnp.sum(wall_kernel[None] * mesh, axis=2)
    span = lax.axis_index("span")
    first = (span - 1) * PANEL_DEV
    local = panel_owner - first
    onehot = (
        local[:, :, None] == jnp.arange(3 * PANEL_DEV, dtype=jnp.int32)[None, None, :]
    ).astype(jnp.float32)
    terms = jnp.einsum("mki,kip->mp", wall_sens, onehot, precision=lax.Precision.HIGHEST)
    panels = reduce_panels(terms)
    return (residual, mesh, panels)


def solution(mesh):
    placed = (
        P(None, "span", "normal", "circ"),
        P(None, "span", "normal", "circ"),
        P(None, "span", "normal", "circ"),
        P(),
        P(),
        P(),
        P("span", "normal", "circ"),
        P("span", "normal", "circ"),
        P("span", "circ"),
    )
    return jax.shard_map(
        on_device,
        mesh=mesh,
        in_specs=placed,
        out_specs=(
            P(None, "span", "normal", "circ"),
            P(None, "span", "normal", "circ"),
            P(None, "span"),
        ),
        check_vma=False,
    )
```

```python
import itertools
import math

import jax
import jax.numpy as jnp
from jax import lax
from jax.sharding import PartitionSpec as P

PANEL_DEV = 128
SWEEPS = 4


def padded_2(array, sides, width, wrap):
    for axis, dim in sides:
        peers, length = (lax.axis_size(axis), array.shape[dim])
        up = [(i, (i + 1) % peers) for i in range(peers if wrap else peers - 1)]
        down = [(j, i) for i, j in up]
        last = lax.slice_in_dim(array, length - width, length, axis=dim)
        initial = lax.slice_in_dim(array, 0, width, axis=dim)
        before = lax.ppermute(last, axis, up)
        after = lax.ppermute(initial, axis, down)
        array = jnp.concatenate([before, array, after], axis=dim)
    return array


def neighbor_sum(padded):
    total = padded[:, 2:, 1:-1, 1:-1] + padded[:, :-2, 1:-1, 1:-1]
    total = total + padded[:, 1:-1, 2:, 1:-1] + padded[:, 1:-1, :-2, 1:-1]
    return total + padded[:, 1:-1, 1:-1, 2:] + padded[:, 1:-1, 1:-1, :-2]


def inner(field):
    return field[:, 1:-1, 1:-1, 1:-1]


def flux_transpose(padded, owner_jac, neighbor_jac):
    psi = padded[:5]
    weights = padded[5:]
    center = inner(psi)
    total = jnp.zeros_like(center)
    for direction in range(3):
        lower = [slice(None), slice(1, -1), slice(1, -1), slice(1, -1)]
        upper = [slice(None), slice(1, -1), slice(1, -1), slice(1, -1)]
        lower[direction + 1] = slice(0, -2)
        upper[direction + 1] = slice(2, None)
        w_here = weights[direction, 1:-1, 1:-1, 1:-1]
        w_lower = weights[direction][tuple(lower[1:])]
        up_term = w_here[None] * (center - psi[tuple(upper)])
        down_term = w_lower[None] * (psi[tuple(lower)] - center)
        total = total + jnp.einsum(
            "uv,ukji->vkji", owner_jac[direction], up_term, precision=lax.Precision.HIGHEST
        )
        total = total + jnp.einsum(
            "uv,ukji->vkji", neighbor_jac[direction], down_term, precision=lax.Precision.HIGHEST
        )
    return total


def relax(mesh_pad, stiff_pad, force_pad):
    weighted = stiff_pad[None] * mesh_pad
    stiff_in = stiff_pad[1:-1, 1:-1, 1:-1]
    diag_term = 6.0 * stiff_in + 1.0
    mesh_in = inner(mesh_pad)
    return (
        mesh_in
        + 0.8
        * (inner(force_pad) - diag_term[None] * mesh_in + neighbor_sum(weighted))
        / diag_term[None]
    )


def run_sweeps(stiff_pad, force_pad):
    mesh_pad = 0.8 * force_pad / (6.0 * stiff_pad[None] + 1.0)
    for sweep in range(1, SWEEPS):
        mesh_pad = relax(mesh_pad, stiff_pad, force_pad)
        stiff_pad = stiff_pad[1:-1, 1:-1, 1:-1]
        force_pad = inner(force_pad)
    return mesh_pad


ORDER = ("circ", "normal", "span")
WRAP = {"circ": True, "normal": False, "span": False}


def edge(array, dim, side, width):
    length = array.shape[dim]
    start = length - width if side < 0 else 0
    return lax.slice_in_dim(array, start, start + width, axis=dim)


def pairs_for(offsets, wrap=()):
    axes = [a for a in ORDER if a in offsets]
    sizes = [lax.axis_size(a) for a in axes]
    pairs = []
    for source in itertools.product(*[range(n) for n in sizes]):
        target, inside = [], True
        for axis, q, n in zip(axes, source, sizes):
            t = q + offsets[axis]
            if WRAP[axis] or axis in wrap:
                t %= n
            elif not 0 <= t < n:
                inside = False
            target.append(t)
        if inside:
            lin = lambda v: sum(x * math.prod(sizes[i + 1 :]) for i, x in enumerate(v))
            pairs.append((lin(source), lin(target)))
    return tuple(axes), pairs


def take(array, rel, dims, width):
    for axis, r in rel.items():
        if r:
            array = edge(array, dims[axis], r, width)
    return array


def receive(array, rel, dims, width):
    rel = {a: r for a, r in rel.items() if r}
    axes, pairs = pairs_for({a: -r for a, r in rel.items()})
    return lax.ppermute(take(array, rel, dims, width), axes, pairs)


def receive_pair(array, rel, axis, dims, width):
    low = dict(rel, **{axis: -1})
    high = dict(rel, **{axis: 1})
    if lax.axis_size(axis) != 2 or WRAP[axis]:
        return receive(array, low, dims, width), receive(array, high, dims, width)
    me = lax.axis_index(axis)
    sent = jnp.where(me == 0, take(array, low, dims, width), take(array, high, dims, width))
    low_nz = {a: r for a, r in low.items() if r}
    axes, pairs = pairs_for({a: -r for a, r in low_nz.items()})
    _, back = pairs_for({a: -r for a, r in dict(low_nz, **{axis: 1}).items()})
    got = lax.ppermute(sent, axes, pairs + back)
    zero = jnp.zeros_like(got)
    return jnp.where(me == 1, got, zero), jnp.where(me == 0, got, zero)


def tile_halos(fields, axis, dim, length):
    rows = 8
    me = lax.axis_index(axis)
    start = (1 - me) * (length - rows)
    sent = jnp.concatenate([lax.dynamic_slice_in_dim(f, start, rows, axis=dim) for f in fields], axis=0)
    got = lax.ppermute(sent, axis, [(0, 1), (1, 0)])
    low = lax.slice_in_dim(got, rows - 1, rows, axis=dim)
    high = lax.slice_in_dim(got, 0, 1, axis=dim)
    zero = jnp.zeros_like(low)
    return jnp.where(me == 1, low, zero), jnp.where(me == 0, high, zero)


def face_halos(fields, axis, dim, wrap):
    length = fields[0].shape[dim]
    if axis == "normal" and lax.axis_size(axis) == 2 and length >= 8:
        return tile_halos(fields, axis, dim, length)
    thin = jnp.concatenate(
        [jnp.concatenate([edge(f, dim, 1, 1), edge(f, dim, -1, 1)], axis=dim) for f in fields], axis=0
    )
    return receive_pair(thin, {}, axis, {axis: dim}, 1)


def padded_sweeps(joined, width):
    dims = {"span": 1, "normal": 2, "circ": 3}
    before_s = receive(joined, {"span": -1}, dims, width)
    after_s = receive(joined, {"span": 1}, dims, width)
    low_n, high_n = receive_pair(joined, {}, "normal", dims, width)
    low_ls, high_ls = receive_pair(joined, {"span": -1}, "normal", dims, width)
    low_hs, high_hs = receive_pair(joined, {"span": 1}, "normal", dims, width)
    top = jnp.concatenate([low_ls, low_n, low_hs], axis=1)
    middle = jnp.concatenate([before_s, joined, after_s], axis=1)
    bottom = jnp.concatenate([high_ls, high_n, high_hs], axis=1)
    plane = jnp.concatenate([top, middle, bottom], axis=2)
    before_c = receive(plane, {"circ": -1}, dims, width)
    after_c = receive(plane, {"circ": 1}, dims, width)
    return jnp.concatenate([before_c, plane, after_c], axis=3)


def jac_apply(jac, term):
    spread = (slice(None), slice(None)) + (None,) * (term.ndim - 1)
    return jnp.sum(jac[spread] * term[:, None], axis=0)


def flux_faces(psi, weights, halos, owner_jac, neighbor_jac):
    inner_terms = []
    for direction in range(3):
        dim = direction + 1
        length = psi.shape[dim]
        low = lax.slice_in_dim(psi, 0, length - 1, axis=dim)
        high = lax.slice_in_dim(psi, 1, length, axis=dim)
        w_low = lax.slice_in_dim(weights[direction], 0, length - 1, axis=direction)
        between = w_low[None] * (low - high)
        inner_terms.append((jac_apply(owner_jac[direction], between), jac_apply(neighbor_jac[direction], between)))
    inner_terms = lax.optimization_barrier(inner_terms)
    total = jnp.zeros_like(psi)
    for direction in range(3):
        dim = direction + 1
        length = psi.shape[dim]
        before, after = halos[direction]
        last = lax.slice_in_dim(psi, length - 1, length, axis=dim)
        first = lax.slice_in_dim(psi, 0, 1, axis=dim)
        w_last = lax.slice_in_dim(weights[direction], length - 1, length, axis=direction)
        up_edge = w_last[None] * (last - after[:5])
        down_edge = before[5][None] * (before[:5] - first)
        up_inner, down_inner = inner_terms[direction]
        up = jnp.concatenate([up_inner, jac_apply(owner_jac[direction], up_edge)], axis=dim)
        down = jnp.concatenate([jac_apply(neighbor_jac[direction], down_edge), down_inner], axis=dim)
        total = total + up
        total = total + down
    return total


def shifted(array, offsets):
    axes, pairs = pairs_for(offsets, ("normal",))
    return lax.ppermute(array, axes, pairs)


def reduce_panels(terms):
    below, own, above = (terms[:, i * PANEL_DEV : (i + 1) * PANEL_DEV] for i in range(3))
    devices = math.prod(lax.axis_size(a) for a in ORDER)
    if devices <= 64:
        spans = lax.axis_size("span")
        relative = jnp.arange(devices, dtype=jnp.int32) // (devices // spans) - lax.axis_index("span") + 1
        chunks = jnp.zeros((devices,) + own.shape, own.dtype)
        for index, block in enumerate((below, own, above)):
            chunks = jnp.where((relative == index)[:, None, None], block[None], chunks)
        return jnp.sum(lax.all_to_all(chunks, ORDER[::-1], 0, 0, tiled=False), axis=0)
    if lax.axis_size("normal") != 2 or lax.axis_size("circ") > 4:
        own = lax.psum(own + shifted(above, {"span": 1}) + shifted(below, {"span": -1}), ("circ", "normal"))
        return own
    partner = {"normal": 1}
    total = own + shifted(above, {"span": 1}) + shifted(below, {"span": -1})
    total = total + shifted(own, partner)
    total = total + shifted(above, dict(partner, span=1)) + shifted(below, dict(partner, span=-1))
    summed = total
    for step in range(1, lax.axis_size("circ")):
        summed = summed + shifted(total, {"circ": step})
    return summed


def on_device(
    adjoint,
    objective_grad,
    face_weights,
    owner_jac,
    neighbor_jac,
    coupling,
    stiffness,
    wall_kernel,
    panel_owner,
):
    halos = [
        face_halos((adjoint, face_weights[d : d + 1]), axis, d + 1, False)
        for d, axis in enumerate(("span", "normal", "circ"))
    ]
    residual = flux_faces(adjoint, face_weights, halos, owner_jac, neighbor_jac) + adjoint - objective_grad
    forcing = jac_apply(coupling.T, residual)
    margin = SWEEPS - 1
    joined = jnp.concatenate([stiffness[None], forcing], axis=0)
    full_pad = padded_sweeps(joined, margin)
    mesh = run_sweeps(full_pad[0], full_pad[1:])
    wall_sens = jnp.sum(wall_kernel[None] * mesh, axis=2)
    span = lax.axis_index("span")
    first = (span - 1) * PANEL_DEV
    local = panel_owner - first
    onehot = (
        local[:, :, None] == jnp.arange(3 * PANEL_DEV, dtype=jnp.int32)[None, None, :]
    ).astype(jnp.float32)
    terms = jnp.einsum("mki,kip->mp", wall_sens, onehot, precision=lax.Precision.HIGHEST)
    panels = reduce_panels(terms)
    return (residual, mesh, panels)


def solution(mesh):
    placed = (
        P(None, "span", "normal", "circ"),
        P(None, "span", "normal", "circ"),
        P(None, "span", "normal", "circ"),
        P(),
        P(),
        P(),
        P("span", "normal", "circ"),
        P("span", "normal", "circ"),
        P("span", "circ"),
    )
    return jax.shard_map(
        on_device,
        mesh=mesh,
        in_specs=placed,
        out_specs=(
            P(None, "span", "normal", "circ"),
            P(None, "span", "normal", "circ"),
            P(None, "span"),
        ),
        check_vma=False,
    )
```

```python
import itertools
import math

import jax
import jax.numpy as jnp
from jax import lax
from jax.sharding import PartitionSpec as P

PANEL_DEV = 128
SWEEPS = 4


def padded_2(array, sides, width, wrap):
    for axis, dim in sides:
        peers, length = (lax.axis_size(axis), array.shape[dim])
        up = [(i, (i + 1) % peers) for i in range(peers if wrap else peers - 1)]
        down = [(j, i) for i, j in up]
        last = lax.slice_in_dim(array, length - width, length, axis=dim)
        initial = lax.slice_in_dim(array, 0, width, axis=dim)
        before = lax.ppermute(last, axis, up)
        after = lax.ppermute(initial, axis, down)
        array = jnp.concatenate([before, array, after], axis=dim)
    return array


def neighbor_sum(padded):
    total = padded[:, 2:, 1:-1, 1:-1] + padded[:, :-2, 1:-1, 1:-1]
    total = total + padded[:, 1:-1, 2:, 1:-1] + padded[:, 1:-1, :-2, 1:-1]
    return total + padded[:, 1:-1, 1:-1, 2:] + padded[:, 1:-1, 1:-1, :-2]


def inner(field):
    return field[:, 1:-1, 1:-1, 1:-1]


def flux_transpose(padded, owner_jac, neighbor_jac):
    psi = padded[:5]
    weights = padded[5:]
    center = inner(psi)
    total = jnp.zeros_like(center)
    for direction in range(3):
        lower = [slice(None), slice(1, -1), slice(1, -1), slice(1, -1)]
        upper = [slice(None), slice(1, -1), slice(1, -1), slice(1, -1)]
        lower[direction + 1] = slice(0, -2)
        upper[direction + 1] = slice(2, None)
        w_here = weights[direction, 1:-1, 1:-1, 1:-1]
        w_lower = weights[direction][tuple(lower[1:])]
        up_term = w_here[None] * (center - psi[tuple(upper)])
        down_term = w_lower[None] * (psi[tuple(lower)] - center)
        total = total + jnp.einsum(
            "uv,ukji->vkji", owner_jac[direction], up_term, precision=lax.Precision.HIGHEST
        )
        total = total + jnp.einsum(
            "uv,ukji->vkji", neighbor_jac[direction], down_term, precision=lax.Precision.HIGHEST
        )
    return total


def relax(mesh_pad, stiff_pad, force_pad):
    weighted = stiff_pad[None] * mesh_pad
    stiff_in = stiff_pad[1:-1, 1:-1, 1:-1]
    diag_term = 6.0 * stiff_in + 1.0
    mesh_in = inner(mesh_pad)
    return (
        mesh_in
        + 0.8
        * (inner(force_pad) - diag_term[None] * mesh_in + neighbor_sum(weighted))
        / diag_term[None]
    )


def run_sweeps(stiff_pad, force_pad):
    mesh_pad = 0.8 * force_pad / (6.0 * stiff_pad[None] + 1.0)
    for sweep in range(1, SWEEPS):
        mesh_pad = relax(mesh_pad, stiff_pad, force_pad)
        stiff_pad = stiff_pad[1:-1, 1:-1, 1:-1]
        force_pad = inner(force_pad)
    return mesh_pad


ORDER = ("circ", "normal", "span")
WRAP = {"circ": True, "normal": False, "span": False}


def edge(array, dim, side, width):
    length = array.shape[dim]
    start = length - width if side < 0 else 0
    return lax.slice_in_dim(array, start, start + width, axis=dim)


def pairs_for(offsets, wrap=()):
    axes = [a for a in ORDER if a in offsets]
    sizes = [lax.axis_size(a) for a in axes]
    pairs = []
    for source in itertools.product(*[range(n) for n in sizes]):
        target, inside = [], True
        for axis, q, n in zip(axes, source, sizes):
            t = q + offsets[axis]
            if WRAP[axis] or axis in wrap:
                t %= n
            elif not 0 <= t < n:
                inside = False
            target.append(t)
        if inside:
            lin = lambda v: sum(x * math.prod(sizes[i + 1 :]) for i, x in enumerate(v))
            pairs.append((lin(source), lin(target)))
    return tuple(axes), pairs


def take(array, rel, dims, width):
    for axis, r in rel.items():
        if r:
            array = edge(array, dims[axis], r, width)
    return array


def receive(array, rel, dims, width, pack=False):
    rel = {a: r for a, r in rel.items() if r}
    axes, pairs = pairs_for({a: -r for a, r in rel.items()})
    slab = take(array, rel, dims, width)
    if not pack:
        return lax.ppermute(slab, axes, pairs)
    size = slab.size
    rows = -(-size // 1024) * 8
    flat = jnp.pad(slab.reshape(-1), (0, rows * 128 - size)).reshape(rows, 128)
    return lax.ppermute(flat, axes, pairs).reshape(-1)[:size].reshape(slab.shape)


def receive_pair(array, rel, axis, dims, width):
    low = dict(rel, **{axis: -1})
    high = dict(rel, **{axis: 1})
    if lax.axis_size(axis) != 2 or WRAP[axis]:
        return receive(array, low, dims, width), receive(array, high, dims, width)
    me = lax.axis_index(axis)
    sent = jnp.where(me == 0, take(array, low, dims, width), take(array, high, dims, width))
    low_nz = {a: r for a, r in low.items() if r}
    axes, pairs = pairs_for({a: -r for a, r in low_nz.items()})
    _, back = pairs_for({a: -r for a, r in dict(low_nz, **{axis: 1}).items()})
    got = lax.ppermute(sent, axes, pairs + back)
    zero = jnp.zeros_like(got)
    return jnp.where(me == 1, got, zero), jnp.where(me == 0, got, zero)


def tile_halos(fields, axis, dim, length):
    rows = 8
    me = lax.axis_index(axis)
    start = (1 - me) * (length - rows)
    sent = jnp.concatenate([lax.dynamic_slice_in_dim(f, start, rows, axis=dim) for f in fields], axis=0)
    got = lax.ppermute(sent, axis, [(0, 1), (1, 0)])
    low = lax.slice_in_dim(got, rows - 1, rows, axis=dim)
    high = lax.slice_in_dim(got, 0, 1, axis=dim)
    zero = jnp.zeros_like(low)
    return jnp.where(me == 1, low, zero), jnp.where(me == 0, high, zero)


def face_halos(fields, axis, dim, wrap):
    length = fields[0].shape[dim]
    if axis == "normal" and lax.axis_size(axis) == 2 and length >= 8:
        return tile_halos(fields, axis, dim, length)
    thin = jnp.concatenate(
        [jnp.concatenate([edge(f, dim, 1, 1), edge(f, dim, -1, 1)], axis=dim) for f in fields], axis=0
    )
    return receive_pair(thin, {}, axis, {axis: dim}, 1)


def padded_sweeps(joined, width):
    dims = {"span": 1, "normal": 2, "circ": 3}
    before_c = receive(joined, {"circ": -1}, dims, width)
    after_c = receive(joined, {"circ": 1}, dims, width)
    low_n, high_n = receive_pair(joined, {}, "normal", dims, width)
    low_lc, high_lc = receive_pair(joined, {"circ": -1}, "normal", dims, width)
    low_hc, high_hc = receive_pair(joined, {"circ": 1}, "normal", dims, width)
    top = jnp.concatenate([low_lc, low_n, low_hc], axis=3)
    middle = jnp.concatenate([before_c, joined, after_c], axis=3)
    bottom = jnp.concatenate([high_lc, high_n, high_hc], axis=3)
    plane = jnp.concatenate([top, middle, bottom], axis=2)
    before_s = receive(plane, {"span": -1}, dims, width, True)
    after_s = receive(plane, {"span": 1}, dims, width, True)
    return jnp.concatenate([before_s, plane, after_s], axis=1)


def jac_apply(jac, term):
    spread = (slice(None), slice(None)) + (None,) * (term.ndim - 1)
    return jnp.sum(jac[spread] * term[:, None], axis=0)


def flux_faces(psi, weights, halos, owner_jac, neighbor_jac):
    inner_terms = []
    for direction in range(3):
        dim = direction + 1
        length = psi.shape[dim]
        low = lax.slice_in_dim(psi, 0, length - 1, axis=dim)
        high = lax.slice_in_dim(psi, 1, length, axis=dim)
        w_low = lax.slice_in_dim(weights[direction], 0, length - 1, axis=direction)
        between = w_low[None] * (low - high)
        inner_terms.append((jac_apply(owner_jac[direction], between), jac_apply(neighbor_jac[direction], between)))
    inner_terms = lax.optimization_barrier(inner_terms)
    total = jnp.zeros_like(psi)
    for direction in range(3):
        dim = direction + 1
        length = psi.shape[dim]
        before, after = halos[direction]
        last = lax.slice_in_dim(psi, length - 1, length, axis=dim)
        first = lax.slice_in_dim(psi, 0, 1, axis=dim)
        w_last = lax.slice_in_dim(weights[direction], length - 1, length, axis=direction)
        up_edge = w_last[None] * (last - after[:5])
        down_edge = before[5][None] * (before[:5] - first)
        up_inner, down_inner = inner_terms[direction]
        up = jnp.concatenate([up_inner, jac_apply(owner_jac[direction], up_edge)], axis=dim)
        down = jnp.concatenate([jac_apply(neighbor_jac[direction], down_edge), down_inner], axis=dim)
        total = total + up
        total = total + down
    return total


def shifted(array, offsets):
    axes, pairs = pairs_for(offsets, ("normal",))
    return lax.ppermute(array, axes, pairs)


def reduce_panels(terms):
    below, own, above = (terms[:, i * PANEL_DEV : (i + 1) * PANEL_DEV] for i in range(3))
    devices = math.prod(lax.axis_size(a) for a in ORDER)
    if devices <= 64:
        spans = lax.axis_size("span")
        relative = jnp.arange(devices, dtype=jnp.int32) // (devices // spans) - lax.axis_index("span") + 1
        chunks = jnp.zeros((devices,) + own.shape, own.dtype)
        for index, block in enumerate((below, own, above)):
            chunks = jnp.where((relative == index)[:, None, None], block[None], chunks)
        return jnp.sum(lax.all_to_all(chunks, ORDER[::-1], 0, 0, tiled=False), axis=0)
    if lax.axis_size("normal") != 2 or lax.axis_size("circ") > 4:
        own = lax.psum(own + shifted(above, {"span": 1}) + shifted(below, {"span": -1}), ("circ", "normal"))
        return own
    partner = {"normal": 1}
    total = own + shifted(above, {"span": 1}) + shifted(below, {"span": -1})
    total = total + shifted(own, partner)
    total = total + shifted(above, dict(partner, span=1)) + shifted(below, dict(partner, span=-1))
    summed = total
    for step in range(1, lax.axis_size("circ")):
        summed = summed + shifted(total, {"circ": step})
    return summed


def on_device(
    adjoint,
    objective_grad,
    face_weights,
    owner_jac,
    neighbor_jac,
    coupling,
    stiffness,
    wall_kernel,
    panel_owner,
):
    halos = [
        face_halos((adjoint, face_weights[d : d + 1]), axis, d + 1, False)
        for d, axis in enumerate(("span", "normal", "circ"))
    ]
    residual = flux_faces(adjoint, face_weights, halos, owner_jac, neighbor_jac) + adjoint - objective_grad
    forcing = jac_apply(coupling.T, residual)
    margin = SWEEPS - 1
    joined = jnp.concatenate([stiffness[None], forcing], axis=0)
    full_pad = padded_sweeps(joined, margin)
    mesh = run_sweeps(full_pad[0], full_pad[1:])
    wall_sens = jnp.sum(wall_kernel[None] * mesh, axis=2)
    span = lax.axis_index("span")
    first = (span - 1) * PANEL_DEV
    local = panel_owner - first
    onehot = (
        local[:, :, None] == jnp.arange(3 * PANEL_DEV, dtype=jnp.int32)[None, None, :]
    ).astype(jnp.float32)
    terms = jnp.einsum("mki,kip->mp", wall_sens, onehot, precision=lax.Precision.HIGHEST)
    panels = reduce_panels(terms)
    return (residual, mesh, panels)


def solution(mesh):
    placed = (
        P(None, "span", "normal", "circ"),
        P(None, "span", "normal", "circ"),
        P(None, "span", "normal", "circ"),
        P(),
        P(),
        P(),
        P("span", "normal", "circ"),
        P("span", "normal", "circ"),
        P("span", "circ"),
    )
    return jax.shard_map(
        on_device,
        mesh=mesh,
        in_specs=placed,
        out_specs=(
            P(None, "span", "normal", "circ"),
            P(None, "span", "normal", "circ"),
            P(None, "span"),
        ),
        check_vma=False,
    )
```

```python
import itertools
import math

import jax
import jax.numpy as jnp
from jax import lax
from jax.sharding import PartitionSpec as P

PANEL_DEV = 128
SWEEPS = 4


def padded_2(array, sides, width, wrap):
    for axis, dim in sides:
        peers, length = (lax.axis_size(axis), array.shape[dim])
        up = [(i, (i + 1) % peers) for i in range(peers if wrap else peers - 1)]
        down = [(j, i) for i, j in up]
        last = lax.slice_in_dim(array, length - width, length, axis=dim)
        initial = lax.slice_in_dim(array, 0, width, axis=dim)
        before = lax.ppermute(last, axis, up)
        after = lax.ppermute(initial, axis, down)
        array = jnp.concatenate([before, array, after], axis=dim)
    return array


def neighbor_sum(padded):
    total = padded[:, 2:, 1:-1, 1:-1] + padded[:, :-2, 1:-1, 1:-1]
    total = total + padded[:, 1:-1, 2:, 1:-1] + padded[:, 1:-1, :-2, 1:-1]
    return total + padded[:, 1:-1, 1:-1, 2:] + padded[:, 1:-1, 1:-1, :-2]


def inner(field):
    return field[:, 1:-1, 1:-1, 1:-1]


def flux_transpose(padded, owner_jac, neighbor_jac):
    psi = padded[:5]
    weights = padded[5:]
    center = inner(psi)
    total = jnp.zeros_like(center)
    for direction in range(3):
        lower = [slice(None), slice(1, -1), slice(1, -1), slice(1, -1)]
        upper = [slice(None), slice(1, -1), slice(1, -1), slice(1, -1)]
        lower[direction + 1] = slice(0, -2)
        upper[direction + 1] = slice(2, None)
        w_here = weights[direction, 1:-1, 1:-1, 1:-1]
        w_lower = weights[direction][tuple(lower[1:])]
        up_term = w_here[None] * (center - psi[tuple(upper)])
        down_term = w_lower[None] * (psi[tuple(lower)] - center)
        total = total + jnp.einsum(
            "uv,ukji->vkji", owner_jac[direction], up_term, precision=lax.Precision.HIGHEST
        )
        total = total + jnp.einsum(
            "uv,ukji->vkji", neighbor_jac[direction], down_term, precision=lax.Precision.HIGHEST
        )
    return total


def relax(mesh_pad, stiff_pad, force_pad):
    weighted = stiff_pad[None] * mesh_pad
    stiff_in = stiff_pad[1:-1, 1:-1, 1:-1]
    diag_term = 6.0 * stiff_in + 1.0
    mesh_in = inner(mesh_pad)
    return (
        mesh_in
        + 0.8
        * (inner(force_pad) - diag_term[None] * mesh_in + neighbor_sum(weighted))
        / diag_term[None]
    )


def run_sweeps(stiff_pad, force_pad):
    mesh_pad = 0.8 * force_pad / (6.0 * stiff_pad[None] + 1.0)
    for sweep in range(1, SWEEPS):
        mesh_pad = relax(mesh_pad, stiff_pad, force_pad)
        stiff_pad = stiff_pad[1:-1, 1:-1, 1:-1]
        force_pad = inner(force_pad)
    return mesh_pad


ORDER = ("circ", "normal", "span")
WRAP = {"circ": True, "normal": False, "span": False}


def edge(array, dim, side, width):
    length = array.shape[dim]
    start = length - width if side < 0 else 0
    return lax.slice_in_dim(array, start, start + width, axis=dim)


def pairs_for(offsets, wrap=()):
    axes = [a for a in ORDER if a in offsets]
    sizes = [lax.axis_size(a) for a in axes]
    pairs = []
    for source in itertools.product(*[range(n) for n in sizes]):
        target, inside = [], True
        for axis, q, n in zip(axes, source, sizes):
            t = q + offsets[axis]
            if WRAP[axis] or axis in wrap:
                t %= n
            elif not 0 <= t < n:
                inside = False
            target.append(t)
        if inside:
            lin = lambda v: sum(x * math.prod(sizes[i + 1 :]) for i, x in enumerate(v))
            pairs.append((lin(source), lin(target)))
    return tuple(axes), pairs


def take(array, rel, dims, width):
    for axis, r in rel.items():
        if r:
            array = edge(array, dims[axis], r, width)
    return array


def receive(array, rel, dims, width, pack=False):
    rel = {a: r for a, r in rel.items() if r}
    axes, pairs = pairs_for({a: -r for a, r in rel.items()})
    slab = take(array, rel, dims, width)
    if not pack:
        return lax.ppermute(slab, axes, pairs)
    size = slab.size
    rows = -(-size // 1024) * 8
    flat = jnp.pad(slab.reshape(-1), (0, rows * 128 - size)).reshape(rows, 128)
    return lax.ppermute(flat, axes, pairs).reshape(-1)[:size].reshape(slab.shape)


def receive_pair(array, rel, axis, dims, width):
    low = dict(rel, **{axis: -1})
    high = dict(rel, **{axis: 1})
    if lax.axis_size(axis) != 2 or WRAP[axis]:
        return receive(array, low, dims, width), receive(array, high, dims, width)
    me = lax.axis_index(axis)
    sent = jnp.where(me == 0, take(array, low, dims, width), take(array, high, dims, width))
    low_nz = {a: r for a, r in low.items() if r}
    axes, pairs = pairs_for({a: -r for a, r in low_nz.items()})
    _, back = pairs_for({a: -r for a, r in dict(low_nz, **{axis: 1}).items()})
    got = lax.ppermute(sent, axes, pairs + back)
    zero = jnp.zeros_like(got)
    return jnp.where(me == 1, got, zero), jnp.where(me == 0, got, zero)


def tile_halos(fields, axis, dim, length):
    rows = 8
    me = lax.axis_index(axis)
    start = (1 - me) * (length - rows)
    sent = jnp.concatenate([lax.dynamic_slice_in_dim(f, start, rows, axis=dim) for f in fields], axis=0)
    got = lax.ppermute(sent, axis, [(0, 1), (1, 0)])
    low = lax.slice_in_dim(got, rows - 1, rows, axis=dim)
    high = lax.slice_in_dim(got, 0, 1, axis=dim)
    zero = jnp.zeros_like(low)
    return jnp.where(me == 1, low, zero), jnp.where(me == 0, high, zero)


def face_halos(fields, axis, dim, wrap):
    length = fields[0].shape[dim]
    if axis == "normal" and lax.axis_size(axis) == 2 and length >= 8:
        return tile_halos(fields, axis, dim, length)
    thin = jnp.concatenate(
        [jnp.concatenate([edge(f, dim, 1, 1), edge(f, dim, -1, 1)], axis=dim) for f in fields], axis=0
    )
    return receive_pair(thin, {}, axis, {axis: dim}, 1)


def padded_sweeps(joined, width):
    dims = {"span": 1, "normal": 2, "circ": 3}
    before_c = receive(joined, {"circ": -1}, dims, width, True)
    after_c = receive(joined, {"circ": 1}, dims, width, True)
    low_n, high_n = receive_pair(joined, {}, "normal", dims, width)
    low_lc, high_lc = receive_pair(joined, {"circ": -1}, "normal", dims, width)
    low_hc, high_hc = receive_pair(joined, {"circ": 1}, "normal", dims, width)
    top = jnp.concatenate([low_lc, low_n, low_hc], axis=3)
    middle = jnp.concatenate([before_c, joined, after_c], axis=3)
    bottom = jnp.concatenate([high_lc, high_n, high_hc], axis=3)
    plane = jnp.concatenate([top, middle, bottom], axis=2)
    before_s = receive(plane, {"span": -1}, dims, width, True)
    after_s = receive(plane, {"span": 1}, dims, width, True)
    return jnp.concatenate([before_s, plane, after_s], axis=1)


def jac_apply(jac, term):
    spread = (slice(None), slice(None)) + (None,) * (term.ndim - 1)
    return jnp.sum(jac[spread] * term[:, None], axis=0)


def flux_faces(psi, weights, halos, owner_jac, neighbor_jac):
    inner_terms = []
    for direction in range(3):
        dim = direction + 1
        length = psi.shape[dim]
        low = lax.slice_in_dim(psi, 0, length - 1, axis=dim)
        high = lax.slice_in_dim(psi, 1, length, axis=dim)
        w_low = lax.slice_in_dim(weights[direction], 0, length - 1, axis=direction)
        between = w_low[None] * (low - high)
        inner_terms.append((jac_apply(owner_jac[direction], between), jac_apply(neighbor_jac[direction], between)))
    inner_terms = lax.optimization_barrier(inner_terms)
    total = jnp.zeros_like(psi)
    for direction in range(3):
        dim = direction + 1
        length = psi.shape[dim]
        before, after = halos[direction]
        last = lax.slice_in_dim(psi, length - 1, length, axis=dim)
        first = lax.slice_in_dim(psi, 0, 1, axis=dim)
        w_last = lax.slice_in_dim(weights[direction], length - 1, length, axis=direction)
        up_edge = w_last[None] * (last - after[:5])
        down_edge = before[5][None] * (before[:5] - first)
        up_inner, down_inner = inner_terms[direction]
        up = jnp.concatenate([up_inner, jac_apply(owner_jac[direction], up_edge)], axis=dim)
        down = jnp.concatenate([jac_apply(neighbor_jac[direction], down_edge), down_inner], axis=dim)
        total = total + up
        total = total + down
    return total


def shifted(array, offsets):
    axes, pairs = pairs_for(offsets, ("normal",))
    return lax.ppermute(array, axes, pairs)


def reduce_panels(terms):
    below, own, above = (terms[:, i * PANEL_DEV : (i + 1) * PANEL_DEV] for i in range(3))
    devices = math.prod(lax.axis_size(a) for a in ORDER)
    if devices <= 64:
        spans = lax.axis_size("span")
        relative = jnp.arange(devices, dtype=jnp.int32) // (devices // spans) - lax.axis_index("span") + 1
        chunks = jnp.zeros((devices,) + own.shape, own.dtype)
        for index, block in enumerate((below, own, above)):
            chunks = jnp.where((relative == index)[:, None, None], block[None], chunks)
        return jnp.sum(lax.all_to_all(chunks, ORDER[::-1], 0, 0, tiled=False), axis=0)
    if lax.axis_size("normal") != 2 or lax.axis_size("circ") > 4:
        own = lax.psum(own + shifted(above, {"span": 1}) + shifted(below, {"span": -1}), ("circ", "normal"))
        return own
    partner = {"normal": 1}
    total = own + shifted(above, {"span": 1}) + shifted(below, {"span": -1})
    total = total + shifted(own, partner)
    total = total + shifted(above, dict(partner, span=1)) + shifted(below, dict(partner, span=-1))
    summed = total
    for step in range(1, lax.axis_size("circ")):
        summed = summed + shifted(total, {"circ": step})
    return summed


def on_device(
    adjoint,
    objective_grad,
    face_weights,
    owner_jac,
    neighbor_jac,
    coupling,
    stiffness,
    wall_kernel,
    panel_owner,
):
    halos = [
        face_halos((adjoint, face_weights[d : d + 1]), axis, d + 1, False)
        for d, axis in enumerate(("span", "normal", "circ"))
    ]
    residual = flux_faces(adjoint, face_weights, halos, owner_jac, neighbor_jac) + adjoint - objective_grad
    forcing = jac_apply(coupling.T, residual)
    margin = SWEEPS - 1
    joined = jnp.concatenate([stiffness[None], forcing], axis=0)
    full_pad = padded_sweeps(joined, margin)
    mesh = run_sweeps(full_pad[0], full_pad[1:])
    wall_sens = jnp.sum(wall_kernel[None] * mesh, axis=2)
    span = lax.axis_index("span")
    first = (span - 1) * PANEL_DEV
    local = panel_owner - first
    onehot = (
        local[:, :, None] == jnp.arange(3 * PANEL_DEV, dtype=jnp.int32)[None, None, :]
    ).astype(jnp.float32)
    terms = jnp.einsum("mki,kip->mp", wall_sens, onehot, precision=lax.Precision.HIGHEST)
    panels = reduce_panels(terms)
    return (residual, mesh, panels)


def solution(mesh):
    placed = (
        P(None, "span", "normal", "circ"),
        P(None, "span", "normal", "circ"),
        P(None, "span", "normal", "circ"),
        P(),
        P(),
        P(),
        P("span", "normal", "circ"),
        P("span", "normal", "circ"),
        P("span", "circ"),
    )
    return jax.shard_map(
        on_device,
        mesh=mesh,
        in_specs=placed,
        out_specs=(
            P(None, "span", "normal", "circ"),
            P(None, "span", "normal", "circ"),
            P(None, "span"),
        ),
        check_vma=False,
    )
```

```python
import itertools
import math

import jax
import jax.numpy as jnp
from jax import lax
from jax.sharding import PartitionSpec as P

PANEL_DEV = 128
SWEEPS = 4


def padded_2(array, sides, width, wrap):
    for axis, dim in sides:
        peers, length = (lax.axis_size(axis), array.shape[dim])
        up = [(i, (i + 1) % peers) for i in range(peers if wrap else peers - 1)]
        down = [(j, i) for i, j in up]
        last = lax.slice_in_dim(array, length - width, length, axis=dim)
        initial = lax.slice_in_dim(array, 0, width, axis=dim)
        before = lax.ppermute(last, axis, up)
        after = lax.ppermute(initial, axis, down)
        array = jnp.concatenate([before, array, after], axis=dim)
    return array


def neighbor_sum(padded):
    total = padded[:, 2:, 1:-1, 1:-1] + padded[:, :-2, 1:-1, 1:-1]
    total = total + padded[:, 1:-1, 2:, 1:-1] + padded[:, 1:-1, :-2, 1:-1]
    return total + padded[:, 1:-1, 1:-1, 2:] + padded[:, 1:-1, 1:-1, :-2]


def inner(field):
    return field[:, 1:-1, 1:-1, 1:-1]


def flux_transpose(padded, owner_jac, neighbor_jac):
    psi = padded[:5]
    weights = padded[5:]
    center = inner(psi)
    total = jnp.zeros_like(center)
    for direction in range(3):
        lower = [slice(None), slice(1, -1), slice(1, -1), slice(1, -1)]
        upper = [slice(None), slice(1, -1), slice(1, -1), slice(1, -1)]
        lower[direction + 1] = slice(0, -2)
        upper[direction + 1] = slice(2, None)
        w_here = weights[direction, 1:-1, 1:-1, 1:-1]
        w_lower = weights[direction][tuple(lower[1:])]
        up_term = w_here[None] * (center - psi[tuple(upper)])
        down_term = w_lower[None] * (psi[tuple(lower)] - center)
        total = total + jnp.einsum(
            "uv,ukji->vkji", owner_jac[direction], up_term, precision=lax.Precision.HIGHEST
        )
        total = total + jnp.einsum(
            "uv,ukji->vkji", neighbor_jac[direction], down_term, precision=lax.Precision.HIGHEST
        )
    return total


def relax(mesh_pad, stiff_pad, force_pad):
    weighted = stiff_pad[None] * mesh_pad
    stiff_in = stiff_pad[1:-1, 1:-1, 1:-1]
    diag_term = 6.0 * stiff_in + 1.0
    mesh_in = inner(mesh_pad)
    return (
        mesh_in
        + 0.8
        * (inner(force_pad) - diag_term[None] * mesh_in + neighbor_sum(weighted))
        / diag_term[None]
    )


def run_sweeps(stiff_pad, force_pad):
    mesh_pad = 0.8 * force_pad / (6.0 * stiff_pad[None] + 1.0)
    for sweep in range(1, SWEEPS):
        mesh_pad = relax(mesh_pad, stiff_pad, force_pad)
        stiff_pad = stiff_pad[1:-1, 1:-1, 1:-1]
        force_pad = inner(force_pad)
    return mesh_pad


ORDER = ("circ", "normal", "span")
WRAP = {"circ": True, "normal": False, "span": False}


def edge(array, dim, side, width):
    length = array.shape[dim]
    start = length - width if side < 0 else 0
    return lax.slice_in_dim(array, start, start + width, axis=dim)


def pairs_for(offsets, wrap=()):
    axes = [a for a in ORDER if a in offsets]
    sizes = [lax.axis_size(a) for a in axes]
    pairs = []
    for source in itertools.product(*[range(n) for n in sizes]):
        target, inside = [], True
        for axis, q, n in zip(axes, source, sizes):
            t = q + offsets[axis]
            if WRAP[axis] or axis in wrap:
                t %= n
            elif not 0 <= t < n:
                inside = False
            target.append(t)
        if inside:
            lin = lambda v: sum(x * math.prod(sizes[i + 1 :]) for i, x in enumerate(v))
            pairs.append((lin(source), lin(target)))
    return tuple(axes), pairs


def take(array, rel, dims, width):
    for axis, r in rel.items():
        if r:
            array = edge(array, dims[axis], r, width)
    return array


def receive(array, rel, dims, width, pack=False):
    rel = {a: r for a, r in rel.items() if r}
    axes, pairs = pairs_for({a: -r for a, r in rel.items()})
    slab = take(array, rel, dims, width)
    if not pack:
        return lax.ppermute(slab, axes, pairs)
    size = slab.size
    rows = -(-size // 1024) * 8
    flat = jnp.pad(slab.reshape(-1), (0, rows * 128 - size)).reshape(rows, 128)
    return lax.ppermute(flat, axes, pairs).reshape(-1)[:size].reshape(slab.shape)


def receive_pair(array, rel, axis, dims, width):
    low = dict(rel, **{axis: -1})
    high = dict(rel, **{axis: 1})
    if lax.axis_size(axis) != 2 or WRAP[axis]:
        return receive(array, low, dims, width), receive(array, high, dims, width)
    me = lax.axis_index(axis)
    sent = jnp.where(me == 0, take(array, low, dims, width), take(array, high, dims, width))
    low_nz = {a: r for a, r in low.items() if r}
    axes, pairs = pairs_for({a: -r for a, r in low_nz.items()})
    _, back = pairs_for({a: -r for a, r in dict(low_nz, **{axis: 1}).items()})
    got = lax.ppermute(sent, axes, pairs + back)
    zero = jnp.zeros_like(got)
    return jnp.where(me == 1, got, zero), jnp.where(me == 0, got, zero)


def tile_halos(fields, axis, dim, length):
    rows = 8
    me = lax.axis_index(axis)
    start = (1 - me) * (length - rows)
    sent = jnp.concatenate([lax.dynamic_slice_in_dim(f, start, rows, axis=dim) for f in fields], axis=0)
    got = lax.ppermute(sent, axis, [(0, 1), (1, 0)])
    low = lax.slice_in_dim(got, rows - 1, rows, axis=dim)
    high = lax.slice_in_dim(got, 0, 1, axis=dim)
    zero = jnp.zeros_like(low)
    return jnp.where(me == 1, low, zero), jnp.where(me == 0, high, zero)


def face_halos(fields, axis, dim, wrap):
    length = fields[0].shape[dim]
    if axis == "normal" and lax.axis_size(axis) == 2 and length >= 8:
        return tile_halos(fields, axis, dim, length)
    thin = jnp.concatenate(
        [jnp.concatenate([edge(f, dim, 1, 1), edge(f, dim, -1, 1)], axis=dim) for f in fields], axis=0
    )
    return receive_pair(thin, {}, axis, {axis: dim}, 1)


def padded_sweeps(joined, width):
    dims = {"span": 1, "normal": 2, "circ": 3}
    before_c = receive(joined, {"circ": -1}, dims, width)
    after_c = receive(joined, {"circ": 1}, dims, width)
    low_n, high_n = receive_pair(joined, {}, "normal", dims, width)
    low_lc, high_lc = receive_pair(joined, {"circ": -1}, "normal", dims, width)
    low_hc, high_hc = receive_pair(joined, {"circ": 1}, "normal", dims, width)
    top = jnp.concatenate([low_lc, low_n, low_hc], axis=3)
    middle = jnp.concatenate([before_c, joined, after_c], axis=3)
    bottom = jnp.concatenate([high_lc, high_n, high_hc], axis=3)
    plane = jnp.concatenate([top, middle, bottom], axis=2)
    before_s = receive(plane, {"span": -1}, dims, width, True)
    after_s = receive(plane, {"span": 1}, dims, width, True)
    return jnp.concatenate([before_s, plane, after_s], axis=1)


def jac_apply(jac, term):
    spread = (slice(None), slice(None)) + (None,) * (term.ndim - 1)
    return jnp.sum(jac[spread] * term[:, None], axis=0)


def flux_faces(psi, weights, halos, owner_jac, neighbor_jac):
    inner_terms = []
    for direction in range(3):
        dim = direction + 1
        length = psi.shape[dim]
        low = lax.slice_in_dim(psi, 0, length - 1, axis=dim)
        high = lax.slice_in_dim(psi, 1, length, axis=dim)
        w_low = lax.slice_in_dim(weights[direction], 0, length - 1, axis=direction)
        between = w_low[None] * (low - high)
        inner_terms.append((jac_apply(owner_jac[direction], between), jac_apply(neighbor_jac[direction], between)))
    inner_terms = lax.optimization_barrier(inner_terms)
    total = jnp.zeros_like(psi)
    for direction in range(3):
        dim = direction + 1
        length = psi.shape[dim]
        before, after = halos[direction]
        last = lax.slice_in_dim(psi, length - 1, length, axis=dim)
        first = lax.slice_in_dim(psi, 0, 1, axis=dim)
        w_last = lax.slice_in_dim(weights[direction], length - 1, length, axis=direction)
        up_edge = w_last[None] * (last - after[:5])
        down_edge = before[5][None] * (before[:5] - first)
        up_inner, down_inner = inner_terms[direction]
        up = jnp.concatenate([up_inner, jac_apply(owner_jac[direction], up_edge)], axis=dim)
        down = jnp.concatenate([jac_apply(neighbor_jac[direction], down_edge), down_inner], axis=dim)
        total = total + up
        total = total + down
    return total


def shifted(array, offsets):
    axes, pairs = pairs_for(offsets, ("normal",))
    return lax.ppermute(array, axes, pairs)


def reduce_panels(terms):
    below, own, above = (terms[:, i * PANEL_DEV : (i + 1) * PANEL_DEV] for i in range(3))
    devices = math.prod(lax.axis_size(a) for a in ORDER)
    if devices <= 64:
        spans = lax.axis_size("span")
        relative = jnp.arange(devices, dtype=jnp.int32) // (devices // spans) - lax.axis_index("span") + 1
        chunks = jnp.zeros((devices, own.size), own.dtype)
        for index, block in enumerate((below, own, above)):
            chunks = jnp.where((relative == index)[:, None], block.reshape(1, -1), chunks)
        got = lax.all_to_all(chunks, ORDER[::-1], 0, 0, tiled=False)
        return jnp.sum(got, axis=0).reshape(own.shape)
    if lax.axis_size("normal") != 2 or lax.axis_size("circ") > 4:
        own = lax.psum(own + shifted(above, {"span": 1}) + shifted(below, {"span": -1}), ("circ", "normal"))
        return own
    partner = {"normal": 1}
    total = own + shifted(above, {"span": 1}) + shifted(below, {"span": -1})
    total = total + shifted(own, partner)
    total = total + shifted(above, dict(partner, span=1)) + shifted(below, dict(partner, span=-1))
    summed = total
    for step in range(1, lax.axis_size("circ")):
        summed = summed + shifted(total, {"circ": step})
    return summed


def on_device(
    adjoint,
    objective_grad,
    face_weights,
    owner_jac,
    neighbor_jac,
    coupling,
    stiffness,
    wall_kernel,
    panel_owner,
):
    halos = [
        face_halos((adjoint, face_weights[d : d + 1]), axis, d + 1, False)
        for d, axis in enumerate(("span", "normal", "circ"))
    ]
    residual = flux_faces(adjoint, face_weights, halos, owner_jac, neighbor_jac) + adjoint - objective_grad
    forcing = jac_apply(coupling.T, residual)
    margin = SWEEPS - 1
    joined = jnp.concatenate([stiffness[None], forcing], axis=0)
    full_pad = padded_sweeps(joined, margin)
    mesh = run_sweeps(full_pad[0], full_pad[1:])
    wall_sens = jnp.sum(wall_kernel[None] * mesh, axis=2)
    span = lax.axis_index("span")
    first = (span - 1) * PANEL_DEV
    local = panel_owner - first
    onehot = (
        local[:, :, None] == jnp.arange(3 * PANEL_DEV, dtype=jnp.int32)[None, None, :]
    ).astype(jnp.float32)
    terms = jnp.einsum("mki,kip->mp", wall_sens, onehot, precision=lax.Precision.HIGHEST)
    panels = reduce_panels(terms)
    return (residual, mesh, panels)


def solution(mesh):
    placed = (
        P(None, "span", "normal", "circ"),
        P(None, "span", "normal", "circ"),
        P(None, "span", "normal", "circ"),
        P(),
        P(),
        P(),
        P("span", "normal", "circ"),
        P("span", "normal", "circ"),
        P("span", "circ"),
    )
    return jax.shard_map(
        on_device,
        mesh=mesh,
        in_specs=placed,
        out_specs=(
            P(None, "span", "normal", "circ"),
            P(None, "span", "normal", "circ"),
            P(None, "span"),
        ),
        check_vma=False,
    )
```

```python
import itertools
import math

import jax
import jax.numpy as jnp
from jax import lax
from jax.sharding import PartitionSpec as P

PANEL_DEV = 128
SWEEPS = 4


def padded_2(array, sides, width, wrap):
    for axis, dim in sides:
        peers, length = (lax.axis_size(axis), array.shape[dim])
        up = [(i, (i + 1) % peers) for i in range(peers if wrap else peers - 1)]
        down = [(j, i) for i, j in up]
        last = lax.slice_in_dim(array, length - width, length, axis=dim)
        initial = lax.slice_in_dim(array, 0, width, axis=dim)
        before = lax.ppermute(last, axis, up)
        after = lax.ppermute(initial, axis, down)
        array = jnp.concatenate([before, array, after], axis=dim)
    return array


def neighbor_sum(padded):
    total = padded[:, 2:, 1:-1, 1:-1] + padded[:, :-2, 1:-1, 1:-1]
    total = total + padded[:, 1:-1, 2:, 1:-1] + padded[:, 1:-1, :-2, 1:-1]
    return total + padded[:, 1:-1, 1:-1, 2:] + padded[:, 1:-1, 1:-1, :-2]


def inner(field):
    return field[:, 1:-1, 1:-1, 1:-1]


def flux_transpose(padded, owner_jac, neighbor_jac):
    psi = padded[:5]
    weights = padded[5:]
    center = inner(psi)
    total = jnp.zeros_like(center)
    for direction in range(3):
        lower = [slice(None), slice(1, -1), slice(1, -1), slice(1, -1)]
        upper = [slice(None), slice(1, -1), slice(1, -1), slice(1, -1)]
        lower[direction + 1] = slice(0, -2)
        upper[direction + 1] = slice(2, None)
        w_here = weights[direction, 1:-1, 1:-1, 1:-1]
        w_lower = weights[direction][tuple(lower[1:])]
        up_term = w_here[None] * (center - psi[tuple(upper)])
        down_term = w_lower[None] * (psi[tuple(lower)] - center)
        total = total + jnp.einsum(
            "uv,ukji->vkji", owner_jac[direction], up_term, precision=lax.Precision.HIGHEST
        )
        total = total + jnp.einsum(
            "uv,ukji->vkji", neighbor_jac[direction], down_term, precision=lax.Precision.HIGHEST
        )
    return total


def relax(mesh_pad, stiff_pad, force_pad):
    weighted = stiff_pad[None] * mesh_pad
    stiff_in = stiff_pad[1:-1, 1:-1, 1:-1]
    diag_term = 6.0 * stiff_in + 1.0
    mesh_in = inner(mesh_pad)
    return (
        mesh_in
        + 0.8
        * (inner(force_pad) - diag_term[None] * mesh_in + neighbor_sum(weighted))
        / diag_term[None]
    )


def run_sweeps(stiff_pad, force_pad):
    mesh_pad = 0.8 * force_pad / (6.0 * stiff_pad[None] + 1.0)
    for sweep in range(1, SWEEPS):
        mesh_pad = relax(mesh_pad, stiff_pad, force_pad)
        stiff_pad = stiff_pad[1:-1, 1:-1, 1:-1]
        force_pad = inner(force_pad)
    return mesh_pad


ORDER = ("circ", "normal", "span")
WRAP = {"circ": True, "normal": False, "span": False}


def edge(array, dim, side, width):
    length = array.shape[dim]
    start = length - width if side < 0 else 0
    return lax.slice_in_dim(array, start, start + width, axis=dim)


def pairs_for(offsets, wrap=()):
    axes = [a for a in ORDER if a in offsets]
    sizes = [lax.axis_size(a) for a in axes]
    pairs = []
    for source in itertools.product(*[range(n) for n in sizes]):
        target, inside = [], True
        for axis, q, n in zip(axes, source, sizes):
            t = q + offsets[axis]
            if WRAP[axis] or axis in wrap:
                t %= n
            elif not 0 <= t < n:
                inside = False
            target.append(t)
        if inside:
            lin = lambda v: sum(x * math.prod(sizes[i + 1 :]) for i, x in enumerate(v))
            pairs.append((lin(source), lin(target)))
    return tuple(axes), pairs


def take(array, rel, dims, width):
    for axis, r in rel.items():
        if r:
            array = edge(array, dims[axis], r, width)
    return array


def receive(array, rel, dims, width, pack=False):
    rel = {a: r for a, r in rel.items() if r}
    axes, pairs = pairs_for({a: -r for a, r in rel.items()})
    slab = take(array, rel, dims, width)
    if not pack:
        return lax.ppermute(slab, axes, pairs)
    size = slab.size
    rows = -(-size // 1024) * 8
    flat = jnp.pad(slab.reshape(-1), (0, rows * 128 - size)).reshape(rows, 128)
    return lax.ppermute(flat, axes, pairs).reshape(-1)[:size].reshape(slab.shape)


def receive_pair(array, rel, axis, dims, width):
    low = dict(rel, **{axis: -1})
    high = dict(rel, **{axis: 1})
    if lax.axis_size(axis) != 2 or WRAP[axis]:
        return receive(array, low, dims, width), receive(array, high, dims, width)
    me = lax.axis_index(axis)
    sent = jnp.where(me == 0, take(array, low, dims, width), take(array, high, dims, width))
    low_nz = {a: r for a, r in low.items() if r}
    axes, pairs = pairs_for({a: -r for a, r in low_nz.items()})
    _, back = pairs_for({a: -r for a, r in dict(low_nz, **{axis: 1}).items()})
    got = lax.ppermute(sent, axes, pairs + back)
    zero = jnp.zeros_like(got)
    return jnp.where(me == 1, got, zero), jnp.where(me == 0, got, zero)


def tile_halos(fields, axis, dim, length):
    rows = 8
    me = lax.axis_index(axis)
    start = (1 - me) * (length - rows)
    sent = jnp.concatenate([lax.dynamic_slice_in_dim(f, start, rows, axis=dim) for f in fields], axis=0)
    got = lax.ppermute(sent, axis, [(0, 1), (1, 0)])
    low = lax.slice_in_dim(got, rows - 1, rows, axis=dim)
    high = lax.slice_in_dim(got, 0, 1, axis=dim)
    zero = jnp.zeros_like(low)
    return jnp.where(me == 1, low, zero), jnp.where(me == 0, high, zero)


def face_halos(fields, axis, dim, wrap):
    length = fields[0].shape[dim]
    if axis == "normal" and lax.axis_size(axis) == 2 and length >= 8:
        return tile_halos(fields, axis, dim, length)
    thin = jnp.concatenate(
        [jnp.concatenate([edge(f, dim, 1, 1), edge(f, dim, -1, 1)], axis=dim) for f in fields], axis=0
    )
    return receive_pair(thin, {}, axis, {axis: dim}, 1)


def padded_sweeps(joined, width):
    dims = {"span": 1, "normal": 2, "circ": 3}
    before_c = receive(joined, {"circ": -1}, dims, width)
    after_c = receive(joined, {"circ": 1}, dims, width)
    low_n, high_n = receive_pair(joined, {}, "normal", dims, width)
    low_lc, high_lc = receive_pair(joined, {"circ": -1}, "normal", dims, width)
    low_hc, high_hc = receive_pair(joined, {"circ": 1}, "normal", dims, width)
    top = jnp.concatenate([low_lc, low_n, low_hc], axis=3)
    middle = jnp.concatenate([before_c, joined, after_c], axis=3)
    bottom = jnp.concatenate([high_lc, high_n, high_hc], axis=3)
    plane = jnp.concatenate([top, middle, bottom], axis=2)
    before_s = receive(plane, {"span": -1}, dims, width, True)
    after_s = receive(plane, {"span": 1}, dims, width, True)
    return jnp.concatenate([before_s, plane, after_s], axis=1)


def jac_apply(jac, term):
    spread = (slice(None), slice(None)) + (None,) * (term.ndim - 1)
    return jnp.sum(jac[spread] * term[:, None], axis=0)


def flux_faces(psi, weights, halos, owner_jac, neighbor_jac):
    inner_terms = []
    for direction in range(3):
        dim = direction + 1
        length = psi.shape[dim]
        low = lax.slice_in_dim(psi, 0, length - 1, axis=dim)
        high = lax.slice_in_dim(psi, 1, length, axis=dim)
        w_low = lax.slice_in_dim(weights[direction], 0, length - 1, axis=direction)
        between = w_low[None] * (low - high)
        inner_terms.append((jac_apply(owner_jac[direction], between), jac_apply(neighbor_jac[direction], between)))
    inner_terms = lax.optimization_barrier(inner_terms)
    total = jnp.zeros_like(psi)
    for direction in range(3):
        dim = direction + 1
        length = psi.shape[dim]
        before, after = halos[direction]
        last = lax.slice_in_dim(psi, length - 1, length, axis=dim)
        first = lax.slice_in_dim(psi, 0, 1, axis=dim)
        w_last = lax.slice_in_dim(weights[direction], length - 1, length, axis=direction)
        up_edge = w_last[None] * (last - after[:5])
        down_edge = before[5][None] * (before[:5] - first)
        up_inner, down_inner = inner_terms[direction]
        up = jnp.concatenate([up_inner, jac_apply(owner_jac[direction], up_edge)], axis=dim)
        down = jnp.concatenate([jac_apply(neighbor_jac[direction], down_edge), down_inner], axis=dim)
        total = total + up
        total = total + down
    return total


def shifted(array, offsets):
    axes, pairs = pairs_for(offsets, ("normal",))
    return lax.ppermute(array, axes, pairs)


def reduce_panels(terms):
    below, own, above = (terms[:, i * PANEL_DEV : (i + 1) * PANEL_DEV] for i in range(3))
    devices = math.prod(lax.axis_size(a) for a in ORDER)
    if devices <= 64:
        spans = lax.axis_size("span")
        relative = jnp.arange(devices, dtype=jnp.int32) // (devices // spans) - lax.axis_index("span") + 1
        chunks = jnp.zeros((devices,) + own.shape, own.dtype)
        for index, block in enumerate((below, own, above)):
            chunks = jnp.where((relative == index)[:, None, None], block[None], chunks)
        return jnp.sum(lax.all_to_all(chunks, ORDER[::-1], 0, 0, tiled=False), axis=0)
    if lax.axis_size("normal") != 2 or lax.axis_size("circ") > 4:
        own = lax.psum(own + shifted(above, {"span": 1}) + shifted(below, {"span": -1}), ("circ", "normal"))
        return own
    partner = {"normal": 1}
    total = own + shifted(above, {"span": 1}) + shifted(below, {"span": -1})
    total = total + shifted(own, partner)
    total = total + shifted(above, dict(partner, span=1)) + shifted(below, dict(partner, span=-1))
    summed = total
    for step in range(1, lax.axis_size("circ")):
        summed = summed + shifted(total, {"circ": step})
    return summed


def on_device(
    adjoint,
    objective_grad,
    face_weights,
    owner_jac,
    neighbor_jac,
    coupling,
    stiffness,
    wall_kernel,
    panel_owner,
):
    halos = [
        face_halos((adjoint, face_weights[d : d + 1]), axis, d + 1, False)
        for d, axis in enumerate(("span", "normal", "circ"))
    ]
    residual = flux_faces(adjoint, face_weights, halos, owner_jac, neighbor_jac) + adjoint - objective_grad
    forcing = jac_apply(coupling.T, residual)
    margin = SWEEPS - 1
    joined = jnp.concatenate([stiffness[None], forcing], axis=0)
    full_pad = padded_sweeps(joined, margin)
    mesh = run_sweeps(full_pad[0], full_pad[1:])
    wall_sens = jnp.sum(wall_kernel[None] * mesh, axis=2)
    span = lax.axis_index("span")
    first = (span - 1) * PANEL_DEV
    local = panel_owner - first
    onehot = (
        local[:, :, None] == jnp.arange(3 * PANEL_DEV, dtype=jnp.int32)[None, None, :]
    ).astype(jnp.float32)
    terms = jnp.einsum("mki,kip->mp", wall_sens, onehot, precision=lax.Precision.HIGH)
    panels = reduce_panels(terms)
    return (residual, mesh, panels)


def solution(mesh):
    placed = (
        P(None, "span", "normal", "circ"),
        P(None, "span", "normal", "circ"),
        P(None, "span", "normal", "circ"),
        P(),
        P(),
        P(),
        P("span", "normal", "circ"),
        P("span", "normal", "circ"),
        P("span", "circ"),
    )
    return jax.shard_map(
        on_device,
        mesh=mesh,
        in_specs=placed,
        out_specs=(
            P(None, "span", "normal", "circ"),
            P(None, "span", "normal", "circ"),
            P(None, "span"),
        ),
        check_vma=False,
    )
```

```python
import itertools
import math

import jax
import jax.numpy as jnp
from jax import lax
from jax.sharding import PartitionSpec as P

PANEL_DEV = 128
SWEEPS = 4


def padded_2(array, sides, width, wrap):
    for axis, dim in sides:
        peers, length = (lax.axis_size(axis), array.shape[dim])
        up = [(i, (i + 1) % peers) for i in range(peers if wrap else peers - 1)]
        down = [(j, i) for i, j in up]
        last = lax.slice_in_dim(array, length - width, length, axis=dim)
        initial = lax.slice_in_dim(array, 0, width, axis=dim)
        before = lax.ppermute(last, axis, up)
        after = lax.ppermute(initial, axis, down)
        array = jnp.concatenate([before, array, after], axis=dim)
    return array


def neighbor_sum(padded):
    total = padded[:, 2:, 1:-1, 1:-1] + padded[:, :-2, 1:-1, 1:-1]
    total = total + padded[:, 1:-1, 2:, 1:-1] + padded[:, 1:-1, :-2, 1:-1]
    return total + padded[:, 1:-1, 1:-1, 2:] + padded[:, 1:-1, 1:-1, :-2]


def inner(field):
    return field[:, 1:-1, 1:-1, 1:-1]


def flux_transpose(padded, owner_jac, neighbor_jac):
    psi = padded[:5]
    weights = padded[5:]
    center = inner(psi)
    total = jnp.zeros_like(center)
    for direction in range(3):
        lower = [slice(None), slice(1, -1), slice(1, -1), slice(1, -1)]
        upper = [slice(None), slice(1, -1), slice(1, -1), slice(1, -1)]
        lower[direction + 1] = slice(0, -2)
        upper[direction + 1] = slice(2, None)
        w_here = weights[direction, 1:-1, 1:-1, 1:-1]
        w_lower = weights[direction][tuple(lower[1:])]
        up_term = w_here[None] * (center - psi[tuple(upper)])
        down_term = w_lower[None] * (psi[tuple(lower)] - center)
        total = total + jnp.einsum(
            "uv,ukji->vkji", owner_jac[direction], up_term, precision=lax.Precision.HIGHEST
        )
        total = total + jnp.einsum(
            "uv,ukji->vkji", neighbor_jac[direction], down_term, precision=lax.Precision.HIGHEST
        )
    return total


def relax(mesh_pad, stiff_pad, force_pad):
    weighted = stiff_pad[None] * mesh_pad
    stiff_in = stiff_pad[1:-1, 1:-1, 1:-1]
    diag_term = 6.0 * stiff_in + 1.0
    mesh_in = inner(mesh_pad)
    return (
        mesh_in
        + 0.8
        * (inner(force_pad) - diag_term[None] * mesh_in + neighbor_sum(weighted))
        / diag_term[None]
    )


def run_sweeps(stiff_pad, force_pad):
    mesh_pad = 0.8 * force_pad / (6.0 * stiff_pad[None] + 1.0)
    for sweep in range(1, SWEEPS):
        mesh_pad = relax(mesh_pad, stiff_pad, force_pad)
        stiff_pad = stiff_pad[1:-1, 1:-1, 1:-1]
        force_pad = inner(force_pad)
    return mesh_pad


ORDER = ("circ", "normal", "span")
WRAP = {"circ": True, "normal": False, "span": False}


def edge(array, dim, side, width):
    length = array.shape[dim]
    start = length - width if side < 0 else 0
    return lax.slice_in_dim(array, start, start + width, axis=dim)


def pairs_for(offsets, wrap=()):
    axes = [a for a in ORDER if a in offsets]
    sizes = [lax.axis_size(a) for a in axes]
    pairs = []
    for source in itertools.product(*[range(n) for n in sizes]):
        target, inside = [], True
        for axis, q, n in zip(axes, source, sizes):
            t = q + offsets[axis]
            if WRAP[axis] or axis in wrap:
                t %= n
            elif not 0 <= t < n:
                inside = False
            target.append(t)
        if inside:
            lin = lambda v: sum(x * math.prod(sizes[i + 1 :]) for i, x in enumerate(v))
            pairs.append((lin(source), lin(target)))
    return tuple(axes), pairs


def take(array, rel, dims, width):
    for axis, r in rel.items():
        if r:
            array = edge(array, dims[axis], r, width)
    return array


def receive(array, rel, dims, width, pack=False):
    rel = {a: r for a, r in rel.items() if r}
    axes, pairs = pairs_for({a: -r for a, r in rel.items()})
    slab = take(array, rel, dims, width)
    if not pack:
        return lax.ppermute(slab, axes, pairs)
    size = slab.size
    rows = -(-size // 1024) * 8
    flat = jnp.pad(slab.reshape(-1), (0, rows * 128 - size)).reshape(rows, 128)
    return lax.ppermute(flat, axes, pairs).reshape(-1)[:size].reshape(slab.shape)


def receive_pair(array, rel, axis, dims, width, pack=False):
    low = dict(rel, **{axis: -1})
    high = dict(rel, **{axis: 1})
    if lax.axis_size(axis) != 2 or WRAP[axis]:
        return receive(array, low, dims, width), receive(array, high, dims, width)
    me = lax.axis_index(axis)
    sent = jnp.where(me == 0, take(array, low, dims, width), take(array, high, dims, width))
    low_nz = {a: r for a, r in low.items() if r}
    axes, pairs = pairs_for({a: -r for a, r in low_nz.items()})
    _, back = pairs_for({a: -r for a, r in dict(low_nz, **{axis: 1}).items()})
    if pack:
        size = sent.size
        rows = -(-size // 1024) * 8
        flat = jnp.pad(sent.reshape(-1), (0, rows * 128 - size)).reshape(rows, 128)
        got = lax.ppermute(flat, axes, pairs + back).reshape(-1)[:size].reshape(sent.shape)
    else:
        got = lax.ppermute(sent, axes, pairs + back)
    zero = jnp.zeros_like(got)
    return jnp.where(me == 1, got, zero), jnp.where(me == 0, got, zero)


def tile_halos(fields, axis, dim, length):
    rows = 8
    me = lax.axis_index(axis)
    start = (1 - me) * (length - rows)
    sent = jnp.concatenate([lax.dynamic_slice_in_dim(f, start, rows, axis=dim) for f in fields], axis=0)
    got = lax.ppermute(sent, axis, [(0, 1), (1, 0)])
    low = lax.slice_in_dim(got, rows - 1, rows, axis=dim)
    high = lax.slice_in_dim(got, 0, 1, axis=dim)
    zero = jnp.zeros_like(low)
    return jnp.where(me == 1, low, zero), jnp.where(me == 0, high, zero)


def face_halos(fields, axis, dim, wrap):
    length = fields[0].shape[dim]
    if axis == "normal" and lax.axis_size(axis) == 2 and length >= 8:
        return tile_halos(fields, axis, dim, length)
    thin = jnp.concatenate(
        [jnp.concatenate([edge(f, dim, 1, 1), edge(f, dim, -1, 1)], axis=dim) for f in fields], axis=0
    )
    return receive_pair(thin, {}, axis, {axis: dim}, 1)


def padded_sweeps(joined, width):
    dims = {"span": 1, "normal": 2, "circ": 3}
    before_c = receive(joined, {"circ": -1}, dims, width)
    after_c = receive(joined, {"circ": 1}, dims, width)
    low_n, high_n = receive_pair(joined, {}, "normal", dims, width)
    low_lc, high_lc = receive_pair(joined, {"circ": -1}, "normal", dims, width, True)
    low_hc, high_hc = receive_pair(joined, {"circ": 1}, "normal", dims, width, True)
    top = jnp.concatenate([low_lc, low_n, low_hc], axis=3)
    middle = jnp.concatenate([before_c, joined, after_c], axis=3)
    bottom = jnp.concatenate([high_lc, high_n, high_hc], axis=3)
    plane = jnp.concatenate([top, middle, bottom], axis=2)
    before_s = receive(plane, {"span": -1}, dims, width, True)
    after_s = receive(plane, {"span": 1}, dims, width, True)
    return jnp.concatenate([before_s, plane, after_s], axis=1)


def jac_apply(jac, term):
    spread = (slice(None), slice(None)) + (None,) * (term.ndim - 1)
    return jnp.sum(jac[spread] * term[:, None], axis=0)


def flux_faces(psi, weights, halos, owner_jac, neighbor_jac):
    inner_terms = []
    for direction in range(3):
        dim = direction + 1
        length = psi.shape[dim]
        low = lax.slice_in_dim(psi, 0, length - 1, axis=dim)
        high = lax.slice_in_dim(psi, 1, length, axis=dim)
        w_low = lax.slice_in_dim(weights[direction], 0, length - 1, axis=direction)
        between = w_low[None] * (low - high)
        inner_terms.append((jac_apply(owner_jac[direction], between), jac_apply(neighbor_jac[direction], between)))
    inner_terms = lax.optimization_barrier(inner_terms)
    total = jnp.zeros_like(psi)
    for direction in range(3):
        dim = direction + 1
        length = psi.shape[dim]
        before, after = halos[direction]
        last = lax.slice_in_dim(psi, length - 1, length, axis=dim)
        first = lax.slice_in_dim(psi, 0, 1, axis=dim)
        w_last = lax.slice_in_dim(weights[direction], length - 1, length, axis=direction)
        up_edge = w_last[None] * (last - after[:5])
        down_edge = before[5][None] * (before[:5] - first)
        up_inner, down_inner = inner_terms[direction]
        up = jnp.concatenate([up_inner, jac_apply(owner_jac[direction], up_edge)], axis=dim)
        down = jnp.concatenate([jac_apply(neighbor_jac[direction], down_edge), down_inner], axis=dim)
        total = total + up
        total = total + down
    return total


def shifted(array, offsets):
    axes, pairs = pairs_for(offsets, ("normal",))
    return lax.ppermute(array, axes, pairs)


def reduce_panels(terms):
    below, own, above = (terms[:, i * PANEL_DEV : (i + 1) * PANEL_DEV] for i in range(3))
    devices = math.prod(lax.axis_size(a) for a in ORDER)
    if devices <= 64:
        spans = lax.axis_size("span")
        relative = jnp.arange(devices, dtype=jnp.int32) // (devices // spans) - lax.axis_index("span") + 1
        chunks = jnp.zeros((devices,) + own.shape, own.dtype)
        for index, block in enumerate((below, own, above)):
            chunks = jnp.where((relative == index)[:, None, None], block[None], chunks)
        return jnp.sum(lax.all_to_all(chunks, ORDER[::-1], 0, 0, tiled=False), axis=0)
    if lax.axis_size("normal") != 2 or lax.axis_size("circ") > 4:
        own = lax.psum(own + shifted(above, {"span": 1}) + shifted(below, {"span": -1}), ("circ", "normal"))
        return own
    partner = {"normal": 1}
    total = own + shifted(above, {"span": 1}) + shifted(below, {"span": -1})
    total = total + shifted(own, partner)
    total = total + shifted(above, dict(partner, span=1)) + shifted(below, dict(partner, span=-1))
    summed = total
    for step in range(1, lax.axis_size("circ")):
        summed = summed + shifted(total, {"circ": step})
    return summed


def on_device(
    adjoint,
    objective_grad,
    face_weights,
    owner_jac,
    neighbor_jac,
    coupling,
    stiffness,
    wall_kernel,
    panel_owner,
):
    halos = [
        face_halos((adjoint, face_weights[d : d + 1]), axis, d + 1, False)
        for d, axis in enumerate(("span", "normal", "circ"))
    ]
    residual = flux_faces(adjoint, face_weights, halos, owner_jac, neighbor_jac) + adjoint - objective_grad
    forcing = jac_apply(coupling.T, residual)
    margin = SWEEPS - 1
    joined = jnp.concatenate([stiffness[None], forcing], axis=0)
    full_pad = padded_sweeps(joined, margin)
    mesh = run_sweeps(full_pad[0], full_pad[1:])
    wall_sens = jnp.sum(wall_kernel[None] * mesh, axis=2)
    span = lax.axis_index("span")
    first = (span - 1) * PANEL_DEV
    local = panel_owner - first
    onehot = (
        local[:, :, None] == jnp.arange(3 * PANEL_DEV, dtype=jnp.int32)[None, None, :]
    ).astype(jnp.float32)
    terms = jnp.einsum("mki,kip->mp", wall_sens, onehot, precision=lax.Precision.HIGHEST)
    panels = reduce_panels(terms)
    return (residual, mesh, panels)


def solution(mesh):
    placed = (
        P(None, "span", "normal", "circ"),
        P(None, "span", "normal", "circ"),
        P(None, "span", "normal", "circ"),
        P(),
        P(),
        P(),
        P("span", "normal", "circ"),
        P("span", "normal", "circ"),
        P("span", "circ"),
    )
    return jax.shard_map(
        on_device,
        mesh=mesh,
        in_specs=placed,
        out_specs=(
            P(None, "span", "normal", "circ"),
            P(None, "span", "normal", "circ"),
            P(None, "span"),
        ),
        check_vma=False,
    )
```

```python
import itertools
import math

import jax
import jax.numpy as jnp
from jax import lax
from jax.sharding import PartitionSpec as P

PANEL_DEV = 128
SWEEPS = 4


def padded_2(array, sides, width, wrap):
    for axis, dim in sides:
        peers, length = (lax.axis_size(axis), array.shape[dim])
        up = [(i, (i + 1) % peers) for i in range(peers if wrap else peers - 1)]
        down = [(j, i) for i, j in up]
        last = lax.slice_in_dim(array, length - width, length, axis=dim)
        initial = lax.slice_in_dim(array, 0, width, axis=dim)
        before = lax.ppermute(last, axis, up)
        after = lax.ppermute(initial, axis, down)
        array = jnp.concatenate([before, array, after], axis=dim)
    return array


def neighbor_sum(padded):
    total = padded[:, 2:, 1:-1, 1:-1] + padded[:, :-2, 1:-1, 1:-1]
    total = total + padded[:, 1:-1, 2:, 1:-1] + padded[:, 1:-1, :-2, 1:-1]
    return total + padded[:, 1:-1, 1:-1, 2:] + padded[:, 1:-1, 1:-1, :-2]


def inner(field):
    return field[:, 1:-1, 1:-1, 1:-1]


def flux_transpose(padded, owner_jac, neighbor_jac):
    psi = padded[:5]
    weights = padded[5:]
    center = inner(psi)
    total = jnp.zeros_like(center)
    for direction in range(3):
        lower = [slice(None), slice(1, -1), slice(1, -1), slice(1, -1)]
        upper = [slice(None), slice(1, -1), slice(1, -1), slice(1, -1)]
        lower[direction + 1] = slice(0, -2)
        upper[direction + 1] = slice(2, None)
        w_here = weights[direction, 1:-1, 1:-1, 1:-1]
        w_lower = weights[direction][tuple(lower[1:])]
        up_term = w_here[None] * (center - psi[tuple(upper)])
        down_term = w_lower[None] * (psi[tuple(lower)] - center)
        total = total + jnp.einsum(
            "uv,ukji->vkji", owner_jac[direction], up_term, precision=lax.Precision.HIGHEST
        )
        total = total + jnp.einsum(
            "uv,ukji->vkji", neighbor_jac[direction], down_term, precision=lax.Precision.HIGHEST
        )
    return total


def relax(mesh_pad, stiff_pad, force_pad):
    weighted = stiff_pad[None] * mesh_pad
    stiff_in = stiff_pad[1:-1, 1:-1, 1:-1]
    diag_term = 6.0 * stiff_in + 1.0
    mesh_in = inner(mesh_pad)
    return (
        mesh_in
        + 0.8
        * (inner(force_pad) - diag_term[None] * mesh_in + neighbor_sum(weighted))
        / diag_term[None]
    )


def run_sweeps(stiff_pad, force_pad):
    mesh_pad = 0.8 * force_pad / (6.0 * stiff_pad[None] + 1.0)
    for sweep in range(1, SWEEPS):
        mesh_pad = relax(mesh_pad, stiff_pad, force_pad)
        stiff_pad = stiff_pad[1:-1, 1:-1, 1:-1]
        force_pad = inner(force_pad)
    return mesh_pad


ORDER = ("circ", "normal", "span")
WRAP = {"circ": True, "normal": False, "span": False}


def edge(array, dim, side, width):
    length = array.shape[dim]
    start = length - width if side < 0 else 0
    return lax.slice_in_dim(array, start, start + width, axis=dim)


def pairs_for(offsets, wrap=()):
    axes = [a for a in ORDER if a in offsets]
    sizes = [lax.axis_size(a) for a in axes]
    pairs = []
    for source in itertools.product(*[range(n) for n in sizes]):
        target, inside = [], True
        for axis, q, n in zip(axes, source, sizes):
            t = q + offsets[axis]
            if WRAP[axis] or axis in wrap:
                t %= n
            elif not 0 <= t < n:
                inside = False
            target.append(t)
        if inside:
            lin = lambda v: sum(x * math.prod(sizes[i + 1 :]) for i, x in enumerate(v))
            pairs.append((lin(source), lin(target)))
    return tuple(axes), pairs


def take(array, rel, dims, width):
    for axis, r in rel.items():
        if r:
            array = edge(array, dims[axis], r, width)
    return array


def receive(array, rel, dims, width, pack=False):
    rel = {a: r for a, r in rel.items() if r}
    axes, pairs = pairs_for({a: -r for a, r in rel.items()})
    slab = take(array, rel, dims, width)
    if not pack:
        return lax.ppermute(slab, axes, pairs)
    size = slab.size
    rows = -(-size // 1024) * 8
    flat = jnp.pad(slab.reshape(-1), (0, rows * 128 - size)).reshape(rows, 128)
    return lax.ppermute(flat, axes, pairs).reshape(-1)[:size].reshape(slab.shape)


def receive_pair(array, rel, axis, dims, width):
    low = dict(rel, **{axis: -1})
    high = dict(rel, **{axis: 1})
    if lax.axis_size(axis) != 2 or WRAP[axis]:
        return receive(array, low, dims, width), receive(array, high, dims, width)
    me = lax.axis_index(axis)
    if rel:
        sent = jnp.where(me == 0, take(array, low, dims, width), take(array, high, dims, width))
    else:
        length = array.shape[dims[axis]]
        sent = lax.dynamic_slice_in_dim(array, (1 - me) * (length - width), width, axis=dims[axis])
    low_nz = {a: r for a, r in low.items() if r}
    axes, pairs = pairs_for({a: -r for a, r in low_nz.items()})
    _, back = pairs_for({a: -r for a, r in dict(low_nz, **{axis: 1}).items()})
    got = lax.ppermute(sent, axes, pairs + back)
    zero = jnp.zeros_like(got)
    return jnp.where(me == 1, got, zero), jnp.where(me == 0, got, zero)


def tile_halos(fields, axis, dim, length):
    rows = 8
    me = lax.axis_index(axis)
    start = (1 - me) * (length - rows)
    sent = jnp.concatenate([lax.dynamic_slice_in_dim(f, start, rows, axis=dim) for f in fields], axis=0)
    got = lax.ppermute(sent, axis, [(0, 1), (1, 0)])
    low = lax.slice_in_dim(got, rows - 1, rows, axis=dim)
    high = lax.slice_in_dim(got, 0, 1, axis=dim)
    zero = jnp.zeros_like(low)
    return jnp.where(me == 1, low, zero), jnp.where(me == 0, high, zero)


def face_halos(fields, axis, dim, wrap):
    length = fields[0].shape[dim]
    if axis == "normal" and lax.axis_size(axis) == 2 and length >= 8:
        return tile_halos(fields, axis, dim, length)
    thin = jnp.concatenate(
        [jnp.concatenate([edge(f, dim, 1, 1), edge(f, dim, -1, 1)], axis=dim) for f in fields], axis=0
    )
    return receive_pair(thin, {}, axis, {axis: dim}, 1)


def padded_sweeps(joined, width):
    dims = {"span": 1, "normal": 2, "circ": 3}
    before_c = receive(joined, {"circ": -1}, dims, width)
    after_c = receive(joined, {"circ": 1}, dims, width)
    low_n, high_n = receive_pair(joined, {}, "normal", dims, width)
    low_lc, high_lc = receive_pair(joined, {"circ": -1}, "normal", dims, width)
    low_hc, high_hc = receive_pair(joined, {"circ": 1}, "normal", dims, width)
    top = jnp.concatenate([low_lc, low_n, low_hc], axis=3)
    middle = jnp.concatenate([before_c, joined, after_c], axis=3)
    bottom = jnp.concatenate([high_lc, high_n, high_hc], axis=3)
    plane = jnp.concatenate([top, middle, bottom], axis=2)
    before_s = receive(plane, {"span": -1}, dims, width, True)
    after_s = receive(plane, {"span": 1}, dims, width, True)
    return jnp.concatenate([before_s, plane, after_s], axis=1)


def jac_apply(jac, term):
    spread = (slice(None), slice(None)) + (None,) * (term.ndim - 1)
    return jnp.sum(jac[spread] * term[:, None], axis=0)


def flux_faces(psi, weights, halos, owner_jac, neighbor_jac):
    inner_terms = []
    for direction in range(3):
        dim = direction + 1
        length = psi.shape[dim]
        low = lax.slice_in_dim(psi, 0, length - 1, axis=dim)
        high = lax.slice_in_dim(psi, 1, length, axis=dim)
        w_low = lax.slice_in_dim(weights[direction], 0, length - 1, axis=direction)
        between = w_low[None] * (low - high)
        inner_terms.append((jac_apply(owner_jac[direction], between), jac_apply(neighbor_jac[direction], between)))
    inner_terms = lax.optimization_barrier(inner_terms)
    total = jnp.zeros_like(psi)
    for direction in range(3):
        dim = direction + 1
        length = psi.shape[dim]
        before, after = halos[direction]
        last = lax.slice_in_dim(psi, length - 1, length, axis=dim)
        first = lax.slice_in_dim(psi, 0, 1, axis=dim)
        w_last = lax.slice_in_dim(weights[direction], length - 1, length, axis=direction)
        up_edge = w_last[None] * (last - after[:5])
        down_edge = before[5][None] * (before[:5] - first)
        up_inner, down_inner = inner_terms[direction]
        up = jnp.concatenate([up_inner, jac_apply(owner_jac[direction], up_edge)], axis=dim)
        down = jnp.concatenate([jac_apply(neighbor_jac[direction], down_edge), down_inner], axis=dim)
        total = total + up
        total = total + down
    return total


def shifted(array, offsets):
    axes, pairs = pairs_for(offsets, ("normal",))
    return lax.ppermute(array, axes, pairs)


def reduce_panels(terms):
    below, own, above = (terms[:, i * PANEL_DEV : (i + 1) * PANEL_DEV] for i in range(3))
    devices = math.prod(lax.axis_size(a) for a in ORDER)
    if devices <= 64:
        spans = lax.axis_size("span")
        relative = jnp.arange(devices, dtype=jnp.int32) // (devices // spans) - lax.axis_index("span") + 1
        chunks = jnp.zeros((devices,) + own.shape, own.dtype)
        for index, block in enumerate((below, own, above)):
            chunks = jnp.where((relative == index)[:, None, None], block[None], chunks)
        return jnp.sum(lax.all_to_all(chunks, ORDER[::-1], 0, 0, tiled=False), axis=0)
    if lax.axis_size("normal") != 2 or lax.axis_size("circ") > 4:
        own = lax.psum(own + shifted(above, {"span": 1}) + shifted(below, {"span": -1}), ("circ", "normal"))
        return own
    partner = {"normal": 1}
    total = own + shifted(above, {"span": 1}) + shifted(below, {"span": -1})
    total = total + shifted(own, partner)
    total = total + shifted(above, dict(partner, span=1)) + shifted(below, dict(partner, span=-1))
    summed = total
    for step in range(1, lax.axis_size("circ")):
        summed = summed + shifted(total, {"circ": step})
    return summed


def on_device(
    adjoint,
    objective_grad,
    face_weights,
    owner_jac,
    neighbor_jac,
    coupling,
    stiffness,
    wall_kernel,
    panel_owner,
):
    halos = [
        face_halos((adjoint, face_weights[d : d + 1]), axis, d + 1, False)
        for d, axis in enumerate(("span", "normal", "circ"))
    ]
    residual = flux_faces(adjoint, face_weights, halos, owner_jac, neighbor_jac) + adjoint - objective_grad
    forcing = jac_apply(coupling.T, residual)
    margin = SWEEPS - 1
    joined = jnp.concatenate([stiffness[None], forcing], axis=0)
    full_pad = padded_sweeps(joined, margin)
    mesh = run_sweeps(full_pad[0], full_pad[1:])
    wall_sens = jnp.sum(wall_kernel[None] * mesh, axis=2)
    span = lax.axis_index("span")
    first = (span - 1) * PANEL_DEV
    local = panel_owner - first
    onehot = (
        local[:, :, None] == jnp.arange(3 * PANEL_DEV, dtype=jnp.int32)[None, None, :]
    ).astype(jnp.float32)
    terms = jnp.einsum("mki,kip->mp", wall_sens, onehot, precision=lax.Precision.HIGHEST)
    panels = reduce_panels(terms)
    return (residual, mesh, panels)


def solution(mesh):
    placed = (
        P(None, "span", "normal", "circ"),
        P(None, "span", "normal", "circ"),
        P(None, "span", "normal", "circ"),
        P(),
        P(),
        P(),
        P("span", "normal", "circ"),
        P("span", "normal", "circ"),
        P("span", "circ"),
    )
    return jax.shard_map(
        on_device,
        mesh=mesh,
        in_specs=placed,
        out_specs=(
            P(None, "span", "normal", "circ"),
            P(None, "span", "normal", "circ"),
            P(None, "span"),
        ),
        check_vma=False,
    )
```
